512 devices in a mesh: energy: 64 (over y, z_lo, core), domain: 8 (over z_hi, x).
Axes of the slice: x: 4, y: 8, z: 8 (z_hi: 2, z_lo: 4; z = z_hi * 4 + z_lo), core: 2. Of those that a mesh axis runs over, the one named last changes fastest.
Arguments:
- green_slab: bfloat16 [64, 8, 2, 3, 64, 2048], P('energy', 'domain'), may hold values from -6 to 6
- self_energy: float32 [64, 8, 2, 2, 2048], P('energy', 'domain'), may hold values from -3 to 3
- pattern: int32 [8, 2560], P('domain'), may hold values from 0 to 5119, as said below
- screened: bfloat16 [64, 8, 2, 64, 80], P('energy', 'domain'), may hold values from -0.625 to 0.625
Outputs:
- screened_lesser: float32 [64, 8, 2, 64, 64], P('energy', 'domain')
The draws below stay inside these ranges and needn't reach their ends.
Inputs may be any that keep to these rules, and one draw needn't show every extreme that they name: `pattern`: within each domain the 2560 positions are distinct flat positions r * 80 + c; the first and the last position of the matrix are always retained.
All inputs are finite; a program needn't handle non-finite values.
Results may differ from the reference program's by a relative error of at most 0.007.
Values may be sent and summed in bfloat16 or wider, within the bound.
No kernel may reach another device: no remote copies, remote signals or barrier semaphores. Data moves between devices by JAX's collectives and lax.ppermute only.
A program may use at most 64 MiB of HBM per device.

```python
import math
import jax
import jax.numpy as jnp
from jax import lax

BLOCK = 2048
ROWS = 64
EDGE = 16
ENERGIES = 64
DOMAINS = 8
ELEM = 2560


def draw_pattern(key, part):
    entry_count = ROWS * (ROWS + EDGE)

    def one_domain(domain_key):
        shuffled = jax.random.permutation(domain_key, entry_count - 2).astype(jnp.int32) + 1
        corner_ids = jnp.array([0, entry_count - 1], dtype=jnp.int32)
        return jnp.concatenate([corner_ids, shuffled[:ELEM - 2]])
    return jax.vmap(one_domain)(jax.random.split(jax.random.fold_in(key, 7), DOMAINS))


def level_of(stream_key, dims, cuts, low, top_value):
    level, own = 1.0, jax.random.fold_in(stream_key, 6)
    for axis_at, shards_of in cuts:
        steps = jnp.exp(jax.random.uniform(jax.random.fold_in(own, axis_at), (shards_of,), jnp.float32, low / len(cuts), top_value / len(cuts)))
        level = level * jnp.repeat(steps, dims[axis_at] // shards_of).reshape([-1 if axis == axis_at else 1 for axis in range(len(dims))])
    return level


def centred(own_key, dims, scale, bound, cuts=(), held_as=jnp.bfloat16):
    drawn = scale * jax.random.normal(own_key, dims, jnp.float32)
    if cuts:
        drawn = drawn * level_of(own_key, dims, cuts, -0.22, 0.18)
    return jnp.clip(drawn, -bound, bound).astype(held_as)


def setup_inputs(seed: int = 0) -> dict:
    splits = jax.random.split(jax.random.key(seed), 5)
    green_slab = centred(splits[0], (ENERGIES, DOMAINS, 2, 3, ROWS, BLOCK), 1.0, 6.0, ((0, 64), (1, 8)))
    self_energy = centred(splits[1], (ENERGIES, DOMAINS, 2, 2, BLOCK), 0.5, 3.0, ((0, 64), (1, 8)), jnp.float32)
    pattern = draw_pattern(jax.random.fold_in(splits[4], 71), 0)
    screened = centred(splits[3], (ENERGIES, DOMAINS, 2, ROWS, ROWS + EDGE), (ROWS + EDGE) ** -0.5, 0.625, ((0, 64), (1, 8)))
    return dict(green_slab=green_slab, self_energy=self_energy, pattern=pattern, screened=screened)


def slab_adjoint(left_real, left_imag, right_real, right_imag):
    left_real = left_real.astype(jnp.float32)
    left_imag = left_imag.astype(jnp.float32)
    right_real = right_real.astype(jnp.float32)
    right_imag = right_imag.astype(jnp.float32)
    real_sum = jnp.einsum('qjrb,jsb->qrs', left_real, right_real) + jnp.einsum('qjrb,jsb->qrs', left_imag, right_imag)
    imag_sum = jnp.einsum('qjrb,jsb->qrs', left_imag, right_real) - jnp.einsum('qjrb,jsb->qrs', left_real, right_imag)
    return (real_sum, imag_sum)

def times_adjoint(left_real, left_imag, right_real, right_imag):
    real_sum = jnp.dot(left_real, right_real.T, preferred_element_type=jnp.float32) + jnp.dot(left_imag, right_imag.T, preferred_element_type=jnp.float32)
    imag_sum = jnp.dot(left_imag, right_real.T, preferred_element_type=jnp.float32) - jnp.dot(left_real, right_imag.T, preferred_element_type=jnp.float32)
    return (real_sum, imag_sum)

def complex_product(left_real, left_imag, right_real, right_imag):
    real_sum = jnp.dot(left_real, right_real, preferred_element_type=jnp.float32) - jnp.dot(left_imag, right_imag, preferred_element_type=jnp.float32)
    imag_sum = jnp.dot(left_real, right_imag, preferred_element_type=jnp.float32) + jnp.dot(left_imag, right_real, preferred_element_type=jnp.float32)
    return (real_sum, imag_sum)

def element_values(own_slab, next_edge, diag_rates, pattern_row):
    block_order = own_slab.shape[3]
    factor = 1.0 / math.sqrt(3.0 * block_order)
    rate_real = jnp.transpose(diag_rates[:, :, 0], (1, 0, 2))[:, :, None, :]
    rate_imag = jnp.transpose(diag_rates[:, :, 1], (1, 0, 2))[:, :, None, :]
    slab_real = own_slab[0].astype(jnp.float32)[None]
    slab_imag = own_slab[1].astype(jnp.float32)[None]
    weighted_real = ((slab_real * rate_real - slab_imag * rate_imag) * factor).astype(jnp.bfloat16)
    weighted_imag = ((slab_real * rate_imag + slab_imag * rate_real) * factor).astype(jnp.bfloat16)
    near_real, near_imag = slab_adjoint(weighted_real, weighted_imag, own_slab[0], own_slab[1])
    edge_real, edge_imag = slab_adjoint(weighted_real[:, 1:3], weighted_imag[:, 1:3], next_edge[0], next_edge[1])
    joined_real = jnp.concatenate([near_real, edge_real], axis=2).reshape(2, -1)
    joined_imag = jnp.concatenate([near_imag, edge_imag], axis=2).reshape(2, -1)
    picked_real = jnp.take(joined_real, pattern_row, axis=1)
    picked_imag = jnp.take(joined_imag, pattern_row, axis=1)
    return jnp.stack([picked_real, picked_imag], axis=1).astype(jnp.bfloat16)

def correlate(values):
    lesser = values[:, :, 0].astype(jnp.float32)
    greater = values[:, :, 1].astype(jnp.float32)
    factor = 1.0 / math.sqrt(ENERGIES)

    def one_lag(lag_index):
        offsets = jnp.arange(ENERGIES, dtype=jnp.int32) - lag_index
        inside = (offsets >= 0).astype(jnp.float32)
        shifted = jnp.take(greater, jnp.clip(offsets, 0, ENERGIES - 1), axis=0) * inside[:, None, None, None]
        real_sum = lax.optimization_barrier(jnp.sum(lesser[:, :, 0] * shifted[:, :, 0] - lesser[:, :, 1] * shifted[:, :, 1], axis=0))
        imag_sum = lax.optimization_barrier(jnp.sum(lesser[:, :, 0] * shifted[:, :, 1] + lesser[:, :, 1] * shifted[:, :, 0], axis=0))
        return jnp.stack([real_sum, imag_sum], axis=1) * factor
    return lax.map(one_lag, jnp.arange(ENERGIES, dtype=jnp.int32)).astype(jnp.bfloat16)

def screen(polar_row, pattern_row, screen_block):
    row_count = screen_block.shape[1]
    col_count = screen_block.shape[2]
    flat_dense = jnp.zeros((2, row_count * col_count), jnp.bfloat16).at[:, pattern_row].set(polar_row)
    dense_pol = flat_dense.reshape(2, row_count, col_count)
    inner_real, inner_imag = times_adjoint(dense_pol[0], dense_pol[1], screen_block[0], screen_block[1])
    inner_real = inner_real.astype(jnp.bfloat16)
    inner_imag = inner_imag.astype(jnp.bfloat16)
    near_real = screen_block[0][:, :row_count]
    near_imag = screen_block[1][:, :row_count]
    across_real, across_imag = complex_product(near_real, near_imag, dense_pol[0][:, row_count:], dense_pol[1][:, row_count:])
    across_real = across_real.astype(jnp.bfloat16)
    across_imag = across_imag.astype(jnp.bfloat16)
    first_real, first_imag = complex_product(near_real, near_imag, inner_real, inner_imag)
    second_real, second_imag = times_adjoint(screen_block[0][:, row_count:], screen_block[1][:, row_count:], across_real, across_imag)
    return jnp.stack([first_real + second_real, first_imag + second_imag], axis=0)

def reference(green_slab, self_energy, pattern, screened):
    padded = jnp.pad(self_energy, ((0, 0), (1, 1), (0, 0), (0, 0), (0, 0)))
    zero_edge = jnp.zeros((2, 2, EDGE, BLOCK), jnp.bfloat16)

    def per_pair(flat_index):
        energy = flat_index // DOMAINS
        domain = flat_index % DOMAINS
        own_slab = green_slab[energy, domain]
        following = jnp.minimum(domain + 1, DOMAINS - 1)
        next_edge = green_slab[energy, following][:, 0:2, :EDGE, :]
        next_edge = jnp.where(domain + 1 < DOMAINS, next_edge, zero_edge)
        diag_rates = lax.dynamic_slice_in_dim(padded[energy], domain, 3, 0)
        return element_values(own_slab, next_edge, diag_rates, pattern[domain])
    pair_ids = jnp.arange(ENERGIES * DOMAINS, dtype=jnp.int32)
    values = lax.map(per_pair, pair_ids).reshape(ENERGIES, DOMAINS, 2, 2, ELEM)
    polarization = correlate(values)

    def per_block(flat_index):
        energy = flat_index // DOMAINS
        domain = flat_index % DOMAINS
        return screen(polarization[energy, domain], pattern[domain], screened[energy, domain])
    result = lax.map(per_block, pair_ids)
    return result.reshape(ENERGIES, DOMAINS, 2, ROWS, ROWS)
```

```python
import math

import jax
import jax.numpy as jnp
from jax import lax
from jax.sharding import PartitionSpec as P

EDGE = 16


def padded_2(cells, sides, width):
    for axis, dim in sides:
        count = lax.axis_size(axis)
        ends = count - 1
        head = lax.slice_in_dim(cells, 0, width, axis=dim)
        tail = lax.slice_in_dim(cells, cells.shape[dim] - width, cells.shape[dim], axis=dim)
        cells = jnp.concatenate(
            [
                lax.ppermute(tail, axis, [(i, (i + 1) % count) for i in range(ends)]),
                cells,
                lax.ppermute(head, axis, [((i + 1) % count, i) for i in range(ends)]),
            ],
            axis=dim,
        )
    return cells


def passed_along(x, axis, by):
    length = lax.axis_size(axis)
    pairs = [(i, i + by) for i in range(length) if 0 <= i + by < length]
    return lax.ppermute(x, axis, pairs)


def slab_adjoint(left_real, left_imag, right_real, right_imag):
    real_sum = jnp.einsum(
        "qjrb,jsb->qrs", left_real, right_real, preferred_element_type=jnp.float32
    ) + jnp.einsum("qjrb,jsb->qrs", left_imag, right_imag, preferred_element_type=jnp.float32)
    imag_sum = jnp.einsum(
        "qjrb,jsb->qrs", left_imag, right_real, preferred_element_type=jnp.float32
    ) - jnp.einsum("qjrb,jsb->qrs", left_real, right_imag, preferred_element_type=jnp.float32)
    return (real_sum, imag_sum)


def times_adjoint(left_real, left_imag, right_real, right_imag):
    real_sum = jnp.dot(left_real, right_real.T, preferred_element_type=jnp.float32) + jnp.dot(
        left_imag, right_imag.T, preferred_element_type=jnp.float32
    )
    imag_sum = jnp.dot(left_imag, right_real.T, preferred_element_type=jnp.float32) - jnp.dot(
        left_real, right_imag.T, preferred_element_type=jnp.float32
    )
    return (real_sum, imag_sum)


def complex_product(left_real, left_imag, right_real, right_imag):
    real_sum = jnp.dot(left_real, right_real, preferred_element_type=jnp.float32) - jnp.dot(
        left_imag, right_imag, preferred_element_type=jnp.float32
    )
    imag_sum = jnp.dot(left_real, right_imag, preferred_element_type=jnp.float32) + jnp.dot(
        left_imag, right_real, preferred_element_type=jnp.float32
    )
    return (real_sum, imag_sum)


def element_values(own_slab, next_edge, diag_rates, pattern_row):
    block_order = own_slab.shape[3]
    factor = 1.0 / math.sqrt(3.0 * block_order)
    rate_real = jnp.transpose(diag_rates[:, :, 0], (1, 0, 2))[:, :, None, :]
    rate_imag = jnp.transpose(diag_rates[:, :, 1], (1, 0, 2))[:, :, None, :]
    slab_real = own_slab[0].astype(jnp.float32)[None]
    slab_imag = own_slab[1].astype(jnp.float32)[None]
    weighted_real = ((slab_real * rate_real - slab_imag * rate_imag) * factor).astype(jnp.bfloat16)
    weighted_imag = ((slab_real * rate_imag + slab_imag * rate_real) * factor).astype(jnp.bfloat16)
    near_real, near_imag = slab_adjoint(weighted_real, weighted_imag, own_slab[0], own_slab[1])
    edge_real, edge_imag = slab_adjoint(
        weighted_real[:, 1:3], weighted_imag[:, 1:3], next_edge[0], next_edge[1]
    )
    joined_real = jnp.concatenate([near_real, edge_real], axis=2).reshape(2, -1)
    joined_imag = jnp.concatenate([near_imag, edge_imag], axis=2).reshape(2, -1)
    picked_real = jnp.take(joined_real, pattern_row, axis=1)
    picked_imag = jnp.take(joined_imag, pattern_row, axis=1)
    return jnp.stack([picked_real, picked_imag], axis=1).astype(jnp.bfloat16)


def lagged_sums(by_element):
    energy_count = by_element.shape[0]
    column_count = by_element.shape[3]
    lesser = by_element[:, 0].astype(jnp.float32)
    backward = by_element[::-1, 1].astype(jnp.float32)
    real_part = (
        lesser[:, None, 0] * backward[None, :, 0] - lesser[:, None, 1] * backward[None, :, 1]
    )
    imag_part = (
        lesser[:, None, 0] * backward[None, :, 1] + lesser[:, None, 1] * backward[None, :, 0]
    )
    joined = jnp.concatenate([real_part, imag_part], axis=2)
    padded = jnp.pad(joined, ((0, 0), (0, energy_count + 1), (0, 0)))
    flat_rows = padded.reshape(energy_count * (2 * energy_count + 1), 2 * column_count)
    skewed = flat_rows[: energy_count * 2 * energy_count].reshape(
        energy_count, 2 * energy_count, 2 * column_count
    )
    totals = jnp.sum(skewed, axis=0)[energy_count - 1 : 2 * energy_count - 1]
    factor = 1.0 / math.sqrt(energy_count)
    return (totals.reshape(energy_count, 2, column_count) * factor).astype(jnp.bfloat16)


def screen(polar_row, pattern_row, screen_block):
    row_count = screen_block.shape[1]
    col_count = screen_block.shape[2]
    flat_dense = (
        jnp.zeros((2, row_count * col_count), jnp.bfloat16).at[:, pattern_row].set(polar_row)
    )
    dense_pol = flat_dense.reshape(2, row_count, col_count)
    inner_real, inner_imag = times_adjoint(
        dense_pol[0], dense_pol[1], screen_block[0], screen_block[1]
    )
    inner_real = inner_real.astype(jnp.bfloat16)
    inner_imag = inner_imag.astype(jnp.bfloat16)
    near_real = screen_block[0][:, :row_count]
    near_imag = screen_block[1][:, :row_count]
    across_real, across_imag = complex_product(
        near_real, near_imag, dense_pol[0][:, row_count:], dense_pol[1][:, row_count:]
    )
    across_real = across_real.astype(jnp.bfloat16)
    across_imag = across_imag.astype(jnp.bfloat16)
    first_real, first_imag = complex_product(near_real, near_imag, inner_real, inner_imag)
    second_real, second_imag = times_adjoint(
        screen_block[0][:, row_count:], screen_block[1][:, row_count:], across_real, across_imag
    )
    return jnp.stack([first_real + second_real, first_imag + second_imag], axis=0)


def own_lag(gathered):
    energy_count = gathered.shape[0]
    lag = lax.axis_index("energy")
    lesser = gathered[:, 0].astype(jnp.float32)
    greater = jnp.roll(gathered[:, 1].astype(jnp.float32), lag, axis=0)
    inside = (jnp.arange(energy_count) >= lag)[:, None, None]
    greater = jnp.where(inside, greater, 0.0)
    real_sum = jnp.sum(lesser[:, 0] * greater[:, 0] - lesser[:, 1] * greater[:, 1], axis=0)
    imag_sum = jnp.sum(lesser[:, 0] * greater[:, 1] + lesser[:, 1] * greater[:, 0], axis=0)
    factor = 1.0 / math.sqrt(energy_count)
    return (jnp.stack([real_sum, imag_sum], axis=0) * factor).astype(jnp.bfloat16)


def body(green_slab, self_energy, pattern, screened):
    nearby = padded_2(self_energy, (("domain", 1),), 1)
    edge_block = green_slab[0, 0, :, 0:2, :EDGE, :]
    following = passed_along(edge_block, "domain", -1)
    values = element_values(green_slab[0, 0], following, nearby[0], pattern[0])
    gathered = lax.all_gather(values, "energy")
    polarization = own_lag(gathered)
    result = screen(polarization, pattern[0], screened[0, 0])
    return result[None, None]


def solution(mesh):
    placed = (
        P("energy", "domain", None, None, None, None),
        P("energy", "domain", None, None, None),
        P("domain", None),
        P("energy", "domain", None, None, None),
    )
    return jax.shard_map(
        body,
        mesh=mesh,
        in_specs=placed,
        out_specs=P("energy", "domain", None, None, None),
        check_vma=False,
    )
```

```python
import math

import jax
import jax.numpy as jnp
from jax import lax
from jax.sharding import PartitionSpec as P

EDGE = 16


def padded_2(cells, sides, width):
    for axis, dim in sides:
        count = lax.axis_size(axis)
        ends = count - 1
        head = lax.slice_in_dim(cells, 0, width, axis=dim)
        tail = lax.slice_in_dim(cells, cells.shape[dim] - width, cells.shape[dim], axis=dim)
        cells = jnp.concatenate(
            [
                lax.ppermute(tail, axis, [(i, (i + 1) % count) for i in range(ends)]),
                cells,
                lax.ppermute(head, axis, [((i + 1) % count, i) for i in range(ends)]),
            ],
            axis=dim,
        )
    return cells


def passed_along(x, axis, by):
    length = lax.axis_size(axis)
    pairs = [(i, i + by) for i in range(length) if 0 <= i + by < length]
    return lax.ppermute(x, axis, pairs)


def slab_adjoint(left_real, left_imag, right_real, right_imag):
    real_sum = jnp.einsum(
        "qjrb,jsb->qrs", left_real, right_real, preferred_element_type=jnp.float32
    ) + jnp.einsum("qjrb,jsb->qrs", left_imag, right_imag, preferred_element_type=jnp.float32)
    imag_sum = jnp.einsum(
        "qjrb,jsb->qrs", left_imag, right_real, preferred_element_type=jnp.float32
    ) - jnp.einsum("qjrb,jsb->qrs", left_real, right_imag, preferred_element_type=jnp.float32)
    return (real_sum, imag_sum)


def times_adjoint(left_real, left_imag, right_real, right_imag):
    real_sum = jnp.dot(left_real, right_real.T, preferred_element_type=jnp.float32) + jnp.dot(
        left_imag, right_imag.T, preferred_element_type=jnp.float32
    )
    imag_sum = jnp.dot(left_imag, right_real.T, preferred_element_type=jnp.float32) - jnp.dot(
        left_real, right_imag.T, preferred_element_type=jnp.float32
    )
    return (real_sum, imag_sum)


def complex_product(left_real, left_imag, right_real, right_imag):
    real_sum = jnp.dot(left_real, right_real, preferred_element_type=jnp.float32) - jnp.dot(
        left_imag, right_imag, preferred_element_type=jnp.float32
    )
    imag_sum = jnp.dot(left_real, right_imag, preferred_element_type=jnp.float32) + jnp.dot(
        left_imag, right_real, preferred_element_type=jnp.float32
    )
    return (real_sum, imag_sum)


def element_values(own_slab, next_edge, diag_rates, pattern_row):
    block_order = own_slab.shape[3]
    factor = 1.0 / math.sqrt(3.0 * block_order)
    rate_real = jnp.transpose(diag_rates[:, :, 0], (1, 0, 2))[:, :, None, :]
    rate_imag = jnp.transpose(diag_rates[:, :, 1], (1, 0, 2))[:, :, None, :]
    slab_real = own_slab[0].astype(jnp.float32)[None]
    slab_imag = own_slab[1].astype(jnp.float32)[None]
    weighted_real = ((slab_real * rate_real - slab_imag * rate_imag) * factor).astype(jnp.bfloat16)
    weighted_imag = ((slab_real * rate_imag + slab_imag * rate_real) * factor).astype(jnp.bfloat16)
    near_real, near_imag = slab_adjoint(weighted_real, weighted_imag, own_slab[0], own_slab[1])
    edge_real, edge_imag = slab_adjoint(
        weighted_real[:, 1:3], weighted_imag[:, 1:3], next_edge[0], next_edge[1]
    )
    joined_real = jnp.concatenate([near_real, edge_real], axis=2).reshape(2, -1)
    joined_imag = jnp.concatenate([near_imag, edge_imag], axis=2).reshape(2, -1)
    picked_real = jnp.take(joined_real, pattern_row, axis=1)
    picked_imag = jnp.take(joined_imag, pattern_row, axis=1)
    return jnp.stack([picked_real, picked_imag], axis=1).astype(jnp.bfloat16)


def lagged_sums(by_element):
    energy_count = by_element.shape[0]
    column_count = by_element.shape[3]
    lesser = by_element[:, 0].astype(jnp.float32)
    backward = by_element[::-1, 1].astype(jnp.float32)
    real_part = (
        lesser[:, None, 0] * backward[None, :, 0] - lesser[:, None, 1] * backward[None, :, 1]
    )
    imag_part = (
        lesser[:, None, 0] * backward[None, :, 1] + lesser[:, None, 1] * backward[None, :, 0]
    )
    joined = jnp.concatenate([real_part, imag_part], axis=2)
    padded = jnp.pad(joined, ((0, 0), (0, energy_count + 1), (0, 0)))
    flat_rows = padded.reshape(energy_count * (2 * energy_count + 1), 2 * column_count)
    skewed = flat_rows[: energy_count * 2 * energy_count].reshape(
        energy_count, 2 * energy_count, 2 * column_count
    )
    totals = jnp.sum(skewed, axis=0)[energy_count - 1 : 2 * energy_count - 1]
    factor = 1.0 / math.sqrt(energy_count)
    return (totals.reshape(energy_count, 2, column_count) * factor).astype(jnp.bfloat16)


def screen(polar_row, pattern_row, screen_block):
    row_count = screen_block.shape[1]
    col_count = screen_block.shape[2]
    flat_dense = (
        jnp.zeros((2, row_count * col_count), jnp.bfloat16).at[:, pattern_row].set(polar_row)
    )
    dense_pol = flat_dense.reshape(2, row_count, col_count)
    inner_real, inner_imag = times_adjoint(
        dense_pol[0], dense_pol[1], screen_block[0], screen_block[1]
    )
    inner_real = inner_real.astype(jnp.bfloat16)
    inner_imag = inner_imag.astype(jnp.bfloat16)
    near_real = screen_block[0][:, :row_count]
    near_imag = screen_block[1][:, :row_count]
    across_real, across_imag = complex_product(
        near_real, near_imag, dense_pol[0][:, row_count:], dense_pol[1][:, row_count:]
    )
    across_real = across_real.astype(jnp.bfloat16)
    across_imag = across_imag.astype(jnp.bfloat16)
    first_real, first_imag = complex_product(near_real, near_imag, inner_real, inner_imag)
    second_real, second_imag = times_adjoint(
        screen_block[0][:, row_count:], screen_block[1][:, row_count:], across_real, across_imag
    )
    return jnp.stack([first_real + second_real, first_imag + second_imag], axis=0)


def body(green_slab, self_energy, pattern, screened):
    nearby = padded_2(self_energy, (("domain", 1),), 1)
    edge_block = green_slab[0, 0, :, 0:2, :EDGE, :]
    following = passed_along(edge_block, "domain", -1)
    values = element_values(green_slab[0, 0], following, nearby[0], pattern[0])
    chunks = lax.axis_size("energy")
    values = values.reshape(2, 2, chunks, -1).transpose(2, 0, 1, 3)
    by_element = lax.all_to_all(values, "energy", split_axis=0, concat_axis=0, tiled=True)
    polarization = lagged_sums(by_element)
    per_energy = lax.all_to_all(polarization, "energy", split_axis=0, concat_axis=2, tiled=True)
    result = screen(per_energy[0], pattern[0], screened[0, 0])
    return result[None, None]


def solution(mesh):
    placed = (
        P("energy", "domain", None, None, None, None),
        P("energy", "domain", None, None, None),
        P("domain", None),
        P("energy", "domain", None, None, None),
    )
    return jax.shard_map(
        body,
        mesh=mesh,
        in_specs=placed,
        out_specs=P("energy", "domain", None, None, None),
        check_vma=False,
    )
```

```python
import math

import jax
import jax.numpy as jnp
from jax import lax
from jax.sharding import PartitionSpec as P

EDGE = 16


def padded_2(cells, sides, width):
    for axis, dim in sides:
        count = lax.axis_size(axis)
        ends = count - 1
        head = lax.slice_in_dim(cells, 0, width, axis=dim)
        tail = lax.slice_in_dim(cells, cells.shape[dim] - width, cells.shape[dim], axis=dim)
        cells = jnp.concatenate(
            [
                lax.ppermute(tail, axis, [(i, (i + 1) % count) for i in range(ends)]),
                cells,
                lax.ppermute(head, axis, [((i + 1) % count, i) for i in range(ends)]),
            ],
            axis=dim,
        )
    return cells


def passed_along(x, axis, by):
    length = lax.axis_size(axis)
    pairs = [(i, i + by) for i in range(length) if 0 <= i + by < length]
    return lax.ppermute(x, axis, pairs)


def slab_adjoint(left_real, left_imag, right_real, right_imag):
    real_sum = jnp.einsum(
        "qjrb,jsb->qrs", left_real, right_real, preferred_element_type=jnp.float32
    ) + jnp.einsum("qjrb,jsb->qrs", left_imag, right_imag, preferred_element_type=jnp.float32)
    imag_sum = jnp.einsum(
        "qjrb,jsb->qrs", left_imag, right_real, preferred_element_type=jnp.float32
    ) - jnp.einsum("qjrb,jsb->qrs", left_real, right_imag, preferred_element_type=jnp.float32)
    return (real_sum, imag_sum)


def times_adjoint(left_real, left_imag, right_real, right_imag):
    real_sum = jnp.dot(left_real, right_real.T, preferred_element_type=jnp.float32) + jnp.dot(
        left_imag, right_imag.T, preferred_element_type=jnp.float32
    )
    imag_sum = jnp.dot(left_imag, right_real.T, preferred_element_type=jnp.float32) - jnp.dot(
        left_real, right_imag.T, preferred_element_type=jnp.float32
    )
    return (real_sum, imag_sum)


def complex_product(left_real, left_imag, right_real, right_imag):
    real_sum = jnp.dot(left_real, right_real, preferred_element_type=jnp.float32) - jnp.dot(
        left_imag, right_imag, preferred_element_type=jnp.float32
    )
    imag_sum = jnp.dot(left_real, right_imag, preferred_element_type=jnp.float32) + jnp.dot(
        left_imag, right_real, preferred_element_type=jnp.float32
    )
    return (real_sum, imag_sum)


def element_values(own_slab, next_edge, diag_rates, pattern_row):
    block_order = own_slab.shape[3]
    factor = 1.0 / math.sqrt(3.0 * block_order)
    rate_real = jnp.transpose(diag_rates[:, :, 0], (1, 0, 2))[:, :, None, :]
    rate_imag = jnp.transpose(diag_rates[:, :, 1], (1, 0, 2))[:, :, None, :]
    slab_real = own_slab[0].astype(jnp.float32)[None]
    slab_imag = own_slab[1].astype(jnp.float32)[None]
    weighted_real = ((slab_real * rate_real - slab_imag * rate_imag) * factor).astype(jnp.bfloat16)
    weighted_imag = ((slab_real * rate_imag + slab_imag * rate_real) * factor).astype(jnp.bfloat16)
    near_real, near_imag = slab_adjoint(weighted_real, weighted_imag, own_slab[0], own_slab[1])
    edge_real, edge_imag = slab_adjoint(
        weighted_real[:, 1:3], weighted_imag[:, 1:3], next_edge[0], next_edge[1]
    )
    joined_real = jnp.concatenate([near_real, edge_real], axis=2).reshape(2, -1)
    joined_imag = jnp.concatenate([near_imag, edge_imag], axis=2).reshape(2, -1)
    joined = jnp.stack([joined_real, joined_imag], axis=1).astype(jnp.bfloat16)
    return jnp.take(joined.reshape(4, -1), pattern_row, axis=1).reshape(2, 2, -1)


def lagged_sums(by_element):
    energy_count = by_element.shape[0]
    column_count = by_element.shape[3]
    lesser = by_element[:, 0].astype(jnp.float32)
    backward = by_element[::-1, 1].astype(jnp.float32)
    real_part = (
        lesser[:, None, 0] * backward[None, :, 0] - lesser[:, None, 1] * backward[None, :, 1]
    )
    imag_part = (
        lesser[:, None, 0] * backward[None, :, 1] + lesser[:, None, 1] * backward[None, :, 0]
    )
    joined = jnp.concatenate([real_part, imag_part], axis=2)
    padded = jnp.pad(joined, ((0, 0), (0, energy_count + 1), (0, 0)))
    flat_rows = padded.reshape(energy_count * (2 * energy_count + 1), 2 * column_count)
    skewed = flat_rows[: energy_count * 2 * energy_count].reshape(
        energy_count, 2 * energy_count, 2 * column_count
    )
    totals = jnp.sum(skewed, axis=0)[energy_count - 1 : 2 * energy_count - 1]
    factor = 1.0 / math.sqrt(energy_count)
    return (totals.reshape(energy_count, 2, column_count) * factor).astype(jnp.bfloat16)


def screen(polar_row, pattern_row, screen_block):
    row_count = screen_block.shape[1]
    col_count = screen_block.shape[2]
    flat_dense = (
        jnp.zeros((2, row_count * col_count), jnp.bfloat16).at[:, pattern_row].set(polar_row)
    )
    dense_pol = flat_dense.reshape(2, row_count, col_count)
    inner_real, inner_imag = times_adjoint(
        dense_pol[0], dense_pol[1], screen_block[0], screen_block[1]
    )
    inner_real = inner_real.astype(jnp.bfloat16)
    inner_imag = inner_imag.astype(jnp.bfloat16)
    near_real = screen_block[0][:, :row_count]
    near_imag = screen_block[1][:, :row_count]
    across_real, across_imag = complex_product(
        near_real, near_imag, dense_pol[0][:, row_count:], dense_pol[1][:, row_count:]
    )
    across_real = across_real.astype(jnp.bfloat16)
    across_imag = across_imag.astype(jnp.bfloat16)
    first_real, first_imag = complex_product(near_real, near_imag, inner_real, inner_imag)
    second_real, second_imag = times_adjoint(
        screen_block[0][:, row_count:], screen_block[1][:, row_count:], across_real, across_imag
    )
    return jnp.stack([first_real + second_real, first_imag + second_imag], axis=0)


def body(green_slab, self_energy, pattern, screened):
    nearby = padded_2(self_energy, (("domain", 1),), 1)
    edge_block = green_slab[0, 0, :, 0:2, :EDGE, :]
    following = passed_along(edge_block, "domain", -1)
    values = element_values(green_slab[0, 0], following, nearby[0], pattern[0])
    chunks = lax.axis_size("energy")
    values = values.reshape(2, 2, chunks, -1).transpose(2, 0, 1, 3)
    by_element = lax.all_to_all(values, "energy", split_axis=0, concat_axis=0, tiled=True)
    polarization = lagged_sums(by_element)
    per_energy = lax.all_to_all(polarization, "energy", split_axis=0, concat_axis=2, tiled=True)
    result = screen(per_energy[0], pattern[0], screened[0, 0])
    return result[None, None]


def solution(mesh):
    placed = (
        P("energy", "domain", None, None, None, None),
        P("energy", "domain", None, None, None),
        P("domain", None),
        P("energy", "domain", None, None, None),
    )
    return jax.shard_map(
        body,
        mesh=mesh,
        in_specs=placed,
        out_specs=P("energy", "domain", None, None, None),
        check_vma=False,
    )
```

```python
import functools
import math

import jax
import jax.numpy as jnp
from jax import lax
from jax.experimental import pallas as pl
from jax.sharding import PartitionSpec as P

EDGE = 16


def padded_2(cells, sides, width):
    for axis, dim in sides:
        count = lax.axis_size(axis)
        ends = count - 1
        head = lax.slice_in_dim(cells, 0, width, axis=dim)
        tail = lax.slice_in_dim(cells, cells.shape[dim] - width, cells.shape[dim], axis=dim)
        cells = jnp.concatenate(
            [
                lax.ppermute(tail, axis, [(i, (i + 1) % count) for i in range(ends)]),
                cells,
                lax.ppermute(head, axis, [((i + 1) % count, i) for i in range(ends)]),
            ],
            axis=dim,
        )
    return cells


def passed_along(x, axis, by):
    length = lax.axis_size(axis)
    pairs = [(i, i + by) for i in range(length) if 0 <= i + by < length]
    return lax.ppermute(x, axis, pairs)


def times_adjoint(left_real, left_imag, right_real, right_imag):
    real_sum = jnp.dot(left_real, right_real.T, preferred_element_type=jnp.float32) + jnp.dot(
        left_imag, right_imag.T, preferred_element_type=jnp.float32
    )
    imag_sum = jnp.dot(left_imag, right_real.T, preferred_element_type=jnp.float32) - jnp.dot(
        left_real, right_imag.T, preferred_element_type=jnp.float32
    )
    return (real_sum, imag_sum)


def complex_product(left_real, left_imag, right_real, right_imag):
    real_sum = jnp.dot(left_real, right_real, preferred_element_type=jnp.float32) - jnp.dot(
        left_imag, right_imag, preferred_element_type=jnp.float32
    )
    imag_sum = jnp.dot(left_real, right_imag, preferred_element_type=jnp.float32) + jnp.dot(
        left_imag, right_real, preferred_element_type=jnp.float32
    )
    return (real_sum, imag_sum)


def _weigh_kernel(slab_ref, edge_ref, rate_ref, out_ref, *, factor, rows, edge):
    step = pl.program_id(0)

    @pl.when(step == 0)
    def _():
        out_ref[...] = jnp.zeros_like(out_ref)

    slab_real = slab_ref[0, 0]
    slab_imag = slab_ref[1, 0]
    real_f = slab_real.astype(jnp.float32)
    imag_f = slab_imag.astype(jnp.float32)
    pieces = []
    for q in range(2):
        rate_real = rate_ref[0, q, 0:1, :]
        rate_imag = rate_ref[0, q, 1:2, :]
        pieces.append(((real_f * rate_real - imag_f * rate_imag) * factor).astype(jnp.bfloat16))
        pieces.append(((real_f * rate_imag + imag_f * rate_real) * factor).astype(jnp.bfloat16))
    left = jnp.concatenate(pieces, axis=0)
    right = jnp.concatenate([slab_real, slab_imag, edge_ref[0, 0], edge_ref[1, 0]], axis=0)
    prod = lax.dot_general(left, right, (((1,), (1,)), ((), ())), preferred_element_type=jnp.float32)
    for q in range(2):
        wr = prod[2 * q * rows:(2 * q + 1) * rows]
        wi = prod[(2 * q + 1) * rows:(2 * q + 2) * rows]
        out_ref[q, 0, :, 0:rows] += wr[:, 0:rows] + wi[:, rows:2 * rows]
        out_ref[q, 1, :, 0:rows] += wi[:, 0:rows] - wr[:, rows:2 * rows]

        @pl.when(step > 0)
        def _():
            e0 = 2 * rows
            out_ref[q, 0, :, rows:rows + edge] += wr[:, e0:e0 + edge] + wi[:, e0 + edge:e0 + 2 * edge]
            out_ref[q, 1, :, rows:rows + edge] += wi[:, e0:e0 + edge] - wr[:, e0 + edge:e0 + 2 * edge]


def weighed_products(own_slab, next_edge, diag_rates):
    _, blocks, rows, block_order = own_slab.shape
    edge = next_edge.shape[2]
    factor = 1.0 / math.sqrt(3.0 * block_order)
    kernel = functools.partial(_weigh_kernel, factor=factor, rows=rows, edge=edge)
    return pl.pallas_call(
        kernel,
        grid=(blocks,),
        in_specs=[
            pl.BlockSpec((2, 1, rows, block_order), lambda j: (0, j, 0, 0)),
            pl.BlockSpec((2, 1, edge, block_order), lambda j: (0, jnp.maximum(j - 1, 0), 0, 0)),
            pl.BlockSpec((1, 2, 2, block_order), lambda j: (j, 0, 0, 0)),
        ],
        out_specs=pl.BlockSpec((2, 2, rows, rows + edge), lambda j: (0, 0, 0, 0)),
        out_shape=jax.ShapeDtypeStruct((2, 2, rows, rows + edge), jnp.float32),
    )(own_slab, next_edge, diag_rates)


def element_values(own_slab, next_edge, diag_rates, pattern_row):
    joined = weighed_products(own_slab, next_edge, diag_rates).astype(jnp.bfloat16)
    return jnp.take(joined.reshape(4, -1), pattern_row, axis=1).reshape(2, 2, -1)


def lagged_sums(by_element):
    energy_count = by_element.shape[0]
    column_count = by_element.shape[3]
    lesser = by_element[:, 0].astype(jnp.float32)
    backward = by_element[::-1, 1].astype(jnp.float32)
    real_part = (
        lesser[:, None, 0] * backward[None, :, 0] - lesser[:, None, 1] * backward[None, :, 1]
    )
    imag_part = (
        lesser[:, None, 0] * backward[None, :, 1] + lesser[:, None, 1] * backward[None, :, 0]
    )
    joined = jnp.concatenate([real_part, imag_part], axis=2)
    padded = jnp.pad(joined, ((0, 0), (0, energy_count + 1), (0, 0)))
    flat_rows = padded.reshape(energy_count * (2 * energy_count + 1), 2 * column_count)
    skewed = flat_rows[: energy_count * 2 * energy_count].reshape(
        energy_count, 2 * energy_count, 2 * column_count
    )
    totals = jnp.sum(skewed, axis=0)[energy_count - 1 : 2 * energy_count - 1]
    factor = 1.0 / math.sqrt(energy_count)
    return (totals.reshape(energy_count, 2, column_count) * factor).astype(jnp.bfloat16)


def screen(polar_row, pattern_row, screen_block):
    row_count = screen_block.shape[1]
    col_count = screen_block.shape[2]
    flat_dense = (
        jnp.zeros((2, row_count * col_count), jnp.bfloat16).at[:, pattern_row].set(polar_row)
    )
    dense_pol = flat_dense.reshape(2, row_count, col_count)
    inner_real, inner_imag = times_adjoint(
        dense_pol[0], dense_pol[1], screen_block[0], screen_block[1]
    )
    inner_real = inner_real.astype(jnp.bfloat16)
    inner_imag = inner_imag.astype(jnp.bfloat16)
    near_real = screen_block[0][:, :row_count]
    near_imag = screen_block[1][:, :row_count]
    across_real, across_imag = complex_product(
        near_real, near_imag, dense_pol[0][:, row_count:], dense_pol[1][:, row_count:]
    )
    across_real = across_real.astype(jnp.bfloat16)
    across_imag = across_imag.astype(jnp.bfloat16)
    first_real, first_imag = complex_product(near_real, near_imag, inner_real, inner_imag)
    second_real, second_imag = times_adjoint(
        screen_block[0][:, row_count:], screen_block[1][:, row_count:], across_real, across_imag
    )
    return jnp.stack([first_real + second_real, first_imag + second_imag], axis=0)


def body(green_slab, self_energy, pattern, screened):
    nearby = padded_2(self_energy, (("domain", 1),), 1)
    edge_block = green_slab[0, 0, :, 0:2, :EDGE, :]
    following = passed_along(edge_block, "domain", -1)
    values = element_values(green_slab[0, 0], following, nearby[0], pattern[0])
    chunks = lax.axis_size("energy")
    values = values.reshape(2, 2, chunks, -1).transpose(2, 0, 1, 3)
    by_element = lax.all_to_all(values, "energy", split_axis=0, concat_axis=0, tiled=True)
    polarization = lagged_sums(by_element)
    per_energy = lax.all_to_all(polarization, "energy", split_axis=0, concat_axis=2, tiled=True)
    result = screen(per_energy[0], pattern[0], screened[0, 0])
    return result[None, None]


def solution(mesh):
    placed = (
        P("energy", "domain", None, None, None, None),
        P("energy", "domain", None, None, None),
        P("domain", None),
        P("energy", "domain", None, None, None),
    )
    return jax.shard_map(
        body,
        mesh=mesh,
        in_specs=placed,
        out_specs=P("energy", "domain", None, None, None),
        check_vma=False,
    )
```

```python
import functools
import math

import jax
import jax.numpy as jnp
from jax import lax
from jax.experimental import pallas as pl
from jax.sharding import PartitionSpec as P

EDGE = 16


def padded_2(cells, sides, width):
    for axis, dim in sides:
        count = lax.axis_size(axis)
        ends = count - 1
        head = lax.slice_in_dim(cells, 0, width, axis=dim)
        tail = lax.slice_in_dim(cells, cells.shape[dim] - width, cells.shape[dim], axis=dim)
        cells = jnp.concatenate(
            [
                lax.ppermute(tail, axis, [(i, (i + 1) % count) for i in range(ends)]),
                cells,
                lax.ppermute(head, axis, [((i + 1) % count, i) for i in range(ends)]),
            ],
            axis=dim,
        )
    return cells


def passed_along(x, axis, by):
    length = lax.axis_size(axis)
    pairs = [(i, i + by) for i in range(length) if 0 <= i + by < length]
    return lax.ppermute(x, axis, pairs)


def times_adjoint(left_real, left_imag, right_real, right_imag):
    real_sum = jnp.dot(left_real, right_real.T, preferred_element_type=jnp.float32) + jnp.dot(
        left_imag, right_imag.T, preferred_element_type=jnp.float32
    )
    imag_sum = jnp.dot(left_imag, right_real.T, preferred_element_type=jnp.float32) - jnp.dot(
        left_real, right_imag.T, preferred_element_type=jnp.float32
    )
    return (real_sum, imag_sum)


def complex_product(left_real, left_imag, right_real, right_imag):
    real_sum = jnp.dot(left_real, right_real, preferred_element_type=jnp.float32) - jnp.dot(
        left_imag, right_imag, preferred_element_type=jnp.float32
    )
    imag_sum = jnp.dot(left_real, right_imag, preferred_element_type=jnp.float32) + jnp.dot(
        left_imag, right_real, preferred_element_type=jnp.float32
    )
    return (real_sum, imag_sum)


def _weigh_kernel(slab_ref, edge_ref, rate_ref, out_ref, *, factor, rows, edge):
    step = pl.program_id(0)

    @pl.when(step == 0)
    def _():
        out_ref[...] = jnp.zeros_like(out_ref)

    slab_real = slab_ref[0, 0]
    slab_imag = slab_ref[1, 0]
    real_f = slab_real.astype(jnp.float32)
    imag_f = slab_imag.astype(jnp.float32)
    pieces = []
    for q in range(2):
        rate_real = rate_ref[0, q, 0:1, :]
        rate_imag = rate_ref[0, q, 1:2, :]
        pieces.append(((real_f * rate_real - imag_f * rate_imag) * factor).astype(jnp.bfloat16))
        pieces.append(((real_f * rate_imag + imag_f * rate_real) * factor).astype(jnp.bfloat16))
    left = jnp.concatenate(pieces, axis=0)
    right = jnp.concatenate([slab_real, slab_imag, edge_ref[0, 0], edge_ref[1, 0]], axis=0)
    prod = lax.dot_general(left, right, (((1,), (1,)), ((), ())), preferred_element_type=jnp.float32)
    for q in range(2):
        wr = prod[2 * q * rows:(2 * q + 1) * rows]
        wi = prod[(2 * q + 1) * rows:(2 * q + 2) * rows]
        out_ref[q, 0, :, 0:rows] += wr[:, 0:rows] + wi[:, rows:2 * rows]
        out_ref[q, 1, :, 0:rows] += wi[:, 0:rows] - wr[:, rows:2 * rows]

        @pl.when(step > 0)
        def _():
            e0 = 2 * rows
            out_ref[q, 0, :, rows:rows + edge] += wr[:, e0:e0 + edge] + wi[:, e0 + edge:e0 + 2 * edge]
            out_ref[q, 1, :, rows:rows + edge] += wi[:, e0:e0 + edge] - wr[:, e0 + edge:e0 + 2 * edge]


def weighed_products(own_slab, next_edge, diag_rates):
    _, blocks, rows, block_order = own_slab.shape
    edge = next_edge.shape[2]
    factor = 1.0 / math.sqrt(3.0 * block_order)
    kernel = functools.partial(_weigh_kernel, factor=factor, rows=rows, edge=edge)
    return pl.pallas_call(
        kernel,
        grid=(blocks,),
        in_specs=[
            pl.BlockSpec((2, 1, rows, block_order), lambda j: (0, j, 0, 0)),
            pl.BlockSpec((2, 1, edge, block_order), lambda j: (0, jnp.maximum(j - 1, 0), 0, 0)),
            pl.BlockSpec((1, 2, 2, block_order), lambda j: (j, 0, 0, 0)),
        ],
        out_specs=pl.BlockSpec((2, 2, rows, rows + edge), lambda j: (0, 0, 0, 0)),
        out_shape=jax.ShapeDtypeStruct((2, 2, rows, rows + edge), jnp.float32),
    )(own_slab, next_edge, diag_rates)


def element_values(own_slab, next_edge, diag_rates, pattern_row):
    joined = weighed_products(own_slab, next_edge, diag_rates).astype(jnp.bfloat16)
    return jnp.take(joined.reshape(4, -1), pattern_row, axis=1).reshape(2, 2, -1)


def _lag_kernel(in_ref, out_ref, *, width, factor):
    values = in_ref[...].astype(jnp.float32)
    energy_count = values.shape[0]
    lesser = values[:, 0:2 * width]
    greater = values[:, 2 * width:4 * width]
    swapped = jnp.concatenate([greater[:, width:], greater[:, :width]], axis=1)
    rows = []
    for lag in range(energy_count):
        head = lesser[lag:]
        straight = jnp.sum(head * greater[:energy_count - lag], axis=0, keepdims=True)
        crossed = jnp.sum(head * swapped[:energy_count - lag], axis=0, keepdims=True)
        rows.append(jnp.concatenate([straight[:, :width] - straight[:, width:], crossed[:, :width] + crossed[:, width:]], axis=1))
    out_ref[...] = (jnp.concatenate(rows, axis=0) * factor).astype(out_ref.dtype)


def lag_sums(by_element):
    energy_count, joined = by_element.shape
    width = joined // 4
    kernel = functools.partial(_lag_kernel, width=width, factor=1.0 / math.sqrt(energy_count))
    return pl.pallas_call(
        kernel,
        out_shape=jax.ShapeDtypeStruct((energy_count, 2 * width), jnp.bfloat16),
    )(by_element)


def screen(polar_row, pattern_row, screen_block):
    row_count = screen_block.shape[1]
    col_count = screen_block.shape[2]
    flat_dense = (
        jnp.zeros((2, row_count * col_count), jnp.bfloat16).at[:, pattern_row].set(polar_row)
    )
    dense_pol = flat_dense.reshape(2, row_count, col_count)
    inner_real, inner_imag = times_adjoint(
        dense_pol[0], dense_pol[1], screen_block[0], screen_block[1]
    )
    inner_real = inner_real.astype(jnp.bfloat16)
    inner_imag = inner_imag.astype(jnp.bfloat16)
    near_real = screen_block[0][:, :row_count]
    near_imag = screen_block[1][:, :row_count]
    across_real, across_imag = complex_product(
        near_real, near_imag, dense_pol[0][:, row_count:], dense_pol[1][:, row_count:]
    )
    across_real = across_real.astype(jnp.bfloat16)
    across_imag = across_imag.astype(jnp.bfloat16)
    first_real, first_imag = complex_product(near_real, near_imag, inner_real, inner_imag)
    second_real, second_imag = times_adjoint(
        screen_block[0][:, row_count:], screen_block[1][:, row_count:], across_real, across_imag
    )
    return jnp.stack([first_real + second_real, first_imag + second_imag], axis=0)


def body(green_slab, self_energy, pattern, screened):
    nearby = padded_2(self_energy, (("domain", 1),), 1)
    edge_block = green_slab[0, 0, :, 0:2, :EDGE, :]
    following = passed_along(edge_block, "domain", -1)
    values = element_values(green_slab[0, 0], following, nearby[0], pattern[0])
    chunks = lax.axis_size("energy")
    values = values.reshape(4, chunks, -1).transpose(1, 0, 2).reshape(chunks, -1)
    by_element = lax.all_to_all(values, "energy", split_axis=0, concat_axis=0, tiled=True)
    polarization = lag_sums(by_element)
    per_energy = lax.all_to_all(polarization, "energy", split_axis=0, concat_axis=0, tiled=True)
    per_energy = per_energy.reshape(chunks, 2, -1).transpose(1, 0, 2).reshape(2, -1)
    result = screen(per_energy, pattern[0], screened[0, 0])
    return result[None, None]


def solution(mesh):
    placed = (
        P("energy", "domain", None, None, None, None),
        P("energy", "domain", None, None, None),
        P("domain", None),
        P("energy", "domain", None, None, None),
    )
    return jax.shard_map(
        body,
        mesh=mesh,
        in_specs=placed,
        out_specs=P("energy", "domain", None, None, None),
        check_vma=False,
    )
```

```python
import functools
import math

import jax
import jax.numpy as jnp
from jax import lax
from jax.experimental import pallas as pl
from jax.sharding import Mesh, PartitionSpec as P

EDGE = 16
ENERGY = ("energy_outer", "energy_inner")


def padded_2(cells, sides, width):
    for axis, dim in sides:
        count = lax.axis_size(axis)
        ends = count - 1
        head = lax.slice_in_dim(cells, 0, width, axis=dim)
        tail = lax.slice_in_dim(cells, cells.shape[dim] - width, cells.shape[dim], axis=dim)
        cells = jnp.concatenate(
            [
                lax.ppermute(tail, axis, [(i, (i + 1) % count) for i in range(ends)]),
                cells,
                lax.ppermute(head, axis, [((i + 1) % count, i) for i in range(ends)]),
            ],
            axis=dim,
        )
    return cells


def passed_along(x, axis, by):
    length = lax.axis_size(axis)
    pairs = [(i, i + by) for i in range(length) if 0 <= i + by < length]
    return lax.ppermute(x, axis, pairs)


def times_adjoint(left_real, left_imag, right_real, right_imag):
    real_sum = jnp.dot(left_real, right_real.T, preferred_element_type=jnp.float32) + jnp.dot(
        left_imag, right_imag.T, preferred_element_type=jnp.float32
    )
    imag_sum = jnp.dot(left_imag, right_real.T, preferred_element_type=jnp.float32) - jnp.dot(
        left_real, right_imag.T, preferred_element_type=jnp.float32
    )
    return (real_sum, imag_sum)


def complex_product(left_real, left_imag, right_real, right_imag):
    real_sum = jnp.dot(left_real, right_real, preferred_element_type=jnp.float32) - jnp.dot(
        left_imag, right_imag, preferred_element_type=jnp.float32
    )
    imag_sum = jnp.dot(left_real, right_imag, preferred_element_type=jnp.float32) + jnp.dot(
        left_imag, right_real, preferred_element_type=jnp.float32
    )
    return (real_sum, imag_sum)


def _weigh_kernel(slab_ref, edge_ref, rate_ref, out_ref, *, factor, rows, edge):
    step = pl.program_id(0)

    @pl.when(step == 0)
    def _():
        out_ref[...] = jnp.zeros_like(out_ref)

    slab_real = slab_ref[0, 0]
    slab_imag = slab_ref[1, 0]
    real_f = slab_real.astype(jnp.float32)
    imag_f = slab_imag.astype(jnp.float32)
    pieces = []
    for q in range(2):
        rate_real = rate_ref[0, q, 0:1, :]
        rate_imag = rate_ref[0, q, 1:2, :]
        pieces.append(((real_f * rate_real - imag_f * rate_imag) * factor).astype(jnp.bfloat16))
        pieces.append(((real_f * rate_imag + imag_f * rate_real) * factor).astype(jnp.bfloat16))
    left = jnp.concatenate(pieces, axis=0)
    right = jnp.concatenate([slab_real, slab_imag, edge_ref[0, 0], edge_ref[1, 0]], axis=0)
    prod = lax.dot_general(left, right, (((1,), (1,)), ((), ())), preferred_element_type=jnp.float32)
    for q in range(2):
        wr = prod[2 * q * rows:(2 * q + 1) * rows]
        wi = prod[(2 * q + 1) * rows:(2 * q + 2) * rows]
        out_ref[q, 0, :, 0:rows] += wr[:, 0:rows] + wi[:, rows:2 * rows]
        out_ref[q, 1, :, 0:rows] += wi[:, 0:rows] - wr[:, rows:2 * rows]

        @pl.when(step > 0)
        def _():
            e0 = 2 * rows
            out_ref[q, 0, :, rows:rows + edge] += wr[:, e0:e0 + edge] + wi[:, e0 + edge:e0 + 2 * edge]
            out_ref[q, 1, :, rows:rows + edge] += wi[:, e0:e0 + edge] - wr[:, e0 + edge:e0 + 2 * edge]


def weighed_products(own_slab, next_edge, diag_rates):
    _, blocks, rows, block_order = own_slab.shape
    edge = next_edge.shape[2]
    factor = 1.0 / math.sqrt(3.0 * block_order)
    kernel = functools.partial(_weigh_kernel, factor=factor, rows=rows, edge=edge)
    return pl.pallas_call(
        kernel,
        grid=(blocks,),
        in_specs=[
            pl.BlockSpec((2, 1, rows, block_order), lambda j: (0, j, 0, 0)),
            pl.BlockSpec((2, 1, edge, block_order), lambda j: (0, jnp.maximum(j - 1, 0), 0, 0)),
            pl.BlockSpec((1, 2, 2, block_order), lambda j: (j, 0, 0, 0)),
        ],
        out_specs=pl.BlockSpec((2, 2, rows, rows + edge), lambda j: (0, 0, 0, 0)),
        out_shape=jax.ShapeDtypeStruct((2, 2, rows, rows + edge), jnp.float32),
    )(own_slab, next_edge, diag_rates)


def element_values(own_slab, next_edge, diag_rates, pattern_row):
    joined = weighed_products(own_slab, next_edge, diag_rates).astype(jnp.bfloat16)
    return jnp.take(joined.reshape(4, -1), pattern_row, axis=1).reshape(2, 2, -1)


def _lag_kernel(in_ref, out_ref, *, width, factor):
    values = in_ref[...].astype(jnp.float32)
    energy_count = values.shape[0]
    lesser = values[:, 0:2 * width]
    greater = values[:, 2 * width:4 * width]
    swapped = jnp.concatenate([greater[:, width:], greater[:, :width]], axis=1)
    rows = []
    for lag in range(energy_count):
        head = lesser[lag:]
        straight = jnp.sum(head * greater[:energy_count - lag], axis=0, keepdims=True)
        crossed = jnp.sum(head * swapped[:energy_count - lag], axis=0, keepdims=True)
        rows.append(jnp.concatenate([straight[:, :width] - straight[:, width:], crossed[:, :width] + crossed[:, width:]], axis=1))
    out_ref[...] = (jnp.concatenate(rows, axis=0) * factor).astype(out_ref.dtype)


def lag_sums(by_element):
    energy_count, joined = by_element.shape
    width = joined // 4
    kernel = functools.partial(_lag_kernel, width=width, factor=1.0 / math.sqrt(energy_count))
    return pl.pallas_call(
        kernel,
        out_shape=jax.ShapeDtypeStruct((energy_count, 2 * width), jnp.bfloat16),
    )(by_element)


def screen(polar_row, pattern_row, screen_block):
    row_count = screen_block.shape[1]
    col_count = screen_block.shape[2]
    flat_dense = (
        jnp.zeros((2, row_count * col_count), jnp.bfloat16).at[:, pattern_row].set(polar_row)
    )
    dense_pol = flat_dense.reshape(2, row_count, col_count)
    inner_real, inner_imag = times_adjoint(
        dense_pol[0], dense_pol[1], screen_block[0], screen_block[1]
    )
    inner_real = inner_real.astype(jnp.bfloat16)
    inner_imag = inner_imag.astype(jnp.bfloat16)
    near_real = screen_block[0][:, :row_count]
    near_imag = screen_block[1][:, :row_count]
    across_real, across_imag = complex_product(
        near_real, near_imag, dense_pol[0][:, row_count:], dense_pol[1][:, row_count:]
    )
    across_real = across_real.astype(jnp.bfloat16)
    across_imag = across_imag.astype(jnp.bfloat16)
    first_real, first_imag = complex_product(near_real, near_imag, inner_real, inner_imag)
    second_real, second_imag = times_adjoint(
        screen_block[0][:, row_count:], screen_block[1][:, row_count:], across_real, across_imag
    )
    return jnp.stack([first_real + second_real, first_imag + second_imag], axis=0)


def staged_all_to_all(chunked):
    outer = lax.axis_size(ENERGY[0])
    inner = lax.axis_size(ENERGY[1])
    rest = chunked.shape[1:]
    grid = chunked.reshape(outer, inner, *rest)
    grid = lax.all_to_all(grid, ENERGY[1], split_axis=1, concat_axis=1, tiled=True)
    grid = lax.all_to_all(grid, ENERGY[0], split_axis=0, concat_axis=0, tiled=True)
    return grid.reshape(outer * inner, *rest)


def body(green_slab, self_energy, pattern, screened):
    nearby = padded_2(self_energy, (("domain", 1),), 1)
    edge_block = green_slab[0, 0, :, 0:2, :EDGE, :]
    following = passed_along(edge_block, "domain", -1)
    values = element_values(green_slab[0, 0], following, nearby[0], pattern[0])
    chunks = lax.axis_size(ENERGY)
    values = values.reshape(4, chunks, -1).transpose(1, 0, 2).reshape(chunks, -1)
    by_element = staged_all_to_all(values)
    polarization = lag_sums(by_element)
    per_energy = staged_all_to_all(polarization)
    per_energy = per_energy.reshape(chunks, 2, -1).transpose(1, 0, 2).reshape(2, -1)
    result = screen(per_energy, pattern[0], screened[0, 0])
    return result[None, None]


def solution(mesh):
    energy_count = mesh.shape["energy"]
    outer = 1
    while outer * outer < energy_count:
        outer *= 2
    staged = Mesh(
        mesh.devices.reshape(outer, energy_count // outer, mesh.shape["domain"]),
        (*ENERGY, "domain"),
    )
    placed = (
        P(ENERGY, "domain", None, None, None, None),
        P(ENERGY, "domain", None, None, None),
        P("domain", None),
        P(ENERGY, "domain", None, None, None),
    )
    return jax.shard_map(
        body,
        mesh=staged,
        in_specs=placed,
        out_specs=P(ENERGY, "domain", None, None, None),
        check_vma=False,
    )
```

```python
import functools
import math

import jax
import jax.numpy as jnp
from jax import lax
from jax.experimental import pallas as pl
from jax.sharding import PartitionSpec as P

EDGE = 16


def padded_2(cells, sides, width):
    for axis, dim in sides:
        count = lax.axis_size(axis)
        ends = count - 1
        head = lax.slice_in_dim(cells, 0, width, axis=dim)
        tail = lax.slice_in_dim(cells, cells.shape[dim] - width, cells.shape[dim], axis=dim)
        cells = jnp.concatenate(
            [
                lax.ppermute(tail, axis, [(i, (i + 1) % count) for i in range(ends)]),
                cells,
                lax.ppermute(head, axis, [((i + 1) % count, i) for i in range(ends)]),
            ],
            axis=dim,
        )
    return cells


def passed_along(x, axis, by):
    length = lax.axis_size(axis)
    pairs = [(i, i + by) for i in range(length) if 0 <= i + by < length]
    return lax.ppermute(x, axis, pairs)


def _weigh_kernel(slab_ref, edge_ref, rate_ref, out_ref, *, factor, rows, edge):
    step = pl.program_id(0)

    @pl.when(step == 0)
    def _():
        out_ref[...] = jnp.zeros_like(out_ref)

    slab_real = slab_ref[0, 0]
    slab_imag = slab_ref[1, 0]
    real_f = slab_real.astype(jnp.float32)
    imag_f = slab_imag.astype(jnp.float32)
    pieces = []
    for q in range(2):
        rate_real = rate_ref[0, q, 0:1, :]
        rate_imag = rate_ref[0, q, 1:2, :]
        pieces.append(((real_f * rate_real - imag_f * rate_imag) * factor).astype(jnp.bfloat16))
        pieces.append(((real_f * rate_imag + imag_f * rate_real) * factor).astype(jnp.bfloat16))
    left = jnp.concatenate(pieces, axis=0)
    right = jnp.concatenate([slab_real, slab_imag, edge_ref[0, 0], edge_ref[1, 0]], axis=0)
    prod = lax.dot_general(left, right, (((1,), (1,)), ((), ())), preferred_element_type=jnp.float32)
    for q in range(2):
        wr = prod[2 * q * rows:(2 * q + 1) * rows]
        wi = prod[(2 * q + 1) * rows:(2 * q + 2) * rows]
        out_ref[q, 0, :, 0:rows] += wr[:, 0:rows] + wi[:, rows:2 * rows]
        out_ref[q, 1, :, 0:rows] += wi[:, 0:rows] - wr[:, rows:2 * rows]

        @pl.when(step > 0)
        def _():
            e0 = 2 * rows
            out_ref[q, 0, :, rows:rows + edge] += wr[:, e0:e0 + edge] + wi[:, e0 + edge:e0 + 2 * edge]
            out_ref[q, 1, :, rows:rows + edge] += wi[:, e0:e0 + edge] - wr[:, e0 + edge:e0 + 2 * edge]


def weighed_products(own_slab, next_edge, diag_rates):
    _, blocks, rows, block_order = own_slab.shape
    edge = next_edge.shape[2]
    factor = 1.0 / math.sqrt(3.0 * block_order)
    kernel = functools.partial(_weigh_kernel, factor=factor, rows=rows, edge=edge)
    return pl.pallas_call(
        kernel,
        grid=(blocks,),
        in_specs=[
            pl.BlockSpec((2, 1, rows, block_order), lambda j: (0, j, 0, 0)),
            pl.BlockSpec((2, 1, edge, block_order), lambda j: (0, jnp.maximum(j - 1, 0), 0, 0)),
            pl.BlockSpec((1, 2, 2, block_order), lambda j: (j, 0, 0, 0)),
        ],
        out_specs=pl.BlockSpec((2, 2, rows, rows + edge), lambda j: (0, 0, 0, 0)),
        out_shape=jax.ShapeDtypeStruct((2, 2, rows, rows + edge), jnp.float32),
    )(own_slab, next_edge, diag_rates)


def element_values(own_slab, next_edge, diag_rates, pattern_row):
    joined = weighed_products(own_slab, next_edge, diag_rates).astype(jnp.bfloat16)
    return jnp.take(joined.reshape(4, -1), pattern_row, axis=1).reshape(2, 2, -1)


def _lag_kernel(in_ref, out_ref, *, width, factor):
    values = in_ref[...].astype(jnp.float32)
    energy_count = values.shape[0]
    lesser = values[:, 0:2 * width]
    greater = values[:, 2 * width:4 * width]
    swapped = jnp.concatenate([greater[:, width:], greater[:, :width]], axis=1)
    rows = []
    for lag in range(energy_count):
        head = lesser[lag:]
        straight = jnp.sum(head * greater[:energy_count - lag], axis=0, keepdims=True)
        crossed = jnp.sum(head * swapped[:energy_count - lag], axis=0, keepdims=True)
        rows.append(jnp.concatenate([straight[:, :width] - straight[:, width:], crossed[:, :width] + crossed[:, width:]], axis=1))
    out_ref[...] = (jnp.concatenate(rows, axis=0) * factor).astype(out_ref.dtype)


def lag_sums(by_element):
    energy_count, joined = by_element.shape
    width = joined // 4
    kernel = functools.partial(_lag_kernel, width=width, factor=1.0 / math.sqrt(energy_count))
    return pl.pallas_call(
        kernel,
        out_shape=jax.ShapeDtypeStruct((energy_count, 2 * width), jnp.bfloat16),
    )(by_element)


def _screen_kernel(dense_ref, screen_ref, out_ref, *, rows):
    def nt(a, b):
        return lax.dot_general(a, b, (((1,), (1,)), ((), ())), preferred_element_type=jnp.float32)

    def nn(a, b):
        return jnp.dot(a, b, preferred_element_type=jnp.float32)

    dense_real = dense_ref[0]
    dense_imag = dense_ref[1]
    screen_real = screen_ref[0]
    screen_imag = screen_ref[1]
    inner_real = (nt(dense_real, screen_real) + nt(dense_imag, screen_imag)).astype(jnp.bfloat16)
    inner_imag = (nt(dense_imag, screen_real) - nt(dense_real, screen_imag)).astype(jnp.bfloat16)
    near_real = screen_real[:, :rows]
    near_imag = screen_imag[:, :rows]
    side_real = screen_real[:, rows:]
    side_imag = screen_imag[:, rows:]
    edge_real = dense_real[:, rows:]
    edge_imag = dense_imag[:, rows:]
    across_real = (nn(near_real, edge_real) - nn(near_imag, edge_imag)).astype(jnp.bfloat16)
    across_imag = (nn(near_real, edge_imag) + nn(near_imag, edge_real)).astype(jnp.bfloat16)
    first_real = nn(near_real, inner_real) - nn(near_imag, inner_imag)
    first_imag = nn(near_real, inner_imag) + nn(near_imag, inner_real)
    second_real = nt(side_real, across_real) + nt(side_imag, across_imag)
    second_imag = nt(side_imag, across_real) - nt(side_real, across_imag)
    out_ref[0] = first_real + second_real
    out_ref[1] = first_imag + second_imag


def screen_products(dense_pol, screen_block):
    rows = screen_block.shape[1]
    kernel = functools.partial(_screen_kernel, rows=rows)
    return pl.pallas_call(
        kernel,
        out_shape=jax.ShapeDtypeStruct((2, rows, rows), jnp.float32),
    )(dense_pol, screen_block)


def screen(polar_row, pattern_row, screen_block):
    row_count = screen_block.shape[1]
    col_count = screen_block.shape[2]
    flat_dense = (
        jnp.zeros((2, row_count * col_count), jnp.bfloat16).at[:, pattern_row].set(polar_row)
    )
    return screen_products(flat_dense.reshape(2, row_count, col_count), screen_block)


def body(green_slab, self_energy, pattern, screened):
    nearby = padded_2(self_energy, (("domain", 1),), 1)
    edge_block = green_slab[0, 0, :, 0:2, :EDGE, :]
    following = passed_along(edge_block, "domain", -1)
    values = element_values(green_slab[0, 0], following, nearby[0], pattern[0])
    chunks = lax.axis_size("energy")
    values = values.reshape(4, chunks, -1).transpose(1, 0, 2).reshape(chunks, -1)
    by_element = lax.all_to_all(values, "energy", split_axis=0, concat_axis=0, tiled=True)
    polarization = lag_sums(by_element)
    per_energy = lax.all_to_all(polarization, "energy", split_axis=0, concat_axis=0, tiled=True)
    per_energy = per_energy.reshape(chunks, 2, -1).transpose(1, 0, 2).reshape(2, -1)
    result = screen(per_energy, pattern[0], screened[0, 0])
    return result[None, None]


def solution(mesh):
    placed = (
        P("energy", "domain", None, None, None, None),
        P("energy", "domain", None, None, None),
        P("domain", None),
        P("energy", "domain", None, None, None),
    )
    return jax.shard_map(
        body,
        mesh=mesh,
        in_specs=placed,
        out_specs=P("energy", "domain", None, None, None),
        check_vma=False,
    )
```

```python
import functools
import math

import jax
import jax.numpy as jnp
from jax import lax
from jax.experimental import pallas as pl
from jax.sharding import PartitionSpec as P

EDGE = 16


def passed_along(x, axis, by):
    length = lax.axis_size(axis)
    pairs = [(i, i + by) for i in range(length) if 0 <= i + by < length]
    return lax.ppermute(x, axis, pairs)


def _weigh_kernel(slab_ref, edge_ref, rate_ref, out_ref, *, factor, rows, edge):
    step = pl.program_id(0)

    @pl.when(step == 0)
    def _():
        out_ref[...] = jnp.zeros_like(out_ref)

    slab_real = slab_ref[0, 0]
    slab_imag = slab_ref[1, 0]
    real_f = slab_real.astype(jnp.float32)
    imag_f = slab_imag.astype(jnp.float32)
    pieces = []
    for q in range(2):
        rate_real = rate_ref[0, q, 0:1, :]
        rate_imag = rate_ref[0, q, 1:2, :]
        pieces.append(((real_f * rate_real - imag_f * rate_imag) * factor).astype(jnp.bfloat16))
        pieces.append(((real_f * rate_imag + imag_f * rate_real) * factor).astype(jnp.bfloat16))
    left = jnp.concatenate(pieces, axis=0)
    right = jnp.concatenate([slab_real, slab_imag, edge_ref[0, 0], edge_ref[1, 0]], axis=0)
    prod = lax.dot_general(left, right, (((1,), (1,)), ((), ())), preferred_element_type=jnp.float32)
    for q in range(2):
        wr = prod[2 * q * rows:(2 * q + 1) * rows]
        wi = prod[(2 * q + 1) * rows:(2 * q + 2) * rows]
        out_ref[q, 0, :, 0:rows] += wr[:, 0:rows] + wi[:, rows:2 * rows]
        out_ref[q, 1, :, 0:rows] += wi[:, 0:rows] - wr[:, rows:2 * rows]

        @pl.when(step > 0)
        def _():
            e0 = 2 * rows
            out_ref[q, 0, :, rows:rows + edge] += wr[:, e0:e0 + edge] + wi[:, e0 + edge:e0 + 2 * edge]
            out_ref[q, 1, :, rows:rows + edge] += wi[:, e0:e0 + edge] - wr[:, e0 + edge:e0 + 2 * edge]


def weighed_products(own_slab, next_edge, diag_rates):
    _, blocks, rows, block_order = own_slab.shape
    edge = next_edge.shape[2]
    factor = 1.0 / math.sqrt(3.0 * block_order)
    kernel = functools.partial(_weigh_kernel, factor=factor, rows=rows, edge=edge)
    return pl.pallas_call(
        kernel,
        grid=(blocks,),
        in_specs=[
            pl.BlockSpec((2, 1, rows, block_order), lambda j: (0, j, 0, 0)),
            pl.BlockSpec((2, 1, edge, block_order), lambda j: (0, jnp.maximum(j - 1, 0), 0, 0)),
            pl.BlockSpec((1, 2, 2, block_order), lambda j: (j, 0, 0, 0)),
        ],
        out_specs=pl.BlockSpec((2, 2, rows, rows + edge), lambda j: (0, 0, 0, 0)),
        out_shape=jax.ShapeDtypeStruct((2, 2, rows, rows + edge), jnp.float32),
    )(own_slab, next_edge, diag_rates)


def element_values(own_slab, next_edge, diag_rates, pattern_row):
    joined = weighed_products(own_slab, next_edge, diag_rates).astype(jnp.bfloat16)
    return jnp.take(joined.reshape(4, -1), pattern_row, axis=1).reshape(2, 2, -1)


def _lag_kernel(in_ref, out_ref, *, width, factor):
    values = in_ref[...].astype(jnp.float32)
    energy_count = values.shape[0]
    lesser = values[:, 0:2 * width]
    greater = values[:, 2 * width:4 * width]
    swapped = jnp.concatenate([greater[:, width:], greater[:, :width]], axis=1)
    rows = []
    for lag in range(energy_count):
        head = lesser[lag:]
        straight = jnp.sum(head * greater[:energy_count - lag], axis=0, keepdims=True)
        crossed = jnp.sum(head * swapped[:energy_count - lag], axis=0, keepdims=True)
        rows.append(jnp.concatenate([straight[:, :width] - straight[:, width:], crossed[:, :width] + crossed[:, width:]], axis=1))
    out_ref[...] = (jnp.concatenate(rows, axis=0) * factor).astype(out_ref.dtype)


def lag_sums(by_element):
    energy_count, joined = by_element.shape
    width = joined // 4
    kernel = functools.partial(_lag_kernel, width=width, factor=1.0 / math.sqrt(energy_count))
    return pl.pallas_call(
        kernel,
        out_shape=jax.ShapeDtypeStruct((energy_count, 2 * width), jnp.bfloat16),
    )(by_element)


def _screen_kernel(dense_ref, screen_ref, out_ref, *, rows):
    def nt(a, b):
        return lax.dot_general(a, b, (((1,), (1,)), ((), ())), preferred_element_type=jnp.float32)

    def nn(a, b):
        return jnp.dot(a, b, preferred_element_type=jnp.float32)

    dense_real = dense_ref[0]
    dense_imag = dense_ref[1]
    screen_real = screen_ref[0]
    screen_imag = screen_ref[1]
    inner_real = (nt(dense_real, screen_real) + nt(dense_imag, screen_imag)).astype(jnp.bfloat16)
    inner_imag = (nt(dense_imag, screen_real) - nt(dense_real, screen_imag)).astype(jnp.bfloat16)
    near_real = screen_real[:, :rows]
    near_imag = screen_imag[:, :rows]
    side_real = screen_real[:, rows:]
    side_imag = screen_imag[:, rows:]
    edge_real = dense_real[:, rows:]
    edge_imag = dense_imag[:, rows:]
    across_real = (nn(near_real, edge_real) - nn(near_imag, edge_imag)).astype(jnp.bfloat16)
    across_imag = (nn(near_real, edge_imag) + nn(near_imag, edge_real)).astype(jnp.bfloat16)
    first_real = nn(near_real, inner_real) - nn(near_imag, inner_imag)
    first_imag = nn(near_real, inner_imag) + nn(near_imag, inner_real)
    second_real = nt(side_real, across_real) + nt(side_imag, across_imag)
    second_imag = nt(side_imag, across_real) - nt(side_real, across_imag)
    out_ref[0] = first_real + second_real
    out_ref[1] = first_imag + second_imag


def screen_products(dense_pol, screen_block):
    rows = screen_block.shape[1]
    kernel = functools.partial(_screen_kernel, rows=rows)
    return pl.pallas_call(
        kernel,
        out_shape=jax.ShapeDtypeStruct((2, rows, rows), jnp.float32),
    )(dense_pol, screen_block)


def screen(polar_row, pattern_row, screen_block):
    row_count = screen_block.shape[1]
    col_count = screen_block.shape[2]
    flat_dense = (
        jnp.zeros((2, row_count * col_count), jnp.bfloat16).at[:, pattern_row].set(polar_row)
    )
    return screen_products(flat_dense.reshape(2, row_count, col_count), screen_block)


def split_exact(value):
    high = value.astype(jnp.bfloat16)
    rest = value - high.astype(jnp.float32)
    middle = rest.astype(jnp.bfloat16)
    low = (rest - middle.astype(jnp.float32)).astype(jnp.bfloat16)
    return jnp.stack([high, middle, low], axis=0)


def join_exact(pieces):
    pieces = pieces.astype(jnp.float32)
    return (pieces[0] + pieces[1]) + pieces[2]


def body(green_slab, self_energy, pattern, screened):
    own_rate = self_energy[0, 0]
    block_order = own_rate.shape[-1]
    previous_rate = passed_along(own_rate, "domain", 1)
    edge_block = green_slab[0, 0, :, 0:2, :EDGE, :]
    bundle = jnp.concatenate(
        [edge_block.reshape(-1, block_order), split_exact(own_rate).reshape(-1, block_order)], axis=0
    )
    bundle = passed_along(bundle, "domain", -1)
    edge_rows = edge_block.size // block_order
    following = bundle[:edge_rows].reshape(edge_block.shape)
    next_rate = join_exact(bundle[edge_rows:].reshape(3, *own_rate.shape))
    nearby = jnp.stack([previous_rate, own_rate, next_rate], axis=0)[None]
    values = element_values(green_slab[0, 0], following, nearby[0], pattern[0])
    chunks = lax.axis_size("energy")
    values = values.reshape(4, chunks, -1).transpose(1, 0, 2).reshape(chunks, -1)
    by_element = lax.all_to_all(values, "energy", split_axis=0, concat_axis=0, tiled=True)
    polarization = lag_sums(by_element)
    per_energy = lax.all_to_all(polarization, "energy", split_axis=0, concat_axis=0, tiled=True)
    per_energy = per_energy.reshape(chunks, 2, -1).transpose(1, 0, 2).reshape(2, -1)
    result = screen(per_energy, pattern[0], screened[0, 0])
    return result[None, None]


def solution(mesh):
    placed = (
        P("energy", "domain", None, None, None, None),
        P("energy", "domain", None, None, None),
        P("domain", None),
        P("energy", "domain", None, None, None),
    )
    return jax.shard_map(
        body,
        mesh=mesh,
        in_specs=placed,
        out_specs=P("energy", "domain", None, None, None),
        check_vma=False,
    )
```

```python
import functools
import math

import jax
import jax.numpy as jnp
from jax import lax
from jax.experimental import pallas as pl
from jax.sharding import PartitionSpec as P

EDGE = 16


def passed_along(x, axis, by):
    length = lax.axis_size(axis)
    pairs = [(i, i + by) for i in range(length) if 0 <= i + by < length]
    return lax.ppermute(x, axis, pairs)


def _weigh_kernel(slab_ref, edge_ref, rate_ref, out_ref, *, factor, rows, edge):
    step = pl.program_id(0)

    @pl.when(step == 0)
    def _():
        out_ref[...] = jnp.zeros_like(out_ref)

    slab_real = slab_ref[0, 0]
    slab_imag = slab_ref[1, 0]
    real_f = slab_real.astype(jnp.float32)
    imag_f = slab_imag.astype(jnp.float32)
    pieces = []
    for q in range(2):
        rate_real = rate_ref[0, q, 0:1, :]
        rate_imag = rate_ref[0, q, 1:2, :]
        pieces.append(((real_f * rate_real - imag_f * rate_imag) * factor).astype(jnp.bfloat16))
        pieces.append(((real_f * rate_imag + imag_f * rate_real) * factor).astype(jnp.bfloat16))
    left = jnp.concatenate(pieces, axis=0)
    right = jnp.concatenate([slab_real, slab_imag, edge_ref[0, 0], edge_ref[1, 0]], axis=0)
    prod = lax.dot_general(left, right, (((1,), (1,)), ((), ())), preferred_element_type=jnp.float32)
    for q in range(2):
        wr = prod[2 * q * rows:(2 * q + 1) * rows]
        wi = prod[(2 * q + 1) * rows:(2 * q + 2) * rows]
        out_ref[q, 0, :, 0:rows] += wr[:, 0:rows] + wi[:, rows:2 * rows]
        out_ref[q, 1, :, 0:rows] += wi[:, 0:rows] - wr[:, rows:2 * rows]

        @pl.when(step > 0)
        def _():
            e0 = 2 * rows
            out_ref[q, 0, :, rows:rows + edge] += wr[:, e0:e0 + edge] + wi[:, e0 + edge:e0 + 2 * edge]
            out_ref[q, 1, :, rows:rows + edge] += wi[:, e0:e0 + edge] - wr[:, e0 + edge:e0 + 2 * edge]


def weighed_products(own_slab, next_edge, diag_rates):
    _, blocks, rows, block_order = own_slab.shape
    edge = next_edge.shape[2]
    factor = 1.0 / math.sqrt(3.0 * block_order)
    kernel = functools.partial(_weigh_kernel, factor=factor, rows=rows, edge=edge)
    return pl.pallas_call(
        kernel,
        grid=(blocks,),
        in_specs=[
            pl.BlockSpec((2, 1, rows, block_order), lambda j: (0, j, 0, 0)),
            pl.BlockSpec((2, 1, edge, block_order), lambda j: (0, jnp.maximum(j - 1, 0), 0, 0)),
            pl.BlockSpec((1, 2, 2, block_order), lambda j: (j, 0, 0, 0)),
        ],
        out_specs=pl.BlockSpec((2, 2, rows, rows + edge), lambda j: (0, 0, 0, 0)),
        out_shape=jax.ShapeDtypeStruct((2, 2, rows, rows + edge), jnp.float32),
    )(own_slab, next_edge, diag_rates)


def element_values(own_slab, next_edge, diag_rates, pattern_row):
    joined = weighed_products(own_slab, next_edge, diag_rates).astype(jnp.bfloat16)
    return jnp.take(joined.reshape(4, -1), pattern_row, axis=1).reshape(2, 2, -1)


def _lag_kernel(in_ref, out_ref, *, width, factor):
    values = in_ref[...].astype(jnp.float32)
    energy_count = values.shape[0]
    lesser = values[:, 0:2 * width]
    greater = values[:, 2 * width:4 * width]
    swapped = jnp.concatenate([greater[:, width:], greater[:, :width]], axis=1)
    rows = []
    for lag in range(energy_count):
        head = lesser[lag:]
        straight = jnp.sum(head * greater[:energy_count - lag], axis=0, keepdims=True)
        crossed = jnp.sum(head * swapped[:energy_count - lag], axis=0, keepdims=True)
        rows.append(jnp.concatenate([straight[:, :width] - straight[:, width:], crossed[:, :width] + crossed[:, width:]], axis=1))
    out_ref[...] = (jnp.concatenate(rows, axis=0) * factor).astype(out_ref.dtype)


def lag_sums(by_element):
    energy_count, joined = by_element.shape
    width = joined // 4
    kernel = functools.partial(_lag_kernel, width=width, factor=1.0 / math.sqrt(energy_count))
    return pl.pallas_call(
        kernel,
        out_shape=jax.ShapeDtypeStruct((energy_count, 2 * width), jnp.bfloat16),
    )(by_element)


def _screen_kernel(dense_ref, screen_ref, out_ref, *, rows):
    def nt(a, b):
        return lax.dot_general(a, b, (((1,), (1,)), ((), ())), preferred_element_type=jnp.float32)

    def nn(a, b):
        return jnp.dot(a, b, preferred_element_type=jnp.float32)

    dense_real = dense_ref[0]
    dense_imag = dense_ref[1]
    screen_real = screen_ref[0]
    screen_imag = screen_ref[1]
    inner_real = (nt(dense_real, screen_real) + nt(dense_imag, screen_imag)).astype(jnp.bfloat16)
    inner_imag = (nt(dense_imag, screen_real) - nt(dense_real, screen_imag)).astype(jnp.bfloat16)
    near_real = screen_real[:, :rows]
    near_imag = screen_imag[:, :rows]
    side_real = screen_real[:, rows:]
    side_imag = screen_imag[:, rows:]
    edge_real = dense_real[:, rows:]
    edge_imag = dense_imag[:, rows:]
    across_real = (nn(near_real, edge_real) - nn(near_imag, edge_imag)).astype(jnp.bfloat16)
    across_imag = (nn(near_real, edge_imag) + nn(near_imag, edge_real)).astype(jnp.bfloat16)
    first_real = nn(near_real, inner_real) - nn(near_imag, inner_imag)
    first_imag = nn(near_real, inner_imag) + nn(near_imag, inner_real)
    second_real = nt(side_real, across_real) + nt(side_imag, across_imag)
    second_imag = nt(side_imag, across_real) - nt(side_real, across_imag)
    out_ref[0] = first_real + second_real
    out_ref[1] = first_imag + second_imag


def screen_products(dense_pol, screen_block):
    rows = screen_block.shape[1]
    kernel = functools.partial(_screen_kernel, rows=rows)
    return pl.pallas_call(
        kernel,
        out_shape=jax.ShapeDtypeStruct((2, rows, rows), jnp.float32),
    )(dense_pol, screen_block)


def screen(polar_row, pattern_row, screen_block):
    row_count = screen_block.shape[1]
    col_count = screen_block.shape[2]
    flat_dense = (
        jnp.zeros((2, row_count * col_count), jnp.bfloat16).at[:, pattern_row].set(polar_row)
    )
    return screen_products(flat_dense.reshape(2, row_count, col_count), screen_block)


def split_exact(value):
    high = lax.reduce_precision(value, exponent_bits=8, mantissa_bits=7)
    rest = value - high
    middle = lax.reduce_precision(rest, exponent_bits=8, mantissa_bits=7)
    low = rest - middle
    return jnp.stack([high, middle, low], axis=0).astype(jnp.bfloat16)


def join_exact(pieces):
    pieces = pieces.astype(jnp.float32)
    return (pieces[0] + pieces[1]) + pieces[2]


def body(green_slab, self_energy, pattern, screened):
    own_rate = self_energy[0, 0]
    block_order = own_rate.shape[-1]
    previous_rate = passed_along(own_rate, "domain", 1)
    edge_block = green_slab[0, 0, :, 0:2, :EDGE, :]
    bundle = jnp.concatenate(
        [edge_block.reshape(-1, block_order), split_exact(own_rate).reshape(-1, block_order)], axis=0
    )
    bundle = passed_along(bundle, "domain", -1)
    edge_rows = edge_block.size // block_order
    following = bundle[:edge_rows].reshape(edge_block.shape)
    next_rate = join_exact(bundle[edge_rows:].reshape(3, *own_rate.shape))
    nearby = jnp.stack([previous_rate, own_rate, next_rate], axis=0)[None]
    values = element_values(green_slab[0, 0], following, nearby[0], pattern[0])
    chunks = lax.axis_size("energy")
    values = values.reshape(4, chunks, -1).transpose(1, 0, 2).reshape(chunks, -1)
    by_element = lax.all_to_all(values, "energy", split_axis=0, concat_axis=0, tiled=True)
    polarization = lag_sums(by_element)
    per_energy = lax.all_to_all(polarization, "energy", split_axis=0, concat_axis=0, tiled=True)
    per_energy = per_energy.reshape(chunks, 2, -1).transpose(1, 0, 2).reshape(2, -1)
    result = screen(per_energy, pattern[0], screened[0, 0])
    return result[None, None]


def solution(mesh):
    placed = (
        P("energy", "domain", None, None, None, None),
        P("energy", "domain", None, None, None),
        P("domain", None),
        P("energy", "domain", None, None, None),
    )
    return jax.shard_map(
        body,
        mesh=mesh,
        in_specs=placed,
        out_specs=P("energy", "domain", None, None, None),
        check_vma=False,
    )
```

```python
import functools
import math

import jax
import jax.numpy as jnp
from jax import lax
from jax.experimental import pallas as pl
from jax.sharding import PartitionSpec as P

EDGE = 16


def passed_along(x, axis, by):
    length = lax.axis_size(axis)
    pairs = [(i, i + by) for i in range(length) if 0 <= i + by < length]
    return lax.ppermute(x, axis, pairs)


def _weigh_kernel(slab_ref, edge_ref, rate_ref, out_ref, *, factor, rows, edge):
    step = pl.program_id(0)

    @pl.when(step == 0)
    def _():
        out_ref[...] = jnp.zeros_like(out_ref)

    slab_real = slab_ref[0, 0]
    slab_imag = slab_ref[1, 0]
    real_f = slab_real.astype(jnp.float32)
    imag_f = slab_imag.astype(jnp.float32)
    pieces = []
    for q in range(2):
        rate_real = rate_ref[0, q, 0:1, :]
        rate_imag = rate_ref[0, q, 1:2, :]
        pieces.append(((real_f * rate_real - imag_f * rate_imag) * factor).astype(jnp.bfloat16))
        pieces.append(((real_f * rate_imag + imag_f * rate_real) * factor).astype(jnp.bfloat16))
    left = jnp.concatenate(pieces, axis=0)
    right = jnp.concatenate([slab_real, slab_imag, edge_ref[0, 0], edge_ref[1, 0]], axis=0)
    prod = lax.dot_general(left, right, (((1,), (1,)), ((), ())), preferred_element_type=jnp.float32)
    for q in range(2):
        wr = prod[2 * q * rows:(2 * q + 1) * rows]
        wi = prod[(2 * q + 1) * rows:(2 * q + 2) * rows]
        out_ref[q, 0, :, 0:rows] += wr[:, 0:rows] + wi[:, rows:2 * rows]
        out_ref[q, 1, :, 0:rows] += wi[:, 0:rows] - wr[:, rows:2 * rows]

        @pl.when(step > 0)
        def _():
            e0 = 2 * rows
            out_ref[q, 0, :, rows:rows + edge] += wr[:, e0:e0 + edge] + wi[:, e0 + edge:e0 + 2 * edge]
            out_ref[q, 1, :, rows:rows + edge] += wi[:, e0:e0 + edge] - wr[:, e0 + edge:e0 + 2 * edge]


def weighed_products(own_slab, next_edge, diag_rates):
    _, blocks, rows, block_order = own_slab.shape
    edge = next_edge.shape[2]
    factor = 1.0 / math.sqrt(3.0 * block_order)
    kernel = functools.partial(_weigh_kernel, factor=factor, rows=rows, edge=edge)
    return pl.pallas_call(
        kernel,
        grid=(blocks,),
        in_specs=[
            pl.BlockSpec((2, 1, rows, block_order), lambda j: (0, j, 0, 0)),
            pl.BlockSpec((2, 1, edge, block_order), lambda j: (0, jnp.maximum(j - 1, 0), 0, 0)),
            pl.BlockSpec((1, 2, 2, block_order), lambda j: (j, 0, 0, 0)),
        ],
        out_specs=pl.BlockSpec((2, 2, rows, rows + edge), lambda j: (0, 0, 0, 0)),
        out_shape=jax.ShapeDtypeStruct((2, 2, rows, rows + edge), jnp.float32),
    )(own_slab, next_edge, diag_rates)


def element_values(own_slab, next_edge, diag_rates, pattern_row):
    joined = weighed_products(own_slab, next_edge, diag_rates).astype(jnp.bfloat16)
    return jnp.take(joined.reshape(4, -1), pattern_row, axis=1).reshape(2, 2, -1)


def _lag_kernel(in_ref, out_ref, *, width, factor):
    values = in_ref[...].astype(jnp.float32)
    energy_count = values.shape[0]
    lesser = values[:, 0:2 * width]
    greater = values[:, 2 * width:4 * width]
    swapped = jnp.concatenate([greater[:, width:], greater[:, :width]], axis=1)
    rows = []
    for lag in range(energy_count):
        head = lesser[lag:]
        straight = jnp.sum(head * greater[:energy_count - lag], axis=0, keepdims=True)
        crossed = jnp.sum(head * swapped[:energy_count - lag], axis=0, keepdims=True)
        rows.append(jnp.concatenate([straight[:, :width] - straight[:, width:], crossed[:, :width] + crossed[:, width:]], axis=1))
    out_ref[...] = (jnp.concatenate(rows, axis=0) * factor).astype(out_ref.dtype)


def lag_sums(by_element):
    energy_count, joined = by_element.shape
    width = joined // 4
    kernel = functools.partial(_lag_kernel, width=width, factor=1.0 / math.sqrt(energy_count))
    return pl.pallas_call(
        kernel,
        out_shape=jax.ShapeDtypeStruct((energy_count, 2 * width), jnp.bfloat16),
    )(by_element)


def _screen_kernel(polar_ref, place_ref, screen_ref, out_ref, *, rows, cols):
    def nt(a, b):
        return lax.dot_general(a, b, (((1,), (1,)), ((), ())), preferred_element_type=jnp.float32)

    def nn(a, b):
        return jnp.dot(a, b, preferred_element_type=jnp.float32)

    count = place_ref.shape[1]
    row_hit = lax.broadcasted_iota(jnp.int32, (rows, count), 0) == place_ref[0:1, :]
    col_hit = (lax.broadcasted_iota(jnp.int32, (cols, count), 0) == place_ref[1:2, :]).astype(jnp.bfloat16)
    polar = polar_ref[...].astype(jnp.float32)
    dense = []
    for part in range(2):
        spread = jnp.where(row_hit, polar[part:part + 1, :], 0.0).astype(jnp.bfloat16)
        dense.append(nt(spread, col_hit).astype(jnp.bfloat16))
    dense_real, dense_imag = dense
    screen_real = screen_ref[0]
    screen_imag = screen_ref[1]
    inner_real = (nt(dense_real, screen_real) + nt(dense_imag, screen_imag)).astype(jnp.bfloat16)
    inner_imag = (nt(dense_imag, screen_real) - nt(dense_real, screen_imag)).astype(jnp.bfloat16)
    near_real = screen_real[:, :rows]
    near_imag = screen_imag[:, :rows]
    side_real = screen_real[:, rows:]
    side_imag = screen_imag[:, rows:]
    edge_real = dense_real[:, rows:]
    edge_imag = dense_imag[:, rows:]
    across_real = (nn(near_real, edge_real) - nn(near_imag, edge_imag)).astype(jnp.bfloat16)
    across_imag = (nn(near_real, edge_imag) + nn(near_imag, edge_real)).astype(jnp.bfloat16)
    first_real = nn(near_real, inner_real) - nn(near_imag, inner_imag)
    first_imag = nn(near_real, inner_imag) + nn(near_imag, inner_real)
    second_real = nt(side_real, across_real) + nt(side_imag, across_imag)
    second_imag = nt(side_imag, across_real) - nt(side_real, across_imag)
    out_ref[0] = first_real + second_real
    out_ref[1] = first_imag + second_imag


def screen(polar_row, pattern_row, screen_block):
    rows = screen_block.shape[1]
    cols = screen_block.shape[2]
    place = jnp.stack([pattern_row // cols, pattern_row % cols], axis=0)
    kernel = functools.partial(_screen_kernel, rows=rows, cols=cols)
    return pl.pallas_call(
        kernel,
        out_shape=jax.ShapeDtypeStruct((2, rows, rows), jnp.float32),
    )(polar_row, place, screen_block)


def split_exact(value):
    high = lax.reduce_precision(value, exponent_bits=8, mantissa_bits=7)
    rest = value - high
    middle = lax.reduce_precision(rest, exponent_bits=8, mantissa_bits=7)
    low = rest - middle
    return jnp.stack([high, middle, low], axis=0).astype(jnp.bfloat16)


def join_exact(pieces):
    pieces = pieces.astype(jnp.float32)
    return (pieces[0] + pieces[1]) + pieces[2]


def body(green_slab, self_energy, pattern, screened):
    own_rate = self_energy[0, 0]
    block_order = own_rate.shape[-1]
    previous_rate = passed_along(own_rate, "domain", 1)
    edge_block = green_slab[0, 0, :, 0:2, :EDGE, :]
    bundle = jnp.concatenate(
        [edge_block.reshape(-1, block_order), split_exact(own_rate).reshape(-1, block_order)], axis=0
    )
    bundle = passed_along(bundle, "domain", -1)
    edge_rows = edge_block.size // block_order
    following = bundle[:edge_rows].reshape(edge_block.shape)
    next_rate = join_exact(bundle[edge_rows:].reshape(3, *own_rate.shape))
    nearby = jnp.stack([previous_rate, own_rate, next_rate], axis=0)[None]
    values = element_values(green_slab[0, 0], following, nearby[0], pattern[0])
    chunks = lax.axis_size("energy")
    values = values.reshape(4, chunks, -1).transpose(1, 0, 2).reshape(chunks, -1)
    by_element = lax.all_to_all(values, "energy", split_axis=0, concat_axis=0, tiled=True)
    polarization = lag_sums(by_element)
    per_energy = lax.all_to_all(polarization, "energy", split_axis=0, concat_axis=0, tiled=True)
    per_energy = per_energy.reshape(chunks, 2, -1).transpose(1, 0, 2).reshape(2, -1)
    result = screen(per_energy, pattern[0], screened[0, 0])
    return result[None, None]


def solution(mesh):
    placed = (
        P("energy", "domain", None, None, None, None),
        P("energy", "domain", None, None, None),
        P("domain", None),
        P("energy", "domain", None, None, None),
    )
    return jax.shard_map(
        body,
        mesh=mesh,
        in_specs=placed,
        out_specs=P("energy", "domain", None, None, None),
        check_vma=False,
    )
```

```python
import functools
import math

import jax
import jax.numpy as jnp
from jax import lax
from jax.experimental import pallas as pl
from jax.experimental.pallas import tpu as pltpu
from jax.sharding import PartitionSpec as P

EDGE = 16


def passed_along(x, axis, by):
    length = lax.axis_size(axis)
    pairs = [(i, i + by) for i in range(length) if 0 <= i + by < length]
    return lax.ppermute(x, axis, pairs)


def _weigh_kernel(slab_ref, edge_ref, rate_ref, place_ref, out_ref, acc_ref, *, factor, rows, edge):
    step = pl.program_id(0)

    @pl.when(step == 0)
    def _():
        acc_ref[...] = jnp.zeros_like(acc_ref)

    slab_real = slab_ref[0, 0]
    slab_imag = slab_ref[1, 0]
    real_f = slab_real.astype(jnp.float32)
    imag_f = slab_imag.astype(jnp.float32)
    pieces = []
    for q in range(2):
        rate_real = rate_ref[0, q, 0:1, :]
        rate_imag = rate_ref[0, q, 1:2, :]
        pieces.append(((real_f * rate_real - imag_f * rate_imag) * factor).astype(jnp.bfloat16))
        pieces.append(((real_f * rate_imag + imag_f * rate_real) * factor).astype(jnp.bfloat16))
    left = jnp.concatenate(pieces, axis=0)
    right = jnp.concatenate([slab_real, slab_imag, edge_ref[0, 0], edge_ref[1, 0]], axis=0)
    prod = lax.dot_general(left, right, (((1,), (1,)), ((), ())), preferred_element_type=jnp.float32)
    for q in range(2):
        wr = prod[2 * q * rows:(2 * q + 1) * rows]
        wi = prod[(2 * q + 1) * rows:(2 * q + 2) * rows]
        acc_ref[q, 0, :, 0:rows] += wr[:, 0:rows] + wi[:, rows:2 * rows]
        acc_ref[q, 1, :, 0:rows] += wi[:, 0:rows] - wr[:, rows:2 * rows]

        @pl.when(step > 0)
        def _():
            e0 = 2 * rows
            acc_ref[q, 0, :, rows:rows + edge] += wr[:, e0:e0 + edge] + wi[:, e0 + edge:e0 + 2 * edge]
            acc_ref[q, 1, :, rows:rows + edge] += wi[:, e0:e0 + edge] - wr[:, e0 + edge:e0 + 2 * edge]

    @pl.when(step == pl.num_programs(0) - 1)
    def _():
        cols = rows + edge
        count = place_ref.shape[1]
        joined = jnp.concatenate(
            [acc_ref[q, p] for q in range(2) for p in range(2)], axis=0
        ).astype(jnp.bfloat16)
        col_hit = (lax.broadcasted_iota(jnp.int32, (cols, count), 0) == place_ref[1:2, :]).astype(jnp.bfloat16)
        row_hit = lax.broadcasted_iota(jnp.int32, (rows, count), 0) == place_ref[0:1, :]
        by_column = jnp.dot(joined, col_hit, preferred_element_type=jnp.float32)
        for k in range(4):
            picked = jnp.where(row_hit, by_column[k * rows:(k + 1) * rows], 0.0)
            out_ref[k:k + 1, :] = jnp.sum(picked, axis=0, keepdims=True).astype(out_ref.dtype)


def element_values(own_slab, next_edge, diag_rates, pattern_row):
    _, blocks, rows, block_order = own_slab.shape
    edge = next_edge.shape[2]
    cols = rows + edge
    count = pattern_row.shape[0]
    place = jnp.stack([pattern_row // cols, pattern_row % cols], axis=0)
    factor = 1.0 / math.sqrt(3.0 * block_order)
    kernel = functools.partial(_weigh_kernel, factor=factor, rows=rows, edge=edge)
    return pl.pallas_call(
        kernel,
        grid=(blocks,),
        in_specs=[
            pl.BlockSpec((2, 1, rows, block_order), lambda j: (0, j, 0, 0)),
            pl.BlockSpec((2, 1, edge, block_order), lambda j: (0, jnp.maximum(j - 1, 0), 0, 0)),
            pl.BlockSpec((1, 2, 2, block_order), lambda j: (j, 0, 0, 0)),
            pl.BlockSpec((2, count), lambda j: (0, 0)),
        ],
        out_specs=pl.BlockSpec((4, count), lambda j: (0, 0)),
        out_shape=jax.ShapeDtypeStruct((4, count), jnp.bfloat16),
        scratch_shapes=[pltpu.VMEM((2, 2, rows, cols), jnp.float32)],
    )(own_slab, next_edge, diag_rates, place)


def _lag_kernel(in_ref, out_ref, *, width, factor):
    values = in_ref[...].astype(jnp.float32)
    energy_count = values.shape[0]
    lesser = values[:, 0:2 * width]
    greater = values[:, 2 * width:4 * width]
    swapped = jnp.concatenate([greater[:, width:], greater[:, :width]], axis=1)
    rows = []
    for lag in range(energy_count):
        head = lesser[lag:]
        straight = jnp.sum(head * greater[:energy_count - lag], axis=0, keepdims=True)
        crossed = jnp.sum(head * swapped[:energy_count - lag], axis=0, keepdims=True)
        rows.append(jnp.concatenate([straight[:, :width] - straight[:, width:], crossed[:, :width] + crossed[:, width:]], axis=1))
    out_ref[...] = (jnp.concatenate(rows, axis=0) * factor).astype(out_ref.dtype)


def lag_sums(by_element):
    energy_count, joined = by_element.shape
    width = joined // 4
    kernel = functools.partial(_lag_kernel, width=width, factor=1.0 / math.sqrt(energy_count))
    return pl.pallas_call(
        kernel,
        out_shape=jax.ShapeDtypeStruct((energy_count, 2 * width), jnp.bfloat16),
    )(by_element)


def _screen_kernel(polar_ref, place_ref, screen_ref, out_ref, *, rows, cols):
    def nt(a, b):
        return lax.dot_general(a, b, (((1,), (1,)), ((), ())), preferred_element_type=jnp.float32)

    def nn(a, b):
        return jnp.dot(a, b, preferred_element_type=jnp.float32)

    count = place_ref.shape[1]
    row_hit = lax.broadcasted_iota(jnp.int32, (rows, count), 0) == place_ref[0:1, :]
    col_hit = (lax.broadcasted_iota(jnp.int32, (cols, count), 0) == place_ref[1:2, :]).astype(jnp.bfloat16)
    polar = polar_ref[...].astype(jnp.float32)
    dense = []
    for part in range(2):
        spread = jnp.where(row_hit, polar[part:part + 1, :], 0.0).astype(jnp.bfloat16)
        dense.append(nt(spread, col_hit).astype(jnp.bfloat16))
    dense_real, dense_imag = dense
    screen_real = screen_ref[0]
    screen_imag = screen_ref[1]
    inner_real = (nt(dense_real, screen_real) + nt(dense_imag, screen_imag)).astype(jnp.bfloat16)
    inner_imag = (nt(dense_imag, screen_real) - nt(dense_real, screen_imag)).astype(jnp.bfloat16)
    near_real = screen_real[:, :rows]
    near_imag = screen_imag[:, :rows]
    side_real = screen_real[:, rows:]
    side_imag = screen_imag[:, rows:]
    edge_real = dense_real[:, rows:]
    edge_imag = dense_imag[:, rows:]
    across_real = (nn(near_real, edge_real) - nn(near_imag, edge_imag)).astype(jnp.bfloat16)
    across_imag = (nn(near_real, edge_imag) + nn(near_imag, edge_real)).astype(jnp.bfloat16)
    first_real = nn(near_real, inner_real) - nn(near_imag, inner_imag)
    first_imag = nn(near_real, inner_imag) + nn(near_imag, inner_real)
    second_real = nt(side_real, across_real) + nt(side_imag, across_imag)
    second_imag = nt(side_imag, across_real) - nt(side_real, across_imag)
    out_ref[0] = first_real + second_real
    out_ref[1] = first_imag + second_imag


def screen(polar_row, pattern_row, screen_block):
    rows = screen_block.shape[1]
    cols = screen_block.shape[2]
    place = jnp.stack([pattern_row // cols, pattern_row % cols], axis=0)
    kernel = functools.partial(_screen_kernel, rows=rows, cols=cols)
    return pl.pallas_call(
        kernel,
        out_shape=jax.ShapeDtypeStruct((2, rows, rows), jnp.float32),
    )(polar_row, place, screen_block)


def split_exact(value):
    high = lax.reduce_precision(value, exponent_bits=8, mantissa_bits=7)
    rest = value - high
    middle = lax.reduce_precision(rest, exponent_bits=8, mantissa_bits=7)
    low = rest - middle
    return jnp.stack([high, middle, low], axis=0).astype(jnp.bfloat16)


def join_exact(pieces):
    pieces = pieces.astype(jnp.float32)
    return (pieces[0] + pieces[1]) + pieces[2]


def body(green_slab, self_energy, pattern, screened):
    own_rate = self_energy[0, 0]
    block_order = own_rate.shape[-1]
    previous_rate = passed_along(own_rate, "domain", 1)
    edge_block = green_slab[0, 0, :, 0:2, :EDGE, :]
    bundle = jnp.concatenate(
        [edge_block.reshape(-1, block_order), split_exact(own_rate).reshape(-1, block_order)], axis=0
    )
    bundle = passed_along(bundle, "domain", -1)
    edge_rows = edge_block.size // block_order
    following = bundle[:edge_rows].reshape(edge_block.shape)
    next_rate = join_exact(bundle[edge_rows:].reshape(3, *own_rate.shape))
    nearby = jnp.stack([previous_rate, own_rate, next_rate], axis=0)[None]
    values = element_values(green_slab[0, 0], following, nearby[0], pattern[0])
    chunks = lax.axis_size("energy")
    values = values.reshape(4, chunks, -1).transpose(1, 0, 2).reshape(chunks, -1)
    by_element = lax.all_to_all(values, "energy", split_axis=0, concat_axis=0, tiled=True)
    polarization = lag_sums(by_element)
    per_energy = lax.all_to_all(polarization, "energy", split_axis=0, concat_axis=0, tiled=True)
    per_energy = per_energy.reshape(chunks, 2, -1).transpose(1, 0, 2).reshape(2, -1)
    result = screen(per_energy, pattern[0], screened[0, 0])
    return result[None, None]


def solution(mesh):
    placed = (
        P("energy", "domain", None, None, None, None),
        P("energy", "domain", None, None, None),
        P("domain", None),
        P("energy", "domain", None, None, None),
    )
    return jax.shard_map(
        body,
        mesh=mesh,
        in_specs=placed,
        out_specs=P("energy", "domain", None, None, None),
        check_vma=False,
    )
```

```python
import functools
import math

import jax
import jax.numpy as jnp
from jax import lax
from jax.experimental import pallas as pl
from jax.experimental.pallas import tpu as pltpu
from jax.sharding import PartitionSpec as P

EDGE = 16


def passed_along(x, axis, by):
    length = lax.axis_size(axis)
    pairs = [(i, i + by) for i in range(length) if 0 <= i + by < length]
    return lax.ppermute(x, axis, pairs)


def _weigh_kernel(slab_ref, edge_ref, rate_ref, place_ref, out_ref, acc_ref, *, factor, rows, edge):
    step = pl.program_id(0)

    @pl.when(step == 0)
    def _():
        acc_ref[...] = jnp.zeros_like(acc_ref)

    slab_real = slab_ref[0, 0]
    slab_imag = slab_ref[1, 0]
    real_f = slab_real.astype(jnp.float32)
    imag_f = slab_imag.astype(jnp.float32)
    pieces = []
    for q in range(2):
        rate_real = rate_ref[0, q, 0:1, :]
        rate_imag = rate_ref[0, q, 1:2, :]
        pieces.append(((real_f * rate_real - imag_f * rate_imag) * factor).astype(jnp.bfloat16))
        pieces.append(((real_f * rate_imag + imag_f * rate_real) * factor).astype(jnp.bfloat16))
    left = jnp.concatenate(pieces, axis=0)
    right = jnp.concatenate([slab_real, slab_imag, edge_ref[0, 0], edge_ref[1, 0]], axis=0)
    prod = lax.dot_general(left, right, (((1,), (1,)), ((), ())), preferred_element_type=jnp.float32)
    for q in range(2):
        wr = prod[2 * q * rows:(2 * q + 1) * rows]
        wi = prod[(2 * q + 1) * rows:(2 * q + 2) * rows]
        acc_ref[q, 0, :, 0:rows] += wr[:, 0:rows] + wi[:, rows:2 * rows]
        acc_ref[q, 1, :, 0:rows] += wi[:, 0:rows] - wr[:, rows:2 * rows]

        @pl.when(step > 0)
        def _():
            e0 = 2 * rows
            acc_ref[q, 0, :, rows:rows + edge] += wr[:, e0:e0 + edge] + wi[:, e0 + edge:e0 + 2 * edge]
            acc_ref[q, 1, :, rows:rows + edge] += wi[:, e0:e0 + edge] - wr[:, e0 + edge:e0 + 2 * edge]

    @pl.when(step == pl.num_programs(0) - 1)
    def _():
        cols = rows + edge
        count = place_ref.shape[1]
        joined = jnp.concatenate(
            [acc_ref[q, p] for q in range(2) for p in range(2)], axis=0
        ).astype(jnp.bfloat16)
        col_hit = (lax.broadcasted_iota(jnp.int32, (cols, count), 0) == place_ref[1:2, :]).astype(jnp.bfloat16)
        row_hit = lax.broadcasted_iota(jnp.int32, (rows, count), 0) == place_ref[0:1, :]
        by_column = jnp.dot(joined, col_hit, preferred_element_type=jnp.float32)
        for k in range(4):
            picked = jnp.where(row_hit, by_column[k * rows:(k + 1) * rows], 0.0)
            out_ref[k:k + 1, :] = jnp.sum(picked, axis=0, keepdims=True).astype(out_ref.dtype)


def element_values(own_slab, next_edge, diag_rates, pattern_row):
    _, blocks, rows, block_order = own_slab.shape
    edge = next_edge.shape[2]
    cols = rows + edge
    count = pattern_row.shape[0]
    place = jnp.stack([pattern_row // cols, pattern_row % cols], axis=0)
    factor = 1.0 / math.sqrt(3.0 * block_order)
    kernel = functools.partial(_weigh_kernel, factor=factor, rows=rows, edge=edge)
    return pl.pallas_call(
        kernel,
        grid=(blocks,),
        in_specs=[
            pl.BlockSpec((2, 1, rows, block_order), lambda j: (0, j, 0, 0)),
            pl.BlockSpec((2, 1, edge, block_order), lambda j: (0, jnp.maximum(j - 1, 0), 0, 0)),
            pl.BlockSpec((1, 2, 2, block_order), lambda j: (j, 0, 0, 0)),
            pl.BlockSpec((2, count), lambda j: (0, 0)),
        ],
        out_specs=pl.BlockSpec((4, count), lambda j: (0, 0)),
        out_shape=jax.ShapeDtypeStruct((4, count), jnp.bfloat16),
        scratch_shapes=[pltpu.VMEM((2, 2, rows, cols), jnp.float32)],
    )(own_slab, next_edge, diag_rates, place)


def _lag_kernel(in_ref, out_ref, *, width, factor):
    values = in_ref[...].astype(jnp.float32)
    energy_count = values.shape[0]
    lesser = values[:, 0:2 * width]
    greater = values[:, 2 * width:4 * width]
    swapped = jnp.concatenate([greater[:, width:], greater[:, :width]], axis=1)
    rows = []
    for lag in range(energy_count):
        head = lesser[lag:]
        straight = jnp.sum(head * greater[:energy_count - lag], axis=0, keepdims=True)
        crossed = jnp.sum(head * swapped[:energy_count - lag], axis=0, keepdims=True)
        rows.append(jnp.concatenate([straight[:, :width] - straight[:, width:], crossed[:, :width] + crossed[:, width:]], axis=1))
    out_ref[...] = (jnp.concatenate(rows, axis=0) * factor).astype(out_ref.dtype)


def lag_sums(by_element):
    energy_count, joined = by_element.shape
    width = joined // 4
    kernel = functools.partial(_lag_kernel, width=width, factor=1.0 / math.sqrt(energy_count))
    return pl.pallas_call(
        kernel,
        out_shape=jax.ShapeDtypeStruct((energy_count, 2 * width), jnp.bfloat16),
    )(by_element)


def _screen_kernel(polar_ref, place_ref, screen_ref, out_ref, *, rows, cols):
    def nt(a, b):
        return lax.dot_general(a, b, (((1,), (1,)), ((), ())), preferred_element_type=jnp.float32)

    def nn(a, b):
        return jnp.dot(a, b, preferred_element_type=jnp.float32)

    count = place_ref.shape[1]
    row_hit = lax.broadcasted_iota(jnp.int32, (rows, count), 0) == place_ref[0:1, :]
    col_hit = (lax.broadcasted_iota(jnp.int32, (cols, count), 0) == place_ref[1:2, :]).astype(jnp.bfloat16)
    polar = polar_ref[...].astype(jnp.float32)
    dense = []
    for part in range(2):
        spread = jnp.where(row_hit, polar[part:part + 1, :], 0.0).astype(jnp.bfloat16)
        dense.append(nt(spread, col_hit).astype(jnp.bfloat16))
    dense_real, dense_imag = dense
    screen_real = screen_ref[0]
    screen_imag = screen_ref[1]
    inner_real = (nt(dense_real, screen_real) + nt(dense_imag, screen_imag)).astype(jnp.bfloat16)
    inner_imag = (nt(dense_imag, screen_real) - nt(dense_real, screen_imag)).astype(jnp.bfloat16)
    near_real = screen_real[:, :rows]
    near_imag = screen_imag[:, :rows]
    side_real = screen_real[:, rows:]
    side_imag = screen_imag[:, rows:]
    edge_real = dense_real[:, rows:]
    edge_imag = dense_imag[:, rows:]
    across_real = (nn(near_real, edge_real) - nn(near_imag, edge_imag)).astype(jnp.bfloat16)
    across_imag = (nn(near_real, edge_imag) + nn(near_imag, edge_real)).astype(jnp.bfloat16)
    first_real = nn(near_real, inner_real) - nn(near_imag, inner_imag)
    first_imag = nn(near_real, inner_imag) + nn(near_imag, inner_real)
    second_real = nt(side_real, across_real) + nt(side_imag, across_imag)
    second_imag = nt(side_imag, across_real) - nt(side_real, across_imag)
    out_ref[0] = first_real + second_real
    out_ref[1] = first_imag + second_imag


def screen(polar_row, pattern_row, screen_block):
    rows = screen_block.shape[1]
    cols = screen_block.shape[2]
    place = jnp.stack([pattern_row // cols, pattern_row % cols], axis=0)
    kernel = functools.partial(_screen_kernel, rows=rows, cols=cols)
    return pl.pallas_call(
        kernel,
        out_shape=jax.ShapeDtypeStruct((2, rows, rows), jnp.float32),
    )(polar_row, place, screen_block)


def own_lag(by_energy):
    energy_count = by_energy.shape[0]
    lag = lax.axis_index("energy")
    lesser = by_energy[:, 0:2].astype(jnp.float32)
    greater = jnp.roll(by_energy[:, 2:4].astype(jnp.float32), lag, axis=0)
    inside = (jnp.arange(energy_count) >= lag)[:, None]
    greater = jnp.where(inside[:, None], greater, 0.0)
    real_sum = jnp.sum(lesser[:, 0] * greater[:, 0] - lesser[:, 1] * greater[:, 1], axis=0)
    imag_sum = jnp.sum(lesser[:, 0] * greater[:, 1] + lesser[:, 1] * greater[:, 0], axis=0)
    factor = 1.0 / math.sqrt(energy_count)
    return (jnp.stack([real_sum, imag_sum], axis=0) * factor).astype(jnp.bfloat16)


def split_exact(value):
    high = lax.reduce_precision(value, exponent_bits=8, mantissa_bits=7)
    rest = value - high
    middle = lax.reduce_precision(rest, exponent_bits=8, mantissa_bits=7)
    low = rest - middle
    return jnp.stack([high, middle, low], axis=0).astype(jnp.bfloat16)


def join_exact(pieces):
    pieces = pieces.astype(jnp.float32)
    return (pieces[0] + pieces[1]) + pieces[2]


def body(green_slab, self_energy, pattern, screened):
    own_rate = self_energy[0, 0]
    block_order = own_rate.shape[-1]
    previous_rate = passed_along(own_rate, "domain", 1)
    edge_block = green_slab[0, 0, :, 0:2, :EDGE, :]
    bundle = jnp.concatenate(
        [edge_block.reshape(-1, block_order), split_exact(own_rate).reshape(-1, block_order)], axis=0
    )
    bundle = passed_along(bundle, "domain", -1)
    edge_rows = edge_block.size // block_order
    following = bundle[:edge_rows].reshape(edge_block.shape)
    next_rate = join_exact(bundle[edge_rows:].reshape(3, *own_rate.shape))
    nearby = jnp.stack([previous_rate, own_rate, next_rate], axis=0)[None]
    values = element_values(green_slab[0, 0], following, nearby[0], pattern[0])
    energy_count = lax.axis_size("energy")
    spread = jnp.broadcast_to(values[None], (energy_count, *values.shape))
    by_energy = lax.all_to_all(spread, "energy", split_axis=0, concat_axis=0, tiled=True)
    per_energy = own_lag(by_energy)
    result = screen(per_energy, pattern[0], screened[0, 0])
    return result[None, None]


def solution(mesh):
    placed = (
        P("energy", "domain", None, None, None, None),
        P("energy", "domain", None, None, None),
        P("domain", None),
        P("energy", "domain", None, None, None),
    )
    return jax.shard_map(
        body,
        mesh=mesh,
        in_specs=placed,
        out_specs=P("energy", "domain", None, None, None),
        check_vma=False,
    )
```

```python
import functools
import math

import jax
import jax.numpy as jnp
from jax import lax
from jax.experimental import pallas as pl
from jax.experimental.pallas import tpu as pltpu
from jax.sharding import PartitionSpec as P

EDGE = 16


def passed_along(x, axis, by):
    length = lax.axis_size(axis)
    pairs = [(i, i + by) for i in range(length) if 0 <= i + by < length]
    return lax.ppermute(x, axis, pairs)


def _weigh_kernel(slab_ref, edge_ref, rate_ref, place_ref, out_ref, acc_ref, *, factor, rows, edge):
    step = pl.program_id(0)

    @pl.when(step == 0)
    def _():
        acc_ref[...] = jnp.zeros_like(acc_ref)

    slab_real = slab_ref[0, 0]
    slab_imag = slab_ref[1, 0]
    real_f = slab_real.astype(jnp.float32)
    imag_f = slab_imag.astype(jnp.float32)
    pieces = []
    for q in range(2):
        rate_real = rate_ref[0, q, 0:1, :]
        rate_imag = rate_ref[0, q, 1:2, :]
        pieces.append(((real_f * rate_real - imag_f * rate_imag) * factor).astype(jnp.bfloat16))
        pieces.append(((real_f * rate_imag + imag_f * rate_real) * factor).astype(jnp.bfloat16))
    left = jnp.concatenate(pieces, axis=0)
    right = jnp.concatenate([slab_real, slab_imag, edge_ref[0, 0], edge_ref[1, 0]], axis=0)
    prod = lax.dot_general(left, right, (((1,), (1,)), ((), ())), preferred_element_type=jnp.float32)
    for q in range(2):
        wr = prod[2 * q * rows:(2 * q + 1) * rows]
        wi = prod[(2 * q + 1) * rows:(2 * q + 2) * rows]
        acc_ref[q, 0, :, 0:rows] += wr[:, 0:rows] + wi[:, rows:2 * rows]
        acc_ref[q, 1, :, 0:rows] += wi[:, 0:rows] - wr[:, rows:2 * rows]

        @pl.when(step > 0)
        def _():
            e0 = 2 * rows
            acc_ref[q, 0, :, rows:rows + edge] += wr[:, e0:e0 + edge] + wi[:, e0 + edge:e0 + 2 * edge]
            acc_ref[q, 1, :, rows:rows + edge] += wi[:, e0:e0 + edge] - wr[:, e0 + edge:e0 + 2 * edge]

    @pl.when(step == pl.num_programs(0) - 1)
    def _():
        cols = rows + edge
        count = place_ref.shape[1]
        joined = jnp.concatenate(
            [acc_ref[q, p] for q in range(2) for p in range(2)], axis=0
        ).astype(jnp.bfloat16)
        col_hit = (lax.broadcasted_iota(jnp.int32, (cols, count), 0) == place_ref[1:2, :]).astype(jnp.bfloat16)
        row_hit = lax.broadcasted_iota(jnp.int32, (rows, count), 0) == place_ref[0:1, :]
        by_column = jnp.dot(joined, col_hit, preferred_element_type=jnp.float32)
        for k in range(4):
            picked = jnp.where(row_hit, by_column[k * rows:(k + 1) * rows], 0.0)
            out_ref[k:k + 1, :] = jnp.sum(picked, axis=0, keepdims=True).astype(out_ref.dtype)


def element_values(own_slab, next_edge, diag_rates, pattern_row):
    _, blocks, rows, block_order = own_slab.shape
    edge = next_edge.shape[2]
    cols = rows + edge
    count = pattern_row.shape[0]
    place = jnp.stack([pattern_row // cols, pattern_row % cols], axis=0)
    factor = 1.0 / math.sqrt(3.0 * block_order)
    kernel = functools.partial(_weigh_kernel, factor=factor, rows=rows, edge=edge)
    return pl.pallas_call(
        kernel,
        grid=(blocks,),
        in_specs=[
            pl.BlockSpec((2, 1, rows, block_order), lambda j: (0, j, 0, 0)),
            pl.BlockSpec((2, 1, edge, block_order), lambda j: (0, jnp.maximum(j - 1, 0), 0, 0)),
            pl.BlockSpec((1, 2, 2, block_order), lambda j: (j, 0, 0, 0)),
            pl.BlockSpec((2, count), lambda j: (0, 0)),
        ],
        out_specs=pl.BlockSpec((4, count), lambda j: (0, 0)),
        out_shape=jax.ShapeDtypeStruct((4, count), jnp.bfloat16),
        scratch_shapes=[pltpu.VMEM((2, 2, rows, cols), jnp.float32)],
    )(own_slab, next_edge, diag_rates, place)


def _lag_kernel(in_ref, out_ref, *, width, factor):
    values = in_ref[:, 0, :].astype(jnp.float32)
    energy_count = values.shape[0]
    lesser = values[:, 0:2 * width]
    greater = values[:, 2 * width:4 * width]
    swapped = jnp.concatenate([greater[:, width:], greater[:, :width]], axis=1)
    rows = []
    for lag in range(energy_count):
        head = lesser[lag:]
        straight = jnp.sum(head * greater[:energy_count - lag], axis=0, keepdims=True)
        crossed = jnp.sum(head * swapped[:energy_count - lag], axis=0, keepdims=True)
        rows.append(jnp.concatenate([straight[:, :width] - straight[:, width:], crossed[:, :width] + crossed[:, width:]], axis=1))
    out_ref[:, 0, :] = (jnp.concatenate(rows, axis=0) * factor).astype(out_ref.dtype)


def lag_sums(by_element):
    energy_count, _, joined = by_element.shape
    width = joined // 4
    kernel = functools.partial(_lag_kernel, width=width, factor=1.0 / math.sqrt(energy_count))
    return pl.pallas_call(
        kernel,
        out_shape=jax.ShapeDtypeStruct((energy_count, 1, 2 * width), jnp.bfloat16),
    )(by_element)


def _screen_kernel(polar_ref, place_ref, screen_ref, out_ref, *, rows, cols):
    def nt(a, b):
        return lax.dot_general(a, b, (((1,), (1,)), ((), ())), preferred_element_type=jnp.float32)

    def nn(a, b):
        return jnp.dot(a, b, preferred_element_type=jnp.float32)

    count = place_ref.shape[1]
    row_hit = lax.broadcasted_iota(jnp.int32, (rows, count), 0) == place_ref[0:1, :]
    col_hit = (lax.broadcasted_iota(jnp.int32, (cols, count), 0) == place_ref[1:2, :]).astype(jnp.bfloat16)
    polar = polar_ref[...].astype(jnp.float32)
    dense = []
    for part in range(2):
        spread = jnp.where(row_hit, polar[part:part + 1, :], 0.0).astype(jnp.bfloat16)
        dense.append(nt(spread, col_hit).astype(jnp.bfloat16))
    dense_real, dense_imag = dense
    screen_real = screen_ref[0]
    screen_imag = screen_ref[1]
    inner_real = (nt(dense_real, screen_real) + nt(dense_imag, screen_imag)).astype(jnp.bfloat16)
    inner_imag = (nt(dense_imag, screen_real) - nt(dense_real, screen_imag)).astype(jnp.bfloat16)
    near_real = screen_real[:, :rows]
    near_imag = screen_imag[:, :rows]
    side_real = screen_real[:, rows:]
    side_imag = screen_imag[:, rows:]
    edge_real = dense_real[:, rows:]
    edge_imag = dense_imag[:, rows:]
    across_real = (nn(near_real, edge_real) - nn(near_imag, edge_imag)).astype(jnp.bfloat16)
    across_imag = (nn(near_real, edge_imag) + nn(near_imag, edge_real)).astype(jnp.bfloat16)
    first_real = nn(near_real, inner_real) - nn(near_imag, inner_imag)
    first_imag = nn(near_real, inner_imag) + nn(near_imag, inner_real)
    second_real = nt(side_real, across_real) + nt(side_imag, across_imag)
    second_imag = nt(side_imag, across_real) - nt(side_real, across_imag)
    out_ref[0] = first_real + second_real
    out_ref[1] = first_imag + second_imag


def screen(polar_row, pattern_row, screen_block):
    rows = screen_block.shape[1]
    cols = screen_block.shape[2]
    place = jnp.stack([pattern_row // cols, pattern_row % cols], axis=0)
    kernel = functools.partial(_screen_kernel, rows=rows, cols=cols)
    return pl.pallas_call(
        kernel,
        out_shape=jax.ShapeDtypeStruct((2, rows, rows), jnp.float32),
    )(polar_row, place, screen_block)


def split_exact(value):
    high = lax.reduce_precision(value, exponent_bits=8, mantissa_bits=7)
    rest = value - high
    middle = lax.reduce_precision(rest, exponent_bits=8, mantissa_bits=7)
    low = rest - middle
    return jnp.stack([high, middle, low], axis=0).astype(jnp.bfloat16)


def join_exact(pieces):
    pieces = pieces.astype(jnp.float32)
    return (pieces[0] + pieces[1]) + pieces[2]


def body(green_slab, self_energy, pattern, screened):
    own_rate = self_energy[0, 0]
    block_order = own_rate.shape[-1]
    previous_rate = passed_along(own_rate, "domain", 1)
    edge_block = green_slab[0, 0, :, 0:2, :EDGE, :]
    bundle = jnp.concatenate(
        [edge_block.reshape(-1, block_order), split_exact(own_rate).reshape(-1, block_order)], axis=0
    )
    bundle = passed_along(bundle, "domain", -1)
    edge_rows = edge_block.size // block_order
    following = bundle[:edge_rows].reshape(edge_block.shape)
    next_rate = join_exact(bundle[edge_rows:].reshape(3, *own_rate.shape))
    nearby = jnp.stack([previous_rate, own_rate, next_rate], axis=0)[None]
    values = element_values(green_slab[0, 0], following, nearby[0], pattern[0])
    chunks = lax.axis_size("energy")
    values = values.reshape(4, chunks, -1).transpose(1, 0, 2).reshape(chunks, 1, -1)
    by_element = lax.all_to_all(values, "energy", split_axis=0, concat_axis=0, tiled=True)
    polarization = lag_sums(by_element)
    per_energy = lax.all_to_all(polarization, "energy", split_axis=0, concat_axis=0, tiled=True)
    per_energy = per_energy.reshape(chunks, 2, -1).transpose(1, 0, 2).reshape(2, -1)
    result = screen(per_energy, pattern[0], screened[0, 0])
    return result[None, None]


def solution(mesh):
    placed = (
        P("energy", "domain", None, None, None, None),
        P("energy", "domain", None, None, None),
        P("domain", None),
        P("energy", "domain", None, None, None),
    )
    return jax.shard_map(
        body,
        mesh=mesh,
        in_specs=placed,
        out_specs=P("energy", "domain", None, None, None),
        check_vma=False,
    )
```

```python
import functools
import math

import jax
import jax.numpy as jnp
from jax import lax
from jax.experimental import pallas as pl
from jax.experimental.pallas import tpu as pltpu
from jax.sharding import PartitionSpec as P

EDGE = 16


def passed_along(x, axis, by):
    length = lax.axis_size(axis)
    pairs = [(i, i + by) for i in range(length) if 0 <= i + by < length]
    return lax.ppermute(x, axis, pairs)


def _weigh(real_f, imag_f, rate_ref, block, factor):
    pieces = []
    for q in range(2):
        rate_real = rate_ref[block, q, 0:1, :]
        rate_imag = rate_ref[block, q, 1:2, :]
        pieces.append(((real_f * rate_real - imag_f * rate_imag) * factor).astype(jnp.bfloat16))
        pieces.append(((real_f * rate_imag + imag_f * rate_real) * factor).astype(jnp.bfloat16))
    return jnp.concatenate(pieces, axis=0)


def _adjoint_parts(prod, q, rows, start, width):
    wr = prod[2 * q * rows:(2 * q + 1) * rows]
    wi = prod[(2 * q + 1) * rows:(2 * q + 2) * rows]
    real = wr[:, start:start + width] + wi[:, start + width:start + 2 * width]
    imag = wi[:, start:start + width] - wr[:, start + width:start + 2 * width]
    return real, imag


def _nt(a, b):
    return lax.dot_general(a, b, (((1,), (1,)), ((), ())), preferred_element_type=jnp.float32)


def _early_kernel(slab_ref, rate_ref, near_ref, held_ref, *, factor, rows):
    step = pl.program_id(0)

    @pl.when(step == 0)
    def _():
        near_ref[...] = jnp.zeros_like(near_ref)

    slab_real = slab_ref[0, 0]
    slab_imag = slab_ref[1, 0]
    left = _weigh(slab_real.astype(jnp.float32), slab_imag.astype(jnp.float32), rate_ref, 0, factor)
    prod = _nt(left, jnp.concatenate([slab_real, slab_imag], axis=0))
    for q in range(2):
        real, imag = _adjoint_parts(prod, q, rows, 0, rows)
        near_ref[q, 0] += real
        near_ref[q, 1] += imag

    @pl.when(step == pl.num_programs(0) - 1)
    def _():
        held_ref[...] = left


def _late_kernel(slab_ref, bundle_ref, near_ref, held_ref, place_ref, out_ref, rate_scr,
                 *, factor, rows, edge):
    cols = rows + edge
    edge_rows = 4 * edge
    for piece_q in range(2):
        for part in range(2):
            k = piece_q * 2 + part
            pieces = [bundle_ref[edge_rows + 4 * t + k:edge_rows + 4 * t + k + 1, :].astype(jnp.float32)
                      for t in range(3)]
            rate_scr[0, piece_q, part:part + 1, :] = (pieces[0] + pieces[1]) + pieces[2]
    slab_real = slab_ref[0, 0]
    slab_imag = slab_ref[1, 0]
    left = _weigh(slab_real.astype(jnp.float32), slab_imag.astype(jnp.float32), rate_scr, 0, factor)

    def edge_of(part, block):
        start = part * 2 * edge + block * edge
        return bundle_ref[start:start + edge, :]

    far = _nt(left, jnp.concatenate([slab_real, slab_imag, edge_of(0, 1), edge_of(1, 1)], axis=0))
    own = _nt(held_ref[...], jnp.concatenate([edge_of(0, 0), edge_of(1, 0)], axis=0))
    joined = []
    for q in range(2):
        near_real, near_imag = _adjoint_parts(far, q, rows, 0, rows)
        far_real, far_imag = _adjoint_parts(far, q, rows, 2 * rows, edge)
        own_real, own_imag = _adjoint_parts(own, q, rows, 0, edge)
        joined.append(jnp.concatenate([near_ref[q, 0] + near_real, far_real + own_real], axis=1))
        joined.append(jnp.concatenate([near_ref[q, 1] + near_imag, far_imag + own_imag], axis=1))
    joined = jnp.concatenate(joined, axis=0).astype(jnp.bfloat16)
    count = place_ref.shape[1]
    col_hit = (lax.broadcasted_iota(jnp.int32, (cols, count), 0) == place_ref[1:2, :]).astype(jnp.bfloat16)
    row_hit = lax.broadcasted_iota(jnp.int32, (rows, count), 0) == place_ref[0:1, :]
    by_column = jnp.dot(joined, col_hit, preferred_element_type=jnp.float32)
    for k in range(4):
        picked = jnp.where(row_hit, by_column[k * rows:(k + 1) * rows], 0.0)
        out_ref[k:k + 1, :] = jnp.sum(picked, axis=0, keepdims=True).astype(out_ref.dtype)


def element_values(own_slab, bundle, early_rates, pattern_row, edge):
    _, blocks, rows, block_order = own_slab.shape
    cols = rows + edge
    count = pattern_row.shape[0]
    place = jnp.stack([pattern_row // cols, pattern_row % cols], axis=0)
    factor = 1.0 / math.sqrt(3.0 * block_order)
    near, held = pl.pallas_call(
        functools.partial(_early_kernel, factor=factor, rows=rows),
        grid=(blocks - 1,),
        in_specs=[
            pl.BlockSpec((2, 1, rows, block_order), lambda j: (0, j, 0, 0)),
            pl.BlockSpec((1, 2, 2, block_order), lambda j: (j, 0, 0, 0)),
        ],
        out_specs=[
            pl.BlockSpec((2, 2, rows, rows), lambda j: (0, 0, 0, 0)),
            pl.BlockSpec((4 * rows, block_order), lambda j: (0, 0)),
        ],
        out_shape=[
            jax.ShapeDtypeStruct((2, 2, rows, rows), jnp.float32),
            jax.ShapeDtypeStruct((4 * rows, block_order), jnp.bfloat16),
        ],
    )(own_slab, early_rates)
    last = blocks - 1
    return pl.pallas_call(
        functools.partial(_late_kernel, factor=factor, rows=rows, edge=edge),
        grid=(1,),
        in_specs=[
            pl.BlockSpec((2, 1, rows, block_order), lambda j: (0, last, 0, 0)),
            pl.BlockSpec(bundle.shape, lambda j: (0, 0)),
            pl.BlockSpec((2, 2, rows, rows), lambda j: (0, 0, 0, 0)),
            pl.BlockSpec((4 * rows, block_order), lambda j: (0, 0)),
            pl.BlockSpec((2, count), lambda j: (0, 0)),
        ],
        out_specs=pl.BlockSpec((4, count), lambda j: (0, 0)),
        out_shape=jax.ShapeDtypeStruct((4, count), jnp.bfloat16),
        scratch_shapes=[pltpu.VMEM((1, 2, 2, block_order), jnp.float32)],
    )(own_slab, bundle, near, held, place)


def _lag_kernel(in_ref, out_ref, *, width, factor):
    values = in_ref[:, 0, :].astype(jnp.float32)
    energy_count = values.shape[0]
    lesser = values[:, 0:2 * width]
    greater = values[:, 2 * width:4 * width]
    swapped = jnp.concatenate([greater[:, width:], greater[:, :width]], axis=1)
    rows = []
    for lag in range(energy_count):
        head = lesser[lag:]
        straight = jnp.sum(head * greater[:energy_count - lag], axis=0, keepdims=True)
        crossed = jnp.sum(head * swapped[:energy_count - lag], axis=0, keepdims=True)
        rows.append(jnp.concatenate([straight[:, :width] - straight[:, width:], crossed[:, :width] + crossed[:, width:]], axis=1))
    out_ref[:, 0, :] = (jnp.concatenate(rows, axis=0) * factor).astype(out_ref.dtype)


def lag_sums(by_element):
    energy_count, _, joined = by_element.shape
    width = joined // 4
    kernel = functools.partial(_lag_kernel, width=width, factor=1.0 / math.sqrt(energy_count))
    return pl.pallas_call(
        kernel,
        out_shape=jax.ShapeDtypeStruct((energy_count, 1, 2 * width), jnp.bfloat16),
    )(by_element)


def _screen_kernel(polar_ref, place_ref, screen_ref, out_ref, *, rows, cols):
    def nt(a, b):
        return lax.dot_general(a, b, (((1,), (1,)), ((), ())), preferred_element_type=jnp.float32)

    def nn(a, b):
        return jnp.dot(a, b, preferred_element_type=jnp.float32)

    count = place_ref.shape[1]
    row_hit = lax.broadcasted_iota(jnp.int32, (rows, count), 0) == place_ref[0:1, :]
    col_hit = (lax.broadcasted_iota(jnp.int32, (cols, count), 0) == place_ref[1:2, :]).astype(jnp.bfloat16)
    polar = polar_ref[...].astype(jnp.float32)
    dense = []
    for part in range(2):
        spread = jnp.where(row_hit, polar[part:part + 1, :], 0.0).astype(jnp.bfloat16)
        dense.append(nt(spread, col_hit).astype(jnp.bfloat16))
    dense_real, dense_imag = dense
    screen_real = screen_ref[0]
    screen_imag = screen_ref[1]
    inner_real = (nt(dense_real, screen_real) + nt(dense_imag, screen_imag)).astype(jnp.bfloat16)
    inner_imag = (nt(dense_imag, screen_real) - nt(dense_real, screen_imag)).astype(jnp.bfloat16)
    near_real = screen_real[:, :rows]
    near_imag = screen_imag[:, :rows]
    side_real = screen_real[:, rows:]
    side_imag = screen_imag[:, rows:]
    edge_real = dense_real[:, rows:]
    edge_imag = dense_imag[:, rows:]
    across_real = (nn(near_real, edge_real) - nn(near_imag, edge_imag)).astype(jnp.bfloat16)
    across_imag = (nn(near_real, edge_imag) + nn(near_imag, edge_real)).astype(jnp.bfloat16)
    first_real = nn(near_real, inner_real) - nn(near_imag, inner_imag)
    first_imag = nn(near_real, inner_imag) + nn(near_imag, inner_real)
    second_real = nt(side_real, across_real) + nt(side_imag, across_imag)
    second_imag = nt(side_imag, across_real) - nt(side_real, across_imag)
    out_ref[0] = first_real + second_real
    out_ref[1] = first_imag + second_imag


def screen(polar_row, pattern_row, screen_block):
    rows = screen_block.shape[1]
    cols = screen_block.shape[2]
    place = jnp.stack([pattern_row // cols, pattern_row % cols], axis=0)
    kernel = functools.partial(_screen_kernel, rows=rows, cols=cols)
    return pl.pallas_call(
        kernel,
        out_shape=jax.ShapeDtypeStruct((2, rows, rows), jnp.float32),
    )(polar_row, place, screen_block)


def split_exact(value):
    high = lax.reduce_precision(value, exponent_bits=8, mantissa_bits=7)
    rest = value - high
    middle = lax.reduce_precision(rest, exponent_bits=8, mantissa_bits=7)
    low = rest - middle
    return jnp.stack([high, middle, low], axis=0).astype(jnp.bfloat16)


def body(green_slab, self_energy, pattern, screened):
    own_rate = self_energy[0, 0]
    block_order = own_rate.shape[-1]
    previous_rate = passed_along(own_rate, "domain", 1)
    edge_block = green_slab[0, 0, :, 0:2, :EDGE, :]
    bundle = jnp.concatenate(
        [edge_block.reshape(-1, block_order), split_exact(own_rate).reshape(-1, block_order)], axis=0
    )
    bundle = passed_along(bundle, "domain", -1)
    early_rates = jnp.stack([previous_rate, own_rate], axis=0)
    values = element_values(green_slab[0, 0], bundle, early_rates, pattern[0], EDGE)
    chunks = lax.axis_size("energy")
    values = values.reshape(4, chunks, -1).transpose(1, 0, 2).reshape(chunks, 1, -1)
    by_element = lax.all_to_all(values, "energy", split_axis=0, concat_axis=0, tiled=True)
    polarization = lag_sums(by_element)
    per_energy = lax.all_to_all(polarization, "energy", split_axis=0, concat_axis=0, tiled=True)
    per_energy = per_energy.reshape(chunks, 2, -1).transpose(1, 0, 2).reshape(2, -1)
    result = screen(per_energy, pattern[0], screened[0, 0])
    return result[None, None]


def solution(mesh):
    placed = (
        P("energy", "domain", None, None, None, None),
        P("energy", "domain", None, None, None),
        P("domain", None),
        P("energy", "domain", None, None, None),
    )
    return jax.shard_map(
        body,
        mesh=mesh,
        in_specs=placed,
        out_specs=P("energy", "domain", None, None, None),
        check_vma=False,
    )
```

```python
import functools
import math

import jax
import jax.numpy as jnp
from jax import lax
from jax.experimental import pallas as pl
from jax.experimental.pallas import tpu as pltpu
from jax.sharding import PartitionSpec as P

EDGE = 16


def passed_along(x, axis, by):
    length = lax.axis_size(axis)
    pairs = [(i, i + by) for i in range(length) if 0 <= i + by < length]
    return lax.ppermute(x, axis, pairs)


def _weigh(real_f, imag_f, rate_ref, block, factor):
    pieces = []
    for q in range(2):
        rate_real = rate_ref[block, q, 0:1, :]
        rate_imag = rate_ref[block, q, 1:2, :]
        pieces.append(((real_f * rate_real - imag_f * rate_imag) * factor).astype(jnp.bfloat16))
        pieces.append(((real_f * rate_imag + imag_f * rate_real) * factor).astype(jnp.bfloat16))
    return jnp.concatenate(pieces, axis=0)


def _adjoint_parts(prod, q, rows, start, width):
    wr = prod[2 * q * rows:(2 * q + 1) * rows]
    wi = prod[(2 * q + 1) * rows:(2 * q + 2) * rows]
    real = wr[:, start:start + width] + wi[:, start + width:start + 2 * width]
    imag = wi[:, start:start + width] - wr[:, start + width:start + 2 * width]
    return real, imag


def _place_hits(pattern_ref, rows, cols):
    count = pattern_ref.shape[1]
    position = pattern_ref[...].astype(jnp.float32)
    row = jnp.floor((position + 0.5) * (1.0 / cols))
    col = position - row * cols
    row_hit = lax.broadcasted_iota(jnp.int32, (rows, count), 0).astype(jnp.float32) == row
    col_hit = lax.broadcasted_iota(jnp.int32, (cols, count), 0).astype(jnp.float32) == col
    return row_hit, col_hit


def _nt(a, b):
    return lax.dot_general(a, b, (((1,), (1,)), ((), ())), preferred_element_type=jnp.float32)


def _early_kernel(slab_ref, previous_ref, own_ref, near_ref, held_ref, rate_scr, *, factor, rows):
    step = pl.program_id(0)

    @pl.when(step == 0)
    def _():
        near_ref[...] = jnp.zeros_like(near_ref)
        rate_scr[0] = previous_ref[...]

    @pl.when(step > 0)
    def _():
        rate_scr[0] = own_ref[...]

    slab_real = slab_ref[0, 0]
    slab_imag = slab_ref[1, 0]
    left = _weigh(slab_real.astype(jnp.float32), slab_imag.astype(jnp.float32), rate_scr, 0, factor)
    prod = _nt(left, jnp.concatenate([slab_real, slab_imag], axis=0))
    for q in range(2):
        real, imag = _adjoint_parts(prod, q, rows, 0, rows)
        near_ref[q, 0] += real
        near_ref[q, 1] += imag

    @pl.when(step == pl.num_programs(0) - 1)
    def _():
        held_ref[...] = left


def _late_kernel(slab_ref, bundle_ref, near_ref, held_ref, place_ref, out_ref, rate_scr,
                 *, factor, rows, edge):
    cols = rows + edge
    edge_rows = 4 * edge
    for piece_q in range(2):
        for part in range(2):
            k = piece_q * 2 + part
            pieces = [bundle_ref[edge_rows + 4 * t + k:edge_rows + 4 * t + k + 1, :].astype(jnp.float32)
                      for t in range(3)]
            rate_scr[0, piece_q, part:part + 1, :] = (pieces[0] + pieces[1]) + pieces[2]
    slab_real = slab_ref[0, 0]
    slab_imag = slab_ref[1, 0]
    left = _weigh(slab_real.astype(jnp.float32), slab_imag.astype(jnp.float32), rate_scr, 0, factor)

    def edge_of(part, block):
        start = part * 2 * edge + block * edge
        return bundle_ref[start:start + edge, :]

    far = _nt(left, jnp.concatenate([slab_real, slab_imag, edge_of(0, 1), edge_of(1, 1)], axis=0))
    own = _nt(held_ref[...], jnp.concatenate([edge_of(0, 0), edge_of(1, 0)], axis=0))
    joined = []
    for q in range(2):
        near_real, near_imag = _adjoint_parts(far, q, rows, 0, rows)
        far_real, far_imag = _adjoint_parts(far, q, rows, 2 * rows, edge)
        own_real, own_imag = _adjoint_parts(own, q, rows, 0, edge)
        joined.append(jnp.concatenate([near_ref[q, 0] + near_real, far_real + own_real], axis=1))
        joined.append(jnp.concatenate([near_ref[q, 1] + near_imag, far_imag + own_imag], axis=1))
    joined = jnp.concatenate(joined, axis=0).astype(jnp.bfloat16)
    row_hit, col_hit = _place_hits(place_ref, rows, cols)
    by_column = jnp.dot(joined, col_hit.astype(jnp.bfloat16), preferred_element_type=jnp.float32)
    for k in range(4):
        picked = jnp.where(row_hit, by_column[k * rows:(k + 1) * rows], 0.0)
        out_ref[k:k + 1, :] = jnp.sum(picked, axis=0, keepdims=True).astype(out_ref.dtype)


def element_values(own_slab, bundle, previous_rate, own_rate, pattern_row, edge):
    _, blocks, rows, block_order = own_slab.shape
    count = pattern_row.shape[1]
    factor = 1.0 / math.sqrt(3.0 * block_order)
    near, held = pl.pallas_call(
        functools.partial(_early_kernel, factor=factor, rows=rows),
        grid=(blocks - 1,),
        in_specs=[
            pl.BlockSpec((2, 1, rows, block_order), lambda j: (0, j, 0, 0)),
            pl.BlockSpec((2, 2, block_order), lambda j: (0, 0, 0)),
            pl.BlockSpec((2, 2, block_order), lambda j: (0, 0, 0)),
        ],
        out_specs=[
            pl.BlockSpec((2, 2, rows, rows), lambda j: (0, 0, 0, 0)),
            pl.BlockSpec((4 * rows, block_order), lambda j: (0, 0)),
        ],
        scratch_shapes=[pltpu.VMEM((1, 2, 2, block_order), jnp.float32)],
        out_shape=[
            jax.ShapeDtypeStruct((2, 2, rows, rows), jnp.float32),
            jax.ShapeDtypeStruct((4 * rows, block_order), jnp.bfloat16),
        ],
    )(own_slab, previous_rate, own_rate)
    last = blocks - 1
    return pl.pallas_call(
        functools.partial(_late_kernel, factor=factor, rows=rows, edge=edge),
        grid=(1,),
        in_specs=[
            pl.BlockSpec((2, 1, rows, block_order), lambda j: (0, last, 0, 0)),
            pl.BlockSpec(bundle.shape, lambda j: (0, 0)),
            pl.BlockSpec((2, 2, rows, rows), lambda j: (0, 0, 0, 0)),
            pl.BlockSpec((4 * rows, block_order), lambda j: (0, 0)),
            pl.BlockSpec((1, count), lambda j: (0, 0)),
        ],
        out_specs=pl.BlockSpec((4, count), lambda j: (0, 0)),
        out_shape=jax.ShapeDtypeStruct((4, count), jnp.bfloat16),
        scratch_shapes=[pltpu.VMEM((1, 2, 2, block_order), jnp.float32)],
    )(own_slab, bundle, near, held, pattern_row)


def _lag_kernel(in_ref, out_ref, *, width, factor):
    values = in_ref[:, 0, :].astype(jnp.float32)
    energy_count = values.shape[0]
    lesser = values[:, 0:2 * width]
    greater = values[:, 2 * width:4 * width]
    swapped = jnp.concatenate([greater[:, width:], greater[:, :width]], axis=1)
    rows = []
    for lag in range(energy_count):
        head = lesser[lag:]
        straight = jnp.sum(head * greater[:energy_count - lag], axis=0, keepdims=True)
        crossed = jnp.sum(head * swapped[:energy_count - lag], axis=0, keepdims=True)
        rows.append(jnp.concatenate([straight[:, :width] - straight[:, width:], crossed[:, :width] + crossed[:, width:]], axis=1))
    out_ref[:, 0, :] = (jnp.concatenate(rows, axis=0) * factor).astype(out_ref.dtype)


def lag_sums(by_element):
    energy_count, _, joined = by_element.shape
    width = joined // 4
    kernel = functools.partial(_lag_kernel, width=width, factor=1.0 / math.sqrt(energy_count))
    return pl.pallas_call(
        kernel,
        out_shape=jax.ShapeDtypeStruct((energy_count, 1, 2 * width), jnp.bfloat16),
    )(by_element)


def _screen_kernel(polar_ref, place_ref, screen_ref, out_ref, *, rows, cols):
    def nt(a, b):
        return lax.dot_general(a, b, (((1,), (1,)), ((), ())), preferred_element_type=jnp.float32)

    def nn(a, b):
        return jnp.dot(a, b, preferred_element_type=jnp.float32)

    row_hit, col_hit = _place_hits(place_ref, rows, cols)
    col_hit = col_hit.astype(jnp.bfloat16)
    polar = polar_ref[...].astype(jnp.float32)
    dense = []
    for part in range(2):
        spread = jnp.where(row_hit, polar[part:part + 1, :], 0.0).astype(jnp.bfloat16)
        dense.append(nt(spread, col_hit).astype(jnp.bfloat16))
    dense_real, dense_imag = dense
    screen_real = screen_ref[0]
    screen_imag = screen_ref[1]
    inner_real = (nt(dense_real, screen_real) + nt(dense_imag, screen_imag)).astype(jnp.bfloat16)
    inner_imag = (nt(dense_imag, screen_real) - nt(dense_real, screen_imag)).astype(jnp.bfloat16)
    near_real = screen_real[:, :rows]
    near_imag = screen_imag[:, :rows]
    side_real = screen_real[:, rows:]
    side_imag = screen_imag[:, rows:]
    edge_real = dense_real[:, rows:]
    edge_imag = dense_imag[:, rows:]
    across_real = (nn(near_real, edge_real) - nn(near_imag, edge_imag)).astype(jnp.bfloat16)
    across_imag = (nn(near_real, edge_imag) + nn(near_imag, edge_real)).astype(jnp.bfloat16)
    first_real = nn(near_real, inner_real) - nn(near_imag, inner_imag)
    first_imag = nn(near_real, inner_imag) + nn(near_imag, inner_real)
    second_real = nt(side_real, across_real) + nt(side_imag, across_imag)
    second_imag = nt(side_imag, across_real) - nt(side_real, across_imag)
    out_ref[0] = first_real + second_real
    out_ref[1] = first_imag + second_imag


def screen(polar_row, pattern_row, screen_block):
    rows = screen_block.shape[1]
    cols = screen_block.shape[2]
    kernel = functools.partial(_screen_kernel, rows=rows, cols=cols)
    return pl.pallas_call(
        kernel,
        out_shape=jax.ShapeDtypeStruct((2, rows, rows), jnp.float32),
    )(polar_row, pattern_row, screen_block)


def split_exact(value):
    high = lax.reduce_precision(value, exponent_bits=8, mantissa_bits=7)
    rest = value - high
    middle = lax.reduce_precision(rest, exponent_bits=8, mantissa_bits=7)
    low = rest - middle
    return jnp.stack([high, middle, low], axis=0).astype(jnp.bfloat16)


def body(green_slab, self_energy, pattern, screened):
    own_rate = self_energy[0, 0]
    block_order = own_rate.shape[-1]
    previous_rate = passed_along(own_rate, "domain", 1)
    edge_block = green_slab[0, 0, :, 0:2, :EDGE, :]
    bundle = jnp.concatenate(
        [edge_block.reshape(-1, block_order), split_exact(own_rate).reshape(-1, block_order)], axis=0
    )
    bundle = passed_along(bundle, "domain", -1)
    values = element_values(green_slab[0, 0], bundle, previous_rate, own_rate, pattern, EDGE)
    chunks = lax.axis_size("energy")
    values = values.reshape(4, chunks, -1).transpose(1, 0, 2).reshape(chunks, 1, -1)
    by_element = lax.all_to_all(values, "energy", split_axis=0, concat_axis=0, tiled=True)
    polarization = lag_sums(by_element)
    per_energy = lax.all_to_all(polarization, "energy", split_axis=0, concat_axis=0, tiled=True)
    per_energy = per_energy.reshape(chunks, 2, -1).transpose(1, 0, 2).reshape(2, -1)
    result = screen(per_energy, pattern, screened[0, 0])
    return result[None, None]


def solution(mesh):
    placed = (
        P("energy", "domain", None, None, None, None),
        P("energy", "domain", None, None, None),
        P("domain", None),
        P("energy", "domain", None, None, None),
    )
    return jax.shard_map(
        body,
        mesh=mesh,
        in_specs=placed,
        out_specs=P("energy", "domain", None, None, None),
        check_vma=False,
    )
```

```python
import functools
import math

import jax
import jax.numpy as jnp
from jax import lax
from jax.experimental import pallas as pl
from jax.experimental.pallas import tpu as pltpu
from jax.sharding import PartitionSpec as P

EDGE = 16


def passed_along(x, axis, by):
    length = lax.axis_size(axis)
    pairs = [(i, i + by) for i in range(length) if 0 <= i + by < length]
    return lax.ppermute(x, axis, pairs)


def _weigh(real_f, imag_f, rate_ref, block, factor):
    pieces = []
    for q in range(2):
        rate_real = rate_ref[block, q, 0:1, :]
        rate_imag = rate_ref[block, q, 1:2, :]
        pieces.append(((real_f * rate_real - imag_f * rate_imag) * factor).astype(jnp.bfloat16))
        pieces.append(((real_f * rate_imag + imag_f * rate_real) * factor).astype(jnp.bfloat16))
    return jnp.concatenate(pieces, axis=0)


def _adjoint_parts(prod, q, rows, start, width):
    wr = prod[2 * q * rows:(2 * q + 1) * rows]
    wi = prod[(2 * q + 1) * rows:(2 * q + 2) * rows]
    real = wr[:, start:start + width] + wi[:, start + width:start + 2 * width]
    imag = wi[:, start:start + width] - wr[:, start + width:start + 2 * width]
    return real, imag


def _place_hits(pattern_ref, rows, cols):
    count = pattern_ref.shape[1]
    position = pattern_ref[...].astype(jnp.float32)
    row = jnp.floor((position + 0.5) * (1.0 / cols))
    col = position - row * cols
    row_hit = lax.broadcasted_iota(jnp.int32, (rows, count), 0).astype(jnp.float32) == row
    col_hit = lax.broadcasted_iota(jnp.int32, (cols, count), 0).astype(jnp.float32) == col
    return row_hit, col_hit


def _nt(a, b):
    return lax.dot_general(a, b, (((1,), (1,)), ((), ())), preferred_element_type=jnp.float32)


def _early_kernel(slab_ref, previous_ref, own_ref, near_ref, held_ref, rate_scr, *, factor, rows):
    step = pl.program_id(0)

    @pl.when(step == 0)
    def _():
        near_ref[...] = jnp.zeros_like(near_ref)
        rate_scr[0] = previous_ref[...]

    @pl.when(step > 0)
    def _():
        rate_scr[0] = own_ref[...]

    slab_real = slab_ref[0, 0]
    slab_imag = slab_ref[1, 0]
    left = _weigh(slab_real.astype(jnp.float32), slab_imag.astype(jnp.float32), rate_scr, 0, factor)
    prod = _nt(left, jnp.concatenate([slab_real, slab_imag], axis=0))
    for q in range(2):
        real, imag = _adjoint_parts(prod, q, rows, 0, rows)
        near_ref[q, 0] += real
        near_ref[q, 1] += imag

    @pl.when(step == pl.num_programs(0) - 1)
    def _():
        held_ref[...] = left


def _late_kernel(slab_ref, bundle_ref, near_ref, held_ref, place_ref, out_ref, rate_scr,
                 *, factor, rows, edge):
    cols = rows + edge
    edge_rows = 4 * edge
    for piece_q in range(2):
        for part in range(2):
            k = piece_q * 2 + part
            pieces = [bundle_ref[edge_rows + 4 * t + k:edge_rows + 4 * t + k + 1, :].astype(jnp.float32)
                      for t in range(3)]
            rate_scr[0, piece_q, part:part + 1, :] = (pieces[0] + pieces[1]) + pieces[2]
    slab_real = slab_ref[0, 0]
    slab_imag = slab_ref[1, 0]
    left = _weigh(slab_real.astype(jnp.float32), slab_imag.astype(jnp.float32), rate_scr, 0, factor)

    def edge_of(part, block):
        start = part * 2 * edge + block * edge
        return bundle_ref[start:start + edge, :]

    far = _nt(left, jnp.concatenate([slab_real, slab_imag, edge_of(0, 1), edge_of(1, 1)], axis=0))
    own = _nt(held_ref[...], jnp.concatenate([edge_of(0, 0), edge_of(1, 0)], axis=0))
    joined = []
    for q in range(2):
        near_real, near_imag = _adjoint_parts(far, q, rows, 0, rows)
        far_real, far_imag = _adjoint_parts(far, q, rows, 2 * rows, edge)
        own_real, own_imag = _adjoint_parts(own, q, rows, 0, edge)
        joined.append(jnp.concatenate([near_ref[q, 0] + near_real, far_real + own_real], axis=1))
        joined.append(jnp.concatenate([near_ref[q, 1] + near_imag, far_imag + own_imag], axis=1))
    joined = jnp.concatenate(joined, axis=0).astype(jnp.bfloat16)
    row_hit, col_hit = _place_hits(place_ref, rows, cols)
    by_column = jnp.dot(joined, col_hit.astype(jnp.bfloat16), preferred_element_type=jnp.float32)
    for k in range(4):
        picked = jnp.where(row_hit, by_column[k * rows:(k + 1) * rows], 0.0)
        out_ref[k:k + 1, :] = jnp.sum(picked, axis=0, keepdims=True).astype(out_ref.dtype)


def element_values(own_slab, bundle, previous_rate, own_rate, pattern_row, edge):
    _, blocks, rows, block_order = own_slab.shape
    count = pattern_row.shape[1]
    factor = 1.0 / math.sqrt(3.0 * block_order)
    near, held = pl.pallas_call(
        functools.partial(_early_kernel, factor=factor, rows=rows),
        grid=(blocks - 1,),
        in_specs=[
            pl.BlockSpec((2, 1, rows, block_order), lambda j: (0, j, 0, 0)),
            pl.BlockSpec((2, 2, block_order), lambda j: (0, 0, 0)),
            pl.BlockSpec((2, 2, block_order), lambda j: (0, 0, 0)),
        ],
        out_specs=[
            pl.BlockSpec((2, 2, rows, rows), lambda j: (0, 0, 0, 0)),
            pl.BlockSpec((4 * rows, block_order), lambda j: (0, 0)),
        ],
        scratch_shapes=[pltpu.VMEM((1, 2, 2, block_order), jnp.float32)],
        out_shape=[
            jax.ShapeDtypeStruct((2, 2, rows, rows), jnp.float32),
            jax.ShapeDtypeStruct((4 * rows, block_order), jnp.bfloat16),
        ],
    )(own_slab, previous_rate, own_rate)
    last = blocks - 1
    return pl.pallas_call(
        functools.partial(_late_kernel, factor=factor, rows=rows, edge=edge),
        grid=(1,),
        in_specs=[
            pl.BlockSpec((2, 1, rows, block_order), lambda j: (0, last, 0, 0)),
            pl.BlockSpec(bundle.shape, lambda j: (0, 0)),
            pl.BlockSpec((2, 2, rows, rows), lambda j: (0, 0, 0, 0)),
            pl.BlockSpec((4 * rows, block_order), lambda j: (0, 0)),
            pl.BlockSpec((1, count), lambda j: (0, 0)),
        ],
        out_specs=pl.BlockSpec((4, count), lambda j: (0, 0)),
        out_shape=jax.ShapeDtypeStruct((4, count), jnp.bfloat16),
        scratch_shapes=[pltpu.VMEM((1, 2, 2, block_order), jnp.float32)],
    )(own_slab, bundle, near, held, pattern_row)


def _lag_kernel(in_ref, out_ref, *, width, factor):
    values = in_ref[:, 0, :].astype(jnp.float32)
    energy_count = values.shape[0]
    lesser = values[:, 0:2 * width]
    greater = values[:, 2 * width:4 * width]
    swapped = jnp.concatenate([greater[:, width:], greater[:, :width]], axis=1)
    rows = []
    for lag in range(energy_count):
        head = lesser[lag:]
        straight = jnp.sum(head * greater[:energy_count - lag], axis=0, keepdims=True)
        crossed = jnp.sum(head * swapped[:energy_count - lag], axis=0, keepdims=True)
        rows.append(jnp.concatenate([straight[:, :width] - straight[:, width:], crossed[:, :width] + crossed[:, width:]], axis=1))
    out_ref[:, 0, :] = (jnp.concatenate(rows, axis=0) * factor).astype(out_ref.dtype)


def lag_sums(by_element):
    energy_count, _, joined = by_element.shape
    width = joined // 4
    kernel = functools.partial(_lag_kernel, width=width, factor=1.0 / math.sqrt(energy_count))
    return pl.pallas_call(
        kernel,
        out_shape=jax.ShapeDtypeStruct((energy_count, 1, 2 * width), jnp.bfloat16),
    )(by_element)


def _screen_kernel(polar_ref, place_ref, screen_ref, out_ref, *, rows, cols):
    def nt(a, b):
        return lax.dot_general(a, b, (((1,), (1,)), ((), ())), preferred_element_type=jnp.float32)

    def nn(a, b):
        return jnp.dot(a, b, preferred_element_type=jnp.float32)

    row_hit, col_hit = _place_hits(place_ref, rows, cols)
    col_hit = col_hit.astype(jnp.bfloat16)
    polar = polar_ref[...].astype(jnp.float32)
    dense = []
    for part in range(2):
        spread = jnp.where(row_hit, polar[part:part + 1, :], 0.0).astype(jnp.bfloat16)
        dense.append(nt(spread, col_hit).astype(jnp.bfloat16))
    dense_real, dense_imag = dense
    screen_real = screen_ref[0]
    screen_imag = screen_ref[1]
    inner_real = (nt(dense_real, screen_real) + nt(dense_imag, screen_imag)).astype(jnp.bfloat16)
    inner_imag = (nt(dense_imag, screen_real) - nt(dense_real, screen_imag)).astype(jnp.bfloat16)
    near_real = screen_real[:, :rows]
    near_imag = screen_imag[:, :rows]
    side_real = screen_real[:, rows:]
    side_imag = screen_imag[:, rows:]
    edge_real = dense_real[:, rows:]
    edge_imag = dense_imag[:, rows:]
    across_real = (nn(near_real, edge_real) - nn(near_imag, edge_imag)).astype(jnp.bfloat16)
    across_imag = (nn(near_real, edge_imag) + nn(near_imag, edge_real)).astype(jnp.bfloat16)
    first_real = nn(near_real, inner_real) - nn(near_imag, inner_imag)
    first_imag = nn(near_real, inner_imag) + nn(near_imag, inner_real)
    second_real = nt(side_real, across_real) + nt(side_imag, across_imag)
    second_imag = nt(side_imag, across_real) - nt(side_real, across_imag)
    out_ref[0] = first_real + second_real
    out_ref[1] = first_imag + second_imag


def screen(polar_row, pattern_row, screen_block):
    rows = screen_block.shape[1]
    cols = screen_block.shape[2]
    kernel = functools.partial(_screen_kernel, rows=rows, cols=cols)
    return pl.pallas_call(
        kernel,
        out_shape=jax.ShapeDtypeStruct((2, rows, rows), jnp.float32),
    )(polar_row, pattern_row, screen_block)


def _bundle_kernel(slab_ref, rate_ref, out_ref, *, edge):
    for part in range(2):
        for block in range(2):
            start = (part * 2 + block) * edge
            out_ref[start:start + edge, :] = slab_ref[part, block]
    for q in range(2):
        value = rate_ref[q]
        high = value.astype(jnp.bfloat16)
        rest = value - high.astype(jnp.float32)
        middle = rest.astype(jnp.bfloat16)
        low = (rest - middle.astype(jnp.float32)).astype(jnp.bfloat16)
        for t, piece in enumerate((high, middle, low)):
            start = 4 * edge + 4 * t + 2 * q
            out_ref[start:start + 2, :] = piece


def make_bundle(own_slab, own_rate, edge):
    _, _, rows, block_order = own_slab.shape
    return pl.pallas_call(
        functools.partial(_bundle_kernel, edge=edge),
        grid=(1,),
        in_specs=[
            pl.BlockSpec((2, 2, edge, block_order), lambda j: (0, 0, 0, 0)),
            pl.BlockSpec(own_rate.shape, lambda j: (0, 0, 0)),
        ],
        out_specs=pl.BlockSpec((4 * edge + 12, block_order), lambda j: (0, 0)),
        out_shape=jax.ShapeDtypeStruct((4 * edge + 12, block_order), jnp.bfloat16),
    )(own_slab, own_rate)


def body(green_slab, self_energy, pattern, screened):
    own_rate = self_energy[0, 0]
    previous_rate = passed_along(own_rate, "domain", 1)
    bundle = make_bundle(green_slab[0, 0], own_rate, EDGE)
    bundle = passed_along(bundle, "domain", -1)
    values = element_values(green_slab[0, 0], bundle, previous_rate, own_rate, pattern, EDGE)
    chunks = lax.axis_size("energy")
    values = values.reshape(4, chunks, -1).transpose(1, 0, 2).reshape(chunks, 1, -1)
    by_element = lax.all_to_all(values, "energy", split_axis=0, concat_axis=0, tiled=True)
    polarization = lag_sums(by_element)
    per_energy = lax.all_to_all(polarization, "energy", split_axis=0, concat_axis=0, tiled=True)
    per_energy = per_energy.reshape(chunks, 2, -1).transpose(1, 0, 2).reshape(2, -1)
    result = screen(per_energy, pattern, screened[0, 0])
    return result[None, None]


def solution(mesh):
    placed = (
        P("energy", "domain", None, None, None, None),
        P("energy", "domain", None, None, None),
        P("domain", None),
        P("energy", "domain", None, None, None),
    )
    return jax.shard_map(
        body,
        mesh=mesh,
        in_specs=placed,
        out_specs=P("energy", "domain", None, None, None),
        check_vma=False,
    )
```

```python
import functools
import math

import jax
import jax.numpy as jnp
from jax import lax
from jax.experimental import pallas as pl
from jax.experimental.pallas import tpu as pltpu
from jax.sharding import PartitionSpec as P

EDGE = 16


def passed_along(x, axis, by):
    length = lax.axis_size(axis)
    pairs = [(i, i + by) for i in range(length) if 0 <= i + by < length]
    return lax.ppermute(x, axis, pairs)


def _weigh(real_f, imag_f, rate_ref, block, factor):
    pieces = []
    for q in range(2):
        rate_real = rate_ref[block, q, 0:1, :]
        rate_imag = rate_ref[block, q, 1:2, :]
        pieces.append(((real_f * rate_real - imag_f * rate_imag) * factor).astype(jnp.bfloat16))
        pieces.append(((real_f * rate_imag + imag_f * rate_real) * factor).astype(jnp.bfloat16))
    return jnp.concatenate(pieces, axis=0)


def _adjoint_parts(prod, q, rows, start, width):
    wr = prod[2 * q * rows:(2 * q + 1) * rows]
    wi = prod[(2 * q + 1) * rows:(2 * q + 2) * rows]
    real = wr[:, start:start + width] + wi[:, start + width:start + 2 * width]
    imag = wi[:, start:start + width] - wr[:, start + width:start + 2 * width]
    return real, imag


def _place_hits(pattern_ref, rows, cols):
    count = pattern_ref.shape[1]
    position = pattern_ref[...].astype(jnp.float32)
    row = jnp.floor((position + 0.5) * (1.0 / cols))
    col = position - row * cols
    row_hit = lax.broadcasted_iota(jnp.int32, (rows, count), 0).astype(jnp.float32) == row
    col_hit = lax.broadcasted_iota(jnp.int32, (cols, count), 0).astype(jnp.float32) == col
    return row_hit, col_hit


def _nt(a, b):
    return lax.dot_general(a, b, (((1,), (1,)), ((), ())), preferred_element_type=jnp.float32)


def _early_kernel(slab_ref, previous_ref, own_ref, near_ref, held_ref, rate_scr, *, factor, rows):
    step = pl.program_id(0)

    @pl.when(step == 0)
    def _():
        near_ref[...] = jnp.zeros_like(near_ref)
        rate_scr[0] = previous_ref[...]

    @pl.when(step > 0)
    def _():
        rate_scr[0] = own_ref[...]

    slab_real = slab_ref[0, 0]
    slab_imag = slab_ref[1, 0]
    left = _weigh(slab_real.astype(jnp.float32), slab_imag.astype(jnp.float32), rate_scr, 0, factor)
    prod = _nt(left, jnp.concatenate([slab_real, slab_imag], axis=0))
    for q in range(2):
        real, imag = _adjoint_parts(prod, q, rows, 0, rows)
        near_ref[q, 0] += real
        near_ref[q, 1] += imag

    @pl.when(step == pl.num_programs(0) - 1)
    def _():
        held_ref[...] = left


def _late_kernel(slab_ref, bundle_ref, near_ref, held_ref, place_ref, out_ref, rate_scr,
                 *, factor, rows, edge):
    cols = rows + edge
    edge_rows = 4 * edge
    for piece_q in range(2):
        for part in range(2):
            k = piece_q * 2 + part
            pieces = [bundle_ref[edge_rows + 4 * t + k:edge_rows + 4 * t + k + 1, :].astype(jnp.float32)
                      for t in range(3)]
            rate_scr[0, piece_q, part:part + 1, :] = (pieces[0] + pieces[1]) + pieces[2]
    slab_real = slab_ref[0, 0]
    slab_imag = slab_ref[1, 0]
    left = _weigh(slab_real.astype(jnp.float32), slab_imag.astype(jnp.float32), rate_scr, 0, factor)

    def edge_of(part, block):
        start = part * 2 * edge + block * edge
        return bundle_ref[start:start + edge, :]

    far = _nt(left, jnp.concatenate([slab_real, slab_imag, edge_of(0, 1), edge_of(1, 1)], axis=0))
    own = _nt(held_ref[...], jnp.concatenate([edge_of(0, 0), edge_of(1, 0)], axis=0))
    joined = []
    for q in range(2):
        near_real, near_imag = _adjoint_parts(far, q, rows, 0, rows)
        far_real, far_imag = _adjoint_parts(far, q, rows, 2 * rows, edge)
        own_real, own_imag = _adjoint_parts(own, q, rows, 0, edge)
        joined.append(jnp.concatenate([near_ref[q, 0] + near_real, far_real + own_real], axis=1))
        joined.append(jnp.concatenate([near_ref[q, 1] + near_imag, far_imag + own_imag], axis=1))
    joined = jnp.concatenate(joined, axis=0).astype(jnp.bfloat16)
    row_hit, col_hit = _place_hits(place_ref, rows, cols)
    by_column = jnp.dot(joined, col_hit.astype(jnp.bfloat16), preferred_element_type=jnp.float32)
    for k in range(4):
        picked = jnp.where(row_hit, by_column[k * rows:(k + 1) * rows], 0.0)
        out_ref[k:k + 1, :] = jnp.sum(picked, axis=0, keepdims=True).astype(out_ref.dtype)


def element_values(own_slab, bundle, previous_rate, own_rate, pattern_row, edge):
    _, blocks, rows, block_order = own_slab.shape
    count = pattern_row.shape[1]
    factor = 1.0 / math.sqrt(3.0 * block_order)
    near, held = pl.pallas_call(
        functools.partial(_early_kernel, factor=factor, rows=rows),
        grid=(blocks - 1,),
        in_specs=[
            pl.BlockSpec((2, 1, rows, block_order), lambda j: (0, j, 0, 0)),
            pl.BlockSpec((2, 2, block_order), lambda j: (0, 0, 0)),
            pl.BlockSpec((2, 2, block_order), lambda j: (0, 0, 0)),
        ],
        out_specs=[
            pl.BlockSpec((2, 2, rows, rows), lambda j: (0, 0, 0, 0)),
            pl.BlockSpec((4 * rows, block_order), lambda j: (0, 0)),
        ],
        scratch_shapes=[pltpu.VMEM((1, 2, 2, block_order), jnp.float32)],
        out_shape=[
            jax.ShapeDtypeStruct((2, 2, rows, rows), jnp.float32),
            jax.ShapeDtypeStruct((4 * rows, block_order), jnp.bfloat16),
        ],
    )(own_slab, previous_rate, own_rate)
    last = blocks - 1
    return pl.pallas_call(
        functools.partial(_late_kernel, factor=factor, rows=rows, edge=edge),
        grid=(1,),
        in_specs=[
            pl.BlockSpec((2, 1, rows, block_order), lambda j: (0, last, 0, 0)),
            pl.BlockSpec(bundle.shape, lambda j: (0, 0)),
            pl.BlockSpec((2, 2, rows, rows), lambda j: (0, 0, 0, 0)),
            pl.BlockSpec((4 * rows, block_order), lambda j: (0, 0)),
            pl.BlockSpec((1, count), lambda j: (0, 0)),
        ],
        out_specs=pl.BlockSpec((4, count), lambda j: (0, 0)),
        out_shape=jax.ShapeDtypeStruct((4, count), jnp.bfloat16),
        scratch_shapes=[pltpu.VMEM((1, 2, 2, block_order), jnp.float32)],
    )(own_slab, bundle, near, held, pattern_row)


def _lag_kernel(in_ref, out_ref, *, width, factor):
    values = in_ref[:, 0, :].astype(jnp.float32)
    energy_count = values.shape[0]
    lesser = values[:, 0:2 * width]
    greater = values[:, 2 * width:4 * width]
    swapped = jnp.concatenate([greater[:, width:], greater[:, :width]], axis=1)
    padded = jnp.concatenate([lesser, jnp.zeros_like(lesser)], axis=0)
    straight = jnp.zeros_like(lesser)
    crossed = jnp.zeros_like(lesser)
    for k in range(energy_count):
        window = padded[k:k + energy_count]
        straight = straight + window * greater[k:k + 1]
        crossed = crossed + window * swapped[k:k + 1]
    joined = jnp.concatenate(
        [straight[:, :width] - straight[:, width:], crossed[:, :width] + crossed[:, width:]], axis=1
    )
    out_ref[:, 0, :] = (joined * factor).astype(out_ref.dtype)


def lag_sums(by_element):
    energy_count, _, joined = by_element.shape
    width = joined // 4
    kernel = functools.partial(_lag_kernel, width=width, factor=1.0 / math.sqrt(energy_count))
    return pl.pallas_call(
        kernel,
        out_shape=jax.ShapeDtypeStruct((energy_count, 1, 2 * width), jnp.bfloat16),
    )(by_element)


def _screen_kernel(polar_ref, place_ref, screen_ref, out_ref, *, rows, cols):
    def nt(a, b):
        return lax.dot_general(a, b, (((1,), (1,)), ((), ())), preferred_element_type=jnp.float32)

    def nn(a, b):
        return jnp.dot(a, b, preferred_element_type=jnp.float32)

    row_hit, col_hit = _place_hits(place_ref, rows, cols)
    col_hit = col_hit.astype(jnp.bfloat16)
    polar = polar_ref[...].astype(jnp.float32)
    dense = []
    for part in range(2):
        spread = jnp.where(row_hit, polar[part:part + 1, :], 0.0).astype(jnp.bfloat16)
        dense.append(nt(spread, col_hit).astype(jnp.bfloat16))
    dense_real, dense_imag = dense
    screen_real = screen_ref[0]
    screen_imag = screen_ref[1]
    inner_real = (nt(dense_real, screen_real) + nt(dense_imag, screen_imag)).astype(jnp.bfloat16)
    inner_imag = (nt(dense_imag, screen_real) - nt(dense_real, screen_imag)).astype(jnp.bfloat16)
    near_real = screen_real[:, :rows]
    near_imag = screen_imag[:, :rows]
    side_real = screen_real[:, rows:]
    side_imag = screen_imag[:, rows:]
    edge_real = dense_real[:, rows:]
    edge_imag = dense_imag[:, rows:]
    across_real = (nn(near_real, edge_real) - nn(near_imag, edge_imag)).astype(jnp.bfloat16)
    across_imag = (nn(near_real, edge_imag) + nn(near_imag, edge_real)).astype(jnp.bfloat16)
    first_real = nn(near_real, inner_real) - nn(near_imag, inner_imag)
    first_imag = nn(near_real, inner_imag) + nn(near_imag, inner_real)
    second_real = nt(side_real, across_real) + nt(side_imag, across_imag)
    second_imag = nt(side_imag, across_real) - nt(side_real, across_imag)
    out_ref[0] = first_real + second_real
    out_ref[1] = first_imag + second_imag


def screen(polar_row, pattern_row, screen_block):
    rows = screen_block.shape[1]
    cols = screen_block.shape[2]
    kernel = functools.partial(_screen_kernel, rows=rows, cols=cols)
    return pl.pallas_call(
        kernel,
        out_shape=jax.ShapeDtypeStruct((2, rows, rows), jnp.float32),
    )(polar_row, pattern_row, screen_block)


def split_exact(value):
    high = lax.reduce_precision(value, exponent_bits=8, mantissa_bits=7)
    rest = value - high
    middle = lax.reduce_precision(rest, exponent_bits=8, mantissa_bits=7)
    low = rest - middle
    return jnp.stack([high, middle, low], axis=0).astype(jnp.bfloat16)


def body(green_slab, self_energy, pattern, screened):
    own_rate = self_energy[0, 0]
    block_order = own_rate.shape[-1]
    previous_rate = passed_along(own_rate, "domain", 1)
    edge_block = green_slab[0, 0, :, 0:2, :EDGE, :]
    bundle = jnp.concatenate(
        [edge_block.reshape(-1, block_order), split_exact(own_rate).reshape(-1, block_order)], axis=0
    )
    bundle = passed_along(bundle, "domain", -1)
    values = element_values(green_slab[0, 0], bundle, previous_rate, own_rate, pattern, EDGE)
    chunks = lax.axis_size("energy")
    values = values.reshape(4, chunks, -1).transpose(1, 0, 2).reshape(chunks, 1, -1)
    by_element = lax.all_to_all(values, "energy", split_axis=0, concat_axis=0, tiled=True)
    polarization = lag_sums(by_element)
    per_energy = lax.all_to_all(polarization, "energy", split_axis=0, concat_axis=0, tiled=True)
    per_energy = per_energy.reshape(chunks, 2, -1).transpose(1, 0, 2).reshape(2, -1)
    result = screen(per_energy, pattern, screened[0, 0])
    return result[None, None]


def solution(mesh):
    placed = (
        P("energy", "domain", None, None, None, None),
        P("energy", "domain", None, None, None),
        P("domain", None),
        P("energy", "domain", None, None, None),
    )
    return jax.shard_map(
        body,
        mesh=mesh,
        in_specs=placed,
        out_specs=P("energy", "domain", None, None, None),
        check_vma=False,
    )
```

```python
import functools
import math

import jax
import jax.numpy as jnp
from jax import lax
from jax.experimental import pallas as pl
from jax.experimental.pallas import tpu as pltpu
from jax.sharding import PartitionSpec as P

EDGE = 16


def passed_along(x, axis, by):
    length = lax.axis_size(axis)
    pairs = [(i, i + by) for i in range(length) if 0 <= i + by < length]
    return lax.ppermute(x, axis, pairs)


def _weigh(real_f, imag_f, rate_ref, block, factor):
    pieces = []
    for q in range(2):
        rate_real = rate_ref[block, q, 0:1, :]
        rate_imag = rate_ref[block, q, 1:2, :]
        pieces.append(((real_f * rate_real - imag_f * rate_imag) * factor).astype(jnp.bfloat16))
        pieces.append(((real_f * rate_imag + imag_f * rate_real) * factor).astype(jnp.bfloat16))
    return jnp.concatenate(pieces, axis=0)


def _adjoint_parts(prod, q, rows, start, width):
    wr = prod[2 * q * rows:(2 * q + 1) * rows]
    wi = prod[(2 * q + 1) * rows:(2 * q + 2) * rows]
    real = wr[:, start:start + width] + wi[:, start + width:start + 2 * width]
    imag = wi[:, start:start + width] - wr[:, start + width:start + 2 * width]
    return real, imag


def _place_hits(pattern_ref, rows, cols):
    count = pattern_ref.shape[1]
    position = pattern_ref[...].astype(jnp.float32)
    row = jnp.floor((position + 0.5) * (1.0 / cols))
    col = position - row * cols
    row_hit = lax.broadcasted_iota(jnp.int32, (rows, count), 0).astype(jnp.float32) == row
    col_hit = lax.broadcasted_iota(jnp.int32, (cols, count), 0).astype(jnp.float32) == col
    return row_hit, col_hit


def _nt(a, b):
    return lax.dot_general(a, b, (((1,), (1,)), ((), ())), preferred_element_type=jnp.float32)


def _early_kernel(slab_ref, previous_ref, own_ref, near_ref, held_ref, rate_scr, *, factor, rows):
    step = pl.program_id(0)

    @pl.when(step == 0)
    def _():
        near_ref[...] = jnp.zeros_like(near_ref)
        rate_scr[0] = previous_ref[...]

    @pl.when(step > 0)
    def _():
        rate_scr[0] = own_ref[...]

    slab_real = slab_ref[0, 0]
    slab_imag = slab_ref[1, 0]
    left = _weigh(slab_real.astype(jnp.float32), slab_imag.astype(jnp.float32), rate_scr, 0, factor)
    prod = _nt(left, jnp.concatenate([slab_real, slab_imag], axis=0))
    for q in range(2):
        real, imag = _adjoint_parts(prod, q, rows, 0, rows)
        near_ref[q, 0] += real
        near_ref[q, 1] += imag

    @pl.when(step == pl.num_programs(0) - 1)
    def _():
        held_ref[...] = left


def _late_kernel(slab_ref, bundle_ref, near_ref, held_ref, place_ref, out_ref, rate_scr,
                 *, factor, rows, edge):
    cols = rows + edge
    edge_rows = 4 * edge
    for piece_q in range(2):
        for part in range(2):
            k = piece_q * 2 + part
            pieces = [bundle_ref[edge_rows + 4 * t + k:edge_rows + 4 * t + k + 1, :].astype(jnp.float32)
                      for t in range(3)]
            rate_scr[0, piece_q, part:part + 1, :] = (pieces[0] + pieces[1]) + pieces[2]
    slab_real = slab_ref[0, 0]
    slab_imag = slab_ref[1, 0]
    left = _weigh(slab_real.astype(jnp.float32), slab_imag.astype(jnp.float32), rate_scr, 0, factor)

    def edge_of(part, block):
        start = part * 2 * edge + block * edge
        return bundle_ref[start:start + edge, :]

    far = _nt(left, jnp.concatenate([slab_real, slab_imag, edge_of(0, 1), edge_of(1, 1)], axis=0))
    own = _nt(held_ref[...], jnp.concatenate([edge_of(0, 0), edge_of(1, 0)], axis=0))
    joined = []
    for q in range(2):
        near_real, near_imag = _adjoint_parts(far, q, rows, 0, rows)
        far_real, far_imag = _adjoint_parts(far, q, rows, 2 * rows, edge)
        own_real, own_imag = _adjoint_parts(own, q, rows, 0, edge)
        joined.append(jnp.concatenate([near_ref[q, 0] + near_real, far_real + own_real], axis=1))
        joined.append(jnp.concatenate([near_ref[q, 1] + near_imag, far_imag + own_imag], axis=1))
    joined = jnp.concatenate(joined, axis=0).astype(jnp.bfloat16)
    row_hit, col_hit = _place_hits(place_ref, rows, cols)
    by_column = jnp.dot(joined, col_hit.astype(jnp.bfloat16), preferred_element_type=jnp.float32)
    for k in range(4):
        picked = jnp.where(row_hit, by_column[k * rows:(k + 1) * rows], 0.0)
        out_ref[k:k + 1, :] = jnp.sum(picked, axis=0, keepdims=True).astype(out_ref.dtype)


def element_values(own_slab, bundle, previous_rate, own_rate, pattern_row, edge):
    _, blocks, rows, block_order = own_slab.shape
    count = pattern_row.shape[1]
    factor = 1.0 / math.sqrt(3.0 * block_order)
    near, held = pl.pallas_call(
        functools.partial(_early_kernel, factor=factor, rows=rows),
        grid=(blocks - 1,),
        in_specs=[
            pl.BlockSpec((2, 1, rows, block_order), lambda j: (0, j, 0, 0)),
            pl.BlockSpec((2, 2, block_order), lambda j: (0, 0, 0)),
            pl.BlockSpec((2, 2, block_order), lambda j: (0, 0, 0)),
        ],
        out_specs=[
            pl.BlockSpec((2, 2, rows, rows), lambda j: (0, 0, 0, 0)),
            pl.BlockSpec((4 * rows, block_order), lambda j: (0, 0)),
        ],
        scratch_shapes=[pltpu.VMEM((1, 2, 2, block_order), jnp.float32)],
        out_shape=[
            jax.ShapeDtypeStruct((2, 2, rows, rows), jnp.float32),
            jax.ShapeDtypeStruct((4 * rows, block_order), jnp.bfloat16),
        ],
    )(own_slab, previous_rate, own_rate)
    last = blocks - 1
    return pl.pallas_call(
        functools.partial(_late_kernel, factor=factor, rows=rows, edge=edge),
        grid=(1,),
        in_specs=[
            pl.BlockSpec((2, 1, rows, block_order), lambda j: (0, last, 0, 0)),
            pl.BlockSpec(bundle.shape, lambda j: (0, 0)),
            pl.BlockSpec((2, 2, rows, rows), lambda j: (0, 0, 0, 0)),
            pl.BlockSpec((4 * rows, block_order), lambda j: (0, 0)),
            pl.BlockSpec((1, count), lambda j: (0, 0)),
        ],
        out_specs=pl.BlockSpec((4, count), lambda j: (0, 0)),
        out_shape=jax.ShapeDtypeStruct((4, count), jnp.bfloat16),
        scratch_shapes=[pltpu.VMEM((1, 2, 2, block_order), jnp.float32)],
    )(own_slab, bundle, near, held, pattern_row)


def _lag_kernel(in_ref, out_ref, *, width, factor):
    values = in_ref[:, 0, :].astype(jnp.float32)
    energy_count = values.shape[0]
    lesser = values[:, 0:2 * width]
    greater = values[:, 2 * width:4 * width]
    swapped = jnp.concatenate([greater[:, width:], greater[:, :width]], axis=1)
    padded = jnp.concatenate([lesser, jnp.zeros_like(lesser)], axis=0)
    straight = jnp.zeros_like(lesser)
    crossed = jnp.zeros_like(lesser)
    for k in range(energy_count):
        window = padded[k:k + energy_count]
        straight = straight + window * greater[k:k + 1]
        crossed = crossed + window * swapped[k:k + 1]
    joined = jnp.concatenate(
        [straight[:, :width] - straight[:, width:], crossed[:, :width] + crossed[:, width:]], axis=1
    )
    out_ref[:, 0, :] = (joined * factor).astype(out_ref.dtype)


def lag_sums(by_element):
    energy_count, _, joined = by_element.shape
    width = joined // 4
    kernel = functools.partial(_lag_kernel, width=width, factor=1.0 / math.sqrt(energy_count))
    return pl.pallas_call(
        kernel,
        out_shape=jax.ShapeDtypeStruct((energy_count, 1, 2 * width), jnp.bfloat16),
    )(by_element)


def _screen_kernel(polar_ref, place_ref, screen_ref, out_ref, polar_scr, *, rows, cols):
    def nt(a, b):
        return lax.dot_general(a, b, (((1,), (1,)), ((), ())), preferred_element_type=jnp.float32)

    def nn(a, b):
        return jnp.dot(a, b, preferred_element_type=jnp.float32)

    row_hit, col_hit = _place_hits(place_ref, rows, cols)
    col_hit = col_hit.astype(jnp.bfloat16)
    chunks = polar_ref.shape[0]
    width = polar_ref.shape[2] // 2
    for chunk in range(chunks):
        piece = polar_ref[chunk]
        for part in range(2):
            polar_scr[part:part + 1, chunk * width:(chunk + 1) * width] = piece[:, part * width:(part + 1) * width]
    polar = polar_scr[...].astype(jnp.float32)
    dense = []
    for part in range(2):
        spread = jnp.where(row_hit, polar[part:part + 1, :], 0.0).astype(jnp.bfloat16)
        dense.append(nt(spread, col_hit).astype(jnp.bfloat16))
    dense_real, dense_imag = dense
    screen_real = screen_ref[0]
    screen_imag = screen_ref[1]
    inner_real = (nt(dense_real, screen_real) + nt(dense_imag, screen_imag)).astype(jnp.bfloat16)
    inner_imag = (nt(dense_imag, screen_real) - nt(dense_real, screen_imag)).astype(jnp.bfloat16)
    near_real = screen_real[:, :rows]
    near_imag = screen_imag[:, :rows]
    side_real = screen_real[:, rows:]
    side_imag = screen_imag[:, rows:]
    edge_real = dense_real[:, rows:]
    edge_imag = dense_imag[:, rows:]
    across_real = (nn(near_real, edge_real) - nn(near_imag, edge_imag)).astype(jnp.bfloat16)
    across_imag = (nn(near_real, edge_imag) + nn(near_imag, edge_real)).astype(jnp.bfloat16)
    first_real = nn(near_real, inner_real) - nn(near_imag, inner_imag)
    first_imag = nn(near_real, inner_imag) + nn(near_imag, inner_real)
    second_real = nt(side_real, across_real) + nt(side_imag, across_imag)
    second_imag = nt(side_imag, across_real) - nt(side_real, across_imag)
    out_ref[0] = first_real + second_real
    out_ref[1] = first_imag + second_imag


def screen(polar_row, pattern_row, screen_block):
    rows = screen_block.shape[1]
    cols = screen_block.shape[2]
    kernel = functools.partial(_screen_kernel, rows=rows, cols=cols)
    return pl.pallas_call(
        kernel,
        out_shape=jax.ShapeDtypeStruct((2, rows, rows), jnp.float32),
        scratch_shapes=[pltpu.VMEM((2, pattern_row.shape[1]), polar_row.dtype)],
    )(polar_row, pattern_row, screen_block)


def split_exact(value):
    high = lax.reduce_precision(value, exponent_bits=8, mantissa_bits=7)
    rest = value - high
    middle = lax.reduce_precision(rest, exponent_bits=8, mantissa_bits=7)
    low = rest - middle
    return jnp.stack([high, middle, low], axis=0).astype(jnp.bfloat16)


def body(green_slab, self_energy, pattern, screened):
    own_rate = self_energy[0, 0]
    block_order = own_rate.shape[-1]
    previous_rate = passed_along(own_rate, "domain", 1)
    edge_block = green_slab[0, 0, :, 0:2, :EDGE, :]
    bundle = jnp.concatenate(
        [edge_block.reshape(-1, block_order), split_exact(own_rate).reshape(-1, block_order)], axis=0
    )
    bundle = passed_along(bundle, "domain", -1)
    values = element_values(green_slab[0, 0], bundle, previous_rate, own_rate, pattern, EDGE)
    chunks = lax.axis_size("energy")
    values = values.reshape(4, chunks, -1).transpose(1, 0, 2).reshape(chunks, 1, -1)
    by_element = lax.all_to_all(values, "energy", split_axis=0, concat_axis=0, tiled=True)
    polarization = lag_sums(by_element)
    per_energy = lax.all_to_all(polarization, "energy", split_axis=0, concat_axis=0, tiled=True)
    result = screen(per_energy, pattern, screened[0, 0])
    return result[None, None]


def solution(mesh):
    placed = (
        P("energy", "domain", None, None, None, None),
        P("energy", "domain", None, None, None),
        P("domain", None),
        P("energy", "domain", None, None, None),
    )
    return jax.shard_map(
        body,
        mesh=mesh,
        in_specs=placed,
        out_specs=P("energy", "domain", None, None, None),
        check_vma=False,
    )
```

```python
import functools
import math

import jax
import jax.numpy as jnp
from jax import lax
from jax.experimental import pallas as pl
from jax.experimental.pallas import tpu as pltpu
from jax.sharding import PartitionSpec as P

EDGE = 16


def passed_along(x, axis, by):
    length = lax.axis_size(axis)
    pairs = [(i, i + by) for i in range(length) if 0 <= i + by < length]
    return lax.ppermute(x, axis, pairs)


def _weigh(real_f, imag_f, rate_ref, block, factor):
    pieces = []
    for q in range(2):
        rate_real = rate_ref[block, q, 0:1, :]
        rate_imag = rate_ref[block, q, 1:2, :]
        pieces.append(((real_f * rate_real - imag_f * rate_imag) * factor).astype(jnp.bfloat16))
        pieces.append(((real_f * rate_imag + imag_f * rate_real) * factor).astype(jnp.bfloat16))
    return jnp.concatenate(pieces, axis=0)


def _adjoint_parts(prod, q, rows, start, width):
    wr = prod[2 * q * rows:(2 * q + 1) * rows]
    wi = prod[(2 * q + 1) * rows:(2 * q + 2) * rows]
    real = wr[:, start:start + width] + wi[:, start + width:start + 2 * width]
    imag = wi[:, start:start + width] - wr[:, start + width:start + 2 * width]
    return real, imag


def _place_hits(pattern_ref, rows, cols):
    count = pattern_ref.shape[1]
    position = pattern_ref[...].astype(jnp.float32)
    row = jnp.floor((position + 0.5) * (1.0 / cols))
    col = position - row * cols
    row_hit = lax.broadcasted_iota(jnp.int32, (rows, count), 0).astype(jnp.float32) == row
    col_hit = lax.broadcasted_iota(jnp.int32, (cols, count), 0).astype(jnp.float32) == col
    return row_hit, col_hit


def _nt(a, b):
    return lax.dot_general(a, b, (((1,), (1,)), ((), ())), preferred_element_type=jnp.float32)


def _early_kernel(slab_ref, previous_ref, own_ref, near_ref, held_ref, rate_scr, *, factor, rows):
    step = pl.program_id(0)

    @pl.when(step == 0)
    def _():
        near_ref[...] = jnp.zeros_like(near_ref)
        rate_scr[0] = previous_ref[...]

    @pl.when(step > 0)
    def _():
        rate_scr[0] = own_ref[...]

    slab_real = slab_ref[0, 0]
    slab_imag = slab_ref[1, 0]
    left = _weigh(slab_real.astype(jnp.float32), slab_imag.astype(jnp.float32), rate_scr, 0, factor)
    prod = _nt(left, jnp.concatenate([slab_real, slab_imag], axis=0))
    for q in range(2):
        real, imag = _adjoint_parts(prod, q, rows, 0, rows)
        near_ref[q, 0] += real
        near_ref[q, 1] += imag

    @pl.when(step == pl.num_programs(0) - 1)
    def _():
        held_ref[...] = left


def _late_kernel(slab_ref, bundle_ref, near_ref, held_ref, place_ref, out_ref, rate_scr,
                 *, factor, rows, edge):
    cols = rows + edge
    edge_rows = 4 * edge
    for piece_q in range(2):
        for part in range(2):
            k = piece_q * 2 + part
            pieces = [bundle_ref[edge_rows + 4 * t + k:edge_rows + 4 * t + k + 1, :].astype(jnp.float32)
                      for t in range(3)]
            rate_scr[0, piece_q, part:part + 1, :] = (pieces[0] + pieces[1]) + pieces[2]
    slab_real = slab_ref[0, 0]
    slab_imag = slab_ref[1, 0]
    left = _weigh(slab_real.astype(jnp.float32), slab_imag.astype(jnp.float32), rate_scr, 0, factor)

    def edge_of(part, block):
        start = part * 2 * edge + block * edge
        return bundle_ref[start:start + edge, :]

    far = _nt(left, jnp.concatenate([slab_real, slab_imag, edge_of(0, 1), edge_of(1, 1)], axis=0))
    own = _nt(held_ref[...], jnp.concatenate([edge_of(0, 0), edge_of(1, 0)], axis=0))
    joined = []
    for q in range(2):
        near_real, near_imag = _adjoint_parts(far, q, rows, 0, rows)
        far_real, far_imag = _adjoint_parts(far, q, rows, 2 * rows, edge)
        own_real, own_imag = _adjoint_parts(own, q, rows, 0, edge)
        joined.append(jnp.concatenate([near_ref[q, 0] + near_real, far_real + own_real], axis=1))
        joined.append(jnp.concatenate([near_ref[q, 1] + near_imag, far_imag + own_imag], axis=1))
    joined = jnp.concatenate(joined, axis=0).astype(jnp.bfloat16)
    row_hit, col_hit = _place_hits(place_ref, rows, cols)
    by_column = jnp.dot(joined, col_hit.astype(jnp.bfloat16), preferred_element_type=jnp.float32)
    chunks = out_ref.shape[0]
    width = out_ref.shape[2] // 4
    for k in range(4):
        picked = jnp.where(row_hit, by_column[k * rows:(k + 1) * rows], 0.0)
        picked = jnp.sum(picked, axis=0, keepdims=True).astype(out_ref.dtype)
        for chunk in range(chunks):
            out_ref[chunk, :, k * width:(k + 1) * width] = picked[:, chunk * width:(chunk + 1) * width]


def element_values(own_slab, bundle, previous_rate, own_rate, pattern_row, edge, chunks):
    _, blocks, rows, block_order = own_slab.shape
    count = pattern_row.shape[1]
    factor = 1.0 / math.sqrt(3.0 * block_order)
    near, held = pl.pallas_call(
        functools.partial(_early_kernel, factor=factor, rows=rows),
        grid=(blocks - 1,),
        in_specs=[
            pl.BlockSpec((2, 1, rows, block_order), lambda j: (0, j, 0, 0)),
            pl.BlockSpec((2, 2, block_order), lambda j: (0, 0, 0)),
            pl.BlockSpec((2, 2, block_order), lambda j: (0, 0, 0)),
        ],
        out_specs=[
            pl.BlockSpec((2, 2, rows, rows), lambda j: (0, 0, 0, 0)),
            pl.BlockSpec((4 * rows, block_order), lambda j: (0, 0)),
        ],
        scratch_shapes=[pltpu.VMEM((1, 2, 2, block_order), jnp.float32)],
        out_shape=[
            jax.ShapeDtypeStruct((2, 2, rows, rows), jnp.float32),
            jax.ShapeDtypeStruct((4 * rows, block_order), jnp.bfloat16),
        ],
    )(own_slab, previous_rate, own_rate)
    last = blocks - 1
    return pl.pallas_call(
        functools.partial(_late_kernel, factor=factor, rows=rows, edge=edge),
        grid=(1,),
        in_specs=[
            pl.BlockSpec((2, 1, rows, block_order), lambda j: (0, last, 0, 0)),
            pl.BlockSpec(bundle.shape, lambda j: (0, 0)),
            pl.BlockSpec((2, 2, rows, rows), lambda j: (0, 0, 0, 0)),
            pl.BlockSpec((4 * rows, block_order), lambda j: (0, 0)),
            pl.BlockSpec((1, count), lambda j: (0, 0)),
        ],
        out_specs=pl.BlockSpec((chunks, 1, 4 * count // chunks), lambda j: (0, 0, 0)),
        out_shape=jax.ShapeDtypeStruct((chunks, 1, 4 * count // chunks), jnp.bfloat16),
        scratch_shapes=[pltpu.VMEM((1, 2, 2, block_order), jnp.float32)],
    )(own_slab, bundle, near, held, pattern_row)


def _lag_kernel(in_ref, out_ref, *, width, factor):
    values = in_ref[:, 0, :].astype(jnp.float32)
    energy_count = values.shape[0]
    lesser = values[:, 0:2 * width]
    greater = values[:, 2 * width:4 * width]
    swapped = jnp.concatenate([greater[:, width:], greater[:, :width]], axis=1)
    padded = jnp.concatenate([lesser, jnp.zeros_like(lesser)], axis=0)
    straight = jnp.zeros_like(lesser)
    crossed = jnp.zeros_like(lesser)
    for k in range(energy_count):
        window = padded[k:k + energy_count]
        straight = straight + window * greater[k:k + 1]
        crossed = crossed + window * swapped[k:k + 1]
    joined = jnp.concatenate(
        [straight[:, :width] - straight[:, width:], crossed[:, :width] + crossed[:, width:]], axis=1
    )
    out_ref[:, 0, :] = (joined * factor).astype(out_ref.dtype)


def lag_sums(by_element):
    energy_count, _, joined = by_element.shape
    width = joined // 4
    kernel = functools.partial(_lag_kernel, width=width, factor=1.0 / math.sqrt(energy_count))
    return pl.pallas_call(
        kernel,
        out_shape=jax.ShapeDtypeStruct((energy_count, 1, 2 * width), jnp.bfloat16),
    )(by_element)


def _screen_kernel(polar_ref, place_ref, screen_ref, out_ref, polar_scr, *, rows, cols):
    def nt(a, b):
        return lax.dot_general(a, b, (((1,), (1,)), ((), ())), preferred_element_type=jnp.float32)

    def nn(a, b):
        return jnp.dot(a, b, preferred_element_type=jnp.float32)

    row_hit, col_hit = _place_hits(place_ref, rows, cols)
    col_hit = col_hit.astype(jnp.bfloat16)
    chunks = polar_ref.shape[0]
    width = polar_ref.shape[2] // 2
    for chunk in range(chunks):
        piece = polar_ref[chunk]
        for part in range(2):
            polar_scr[part:part + 1, chunk * width:(chunk + 1) * width] = piece[:, part * width:(part + 1) * width]
    polar = polar_scr[...].astype(jnp.float32)
    dense = []
    for part in range(2):
        spread = jnp.where(row_hit, polar[part:part + 1, :], 0.0).astype(jnp.bfloat16)
        dense.append(nt(spread, col_hit).astype(jnp.bfloat16))
    dense_real, dense_imag = dense
    screen_real = screen_ref[0]
    screen_imag = screen_ref[1]
    inner_real = (nt(dense_real, screen_real) + nt(dense_imag, screen_imag)).astype(jnp.bfloat16)
    inner_imag = (nt(dense_imag, screen_real) - nt(dense_real, screen_imag)).astype(jnp.bfloat16)
    near_real = screen_real[:, :rows]
    near_imag = screen_imag[:, :rows]
    side_real = screen_real[:, rows:]
    side_imag = screen_imag[:, rows:]
    edge_real = dense_real[:, rows:]
    edge_imag = dense_imag[:, rows:]
    across_real = (nn(near_real, edge_real) - nn(near_imag, edge_imag)).astype(jnp.bfloat16)
    across_imag = (nn(near_real, edge_imag) + nn(near_imag, edge_real)).astype(jnp.bfloat16)
    first_real = nn(near_real, inner_real) - nn(near_imag, inner_imag)
    first_imag = nn(near_real, inner_imag) + nn(near_imag, inner_real)
    second_real = nt(side_real, across_real) + nt(side_imag, across_imag)
    second_imag = nt(side_imag, across_real) - nt(side_real, across_imag)
    out_ref[0] = first_real + second_real
    out_ref[1] = first_imag + second_imag


def screen(polar_row, pattern_row, screen_block):
    rows = screen_block.shape[1]
    cols = screen_block.shape[2]
    kernel = functools.partial(_screen_kernel, rows=rows, cols=cols)
    return pl.pallas_call(
        kernel,
        out_shape=jax.ShapeDtypeStruct((2, rows, rows), jnp.float32),
        scratch_shapes=[pltpu.VMEM((2, pattern_row.shape[1]), polar_row.dtype)],
    )(polar_row, pattern_row, screen_block)


def split_exact(value):
    high = lax.reduce_precision(value, exponent_bits=8, mantissa_bits=7)
    rest = value - high
    middle = lax.reduce_precision(rest, exponent_bits=8, mantissa_bits=7)
    low = rest - middle
    return jnp.stack([high, middle, low], axis=0).astype(jnp.bfloat16)


def body(green_slab, self_energy, pattern, screened):
    own_rate = self_energy[0, 0]
    block_order = own_rate.shape[-1]
    previous_rate = passed_along(own_rate, "domain", 1)
    edge_block = green_slab[0, 0, :, 0:2, :EDGE, :]
    bundle = jnp.concatenate(
        [edge_block.reshape(-1, block_order), split_exact(own_rate).reshape(-1, block_order)], axis=0
    )
    bundle = passed_along(bundle, "domain", -1)
    chunks = lax.axis_size("energy")
    values = element_values(green_slab[0, 0], bundle, previous_rate, own_rate, pattern, EDGE, chunks)
    by_element = lax.all_to_all(values, "energy", split_axis=0, concat_axis=0, tiled=True)
    polarization = lag_sums(by_element)
    per_energy = lax.all_to_all(polarization, "energy", split_axis=0, concat_axis=0, tiled=True)
    result = screen(per_energy, pattern, screened[0, 0])
    return result[None, None]


def solution(mesh):
    placed = (
        P("energy", "domain", None, None, None, None),
        P("energy", "domain", None, None, None),
        P("domain", None),
        P("energy", "domain", None, None, None),
    )
    return jax.shard_map(
        body,
        mesh=mesh,
        in_specs=placed,
        out_specs=P("energy", "domain", None, None, None),
        check_vma=False,
    )
```

```python
import functools
import math

import jax
import jax.numpy as jnp
from jax import lax
from jax.experimental import pallas as pl
from jax.experimental.pallas import tpu as pltpu
from jax.sharding import PartitionSpec as P

EDGE = 16


def passed_along(x, axis, by):
    length = lax.axis_size(axis)
    pairs = [(i, i + by) for i in range(length) if 0 <= i + by < length]
    return lax.ppermute(x, axis, pairs)


def _weigh(real_f, imag_f, rate_ref, block, factor):
    pieces = []
    for q in range(2):
        rate_real = rate_ref[block, q, 0:1, :]
        rate_imag = rate_ref[block, q, 1:2, :]
        pieces.append(((real_f * rate_real - imag_f * rate_imag) * factor).astype(jnp.bfloat16))
        pieces.append(((real_f * rate_imag + imag_f * rate_real) * factor).astype(jnp.bfloat16))
    return jnp.concatenate(pieces, axis=0)


def _adjoint_parts(prod, q, rows, start, width):
    wr = prod[2 * q * rows:(2 * q + 1) * rows]
    wi = prod[(2 * q + 1) * rows:(2 * q + 2) * rows]
    real = wr[:, start:start + width] + wi[:, start + width:start + 2 * width]
    imag = wi[:, start:start + width] - wr[:, start + width:start + 2 * width]
    return real, imag


def _place_hits(pattern_ref, rows, cols):
    count = pattern_ref.shape[1]
    position = pattern_ref[...].astype(jnp.float32)
    row = jnp.floor((position + 0.5) * (1.0 / cols))
    col = position - row * cols
    row_hit = lax.broadcasted_iota(jnp.int32, (rows, count), 0).astype(jnp.float32) == row
    col_hit = lax.broadcasted_iota(jnp.int32, (cols, count), 0).astype(jnp.float32) == col
    return row_hit, col_hit


def _nt(a, b):
    return lax.dot_general(a, b, (((1,), (1,)), ((), ())), preferred_element_type=jnp.float32)


def _early_kernel(slab_ref, previous_ref, own_ref, near_ref, held_ref, rate_scr, *, factor, rows):
    step = pl.program_id(0)

    @pl.when(step == 0)
    def _():
        near_ref[...] = jnp.zeros_like(near_ref)
        rate_scr[0] = previous_ref[...]

    @pl.when(step > 0)
    def _():
        rate_scr[0] = own_ref[...]

    slab_real = slab_ref[0, 0]
    slab_imag = slab_ref[1, 0]
    left = _weigh(slab_real.astype(jnp.float32), slab_imag.astype(jnp.float32), rate_scr, 0, factor)
    prod = _nt(left, jnp.concatenate([slab_real, slab_imag], axis=0))
    for q in range(2):
        real, imag = _adjoint_parts(prod, q, rows, 0, rows)
        near_ref[q, 0] += real
        near_ref[q, 1] += imag

    @pl.when(step == pl.num_programs(0) - 1)
    def _():
        held_ref[...] = left


def _late_kernel(slab_ref, bundle_ref, near_ref, held_ref, place_ref, out_ref, rate_scr,
                 *, factor, rows, edge):
    cols = rows + edge
    edge_rows = 4 * edge
    for piece_q in range(2):
        for part in range(2):
            k = piece_q * 2 + part
            pieces = [bundle_ref[edge_rows + 4 * t + k:edge_rows + 4 * t + k + 1, :].astype(jnp.float32)
                      for t in range(3)]
            rate_scr[0, piece_q, part:part + 1, :] = (pieces[0] + pieces[1]) + pieces[2]
    slab_real = slab_ref[0, 0]
    slab_imag = slab_ref[1, 0]
    left = _weigh(slab_real.astype(jnp.float32), slab_imag.astype(jnp.float32), rate_scr, 0, factor)

    def edge_of(part, block):
        start = part * 2 * edge + block * edge
        return bundle_ref[start:start + edge, :]

    far = _nt(left, jnp.concatenate([slab_real, slab_imag, edge_of(0, 1), edge_of(1, 1)], axis=0))
    own = _nt(held_ref[...], jnp.concatenate([edge_of(0, 0), edge_of(1, 0)], axis=0))
    joined = []
    for q in range(2):
        near_real, near_imag = _adjoint_parts(far, q, rows, 0, rows)
        far_real, far_imag = _adjoint_parts(far, q, rows, 2 * rows, edge)
        own_real, own_imag = _adjoint_parts(own, q, rows, 0, edge)
        joined.append(jnp.concatenate([near_ref[q, 0] + near_real, far_real + own_real], axis=1))
        joined.append(jnp.concatenate([near_ref[q, 1] + near_imag, far_imag + own_imag], axis=1))
    joined = jnp.concatenate(joined, axis=0).astype(jnp.bfloat16)
    row_hit, col_hit = _place_hits(place_ref, rows, cols)
    by_column = jnp.dot(joined, col_hit.astype(jnp.bfloat16), preferred_element_type=jnp.float32)
    chunks = out_ref.shape[0]
    width = out_ref.shape[2] // 4
    for k in range(4):
        picked = jnp.where(row_hit, by_column[k * rows:(k + 1) * rows], 0.0)
        picked = jnp.sum(picked, axis=0, keepdims=True).astype(out_ref.dtype)
        for chunk in range(chunks):
            out_ref[chunk, :, k * width:(k + 1) * width] = picked[:, chunk * width:(chunk + 1) * width]


def element_values(own_slab, bundle, previous_rate, own_rate, pattern_row, edge, chunks):
    _, blocks, rows, block_order = own_slab.shape
    count = pattern_row.shape[1]
    factor = 1.0 / math.sqrt(3.0 * block_order)
    near, held = pl.pallas_call(
        functools.partial(_early_kernel, factor=factor, rows=rows),
        grid=(blocks - 1,),
        in_specs=[
            pl.BlockSpec((2, 1, rows, block_order), lambda j: (0, j, 0, 0)),
            pl.BlockSpec((2, 2, block_order), lambda j: (0, 0, 0)),
            pl.BlockSpec((2, 2, block_order), lambda j: (0, 0, 0)),
        ],
        out_specs=[
            pl.BlockSpec((2, 2, rows, rows), lambda j: (0, 0, 0, 0)),
            pl.BlockSpec((4 * rows, block_order), lambda j: (0, 0)),
        ],
        scratch_shapes=[pltpu.VMEM((1, 2, 2, block_order), jnp.float32)],
        out_shape=[
            jax.ShapeDtypeStruct((2, 2, rows, rows), jnp.float32),
            jax.ShapeDtypeStruct((4 * rows, block_order), jnp.bfloat16),
        ],
    )(own_slab, previous_rate, own_rate)
    last = blocks - 1
    return pl.pallas_call(
        functools.partial(_late_kernel, factor=factor, rows=rows, edge=edge),
        grid=(1,),
        in_specs=[
            pl.BlockSpec((2, 1, rows, block_order), lambda j: (0, last, 0, 0)),
            pl.BlockSpec(bundle.shape, lambda j: (0, 0)),
            pl.BlockSpec((2, 2, rows, rows), lambda j: (0, 0, 0, 0)),
            pl.BlockSpec((4 * rows, block_order), lambda j: (0, 0)),
            pl.BlockSpec((1, count), lambda j: (0, 0)),
        ],
        out_specs=pl.BlockSpec((chunks, 1, 4 * count // chunks), lambda j: (0, 0, 0)),
        out_shape=jax.ShapeDtypeStruct((chunks, 1, 4 * count // chunks), jnp.bfloat16),
        scratch_shapes=[pltpu.VMEM((1, 2, 2, block_order), jnp.float32)],
    )(own_slab, bundle, near, held, pattern_row)


def _lag_kernel(in_ref, out_ref, *, width, factor):
    values = in_ref[:, 0, :].astype(jnp.float32)
    energy_count = values.shape[0]
    lesser = values[:, 0:2 * width]
    greater = values[:, 2 * width:4 * width]
    swapped = jnp.concatenate([greater[:, width:], greater[:, :width]], axis=1)
    padded = jnp.concatenate([lesser, jnp.zeros_like(lesser)], axis=0)
    straight = jnp.zeros_like(lesser)
    crossed = jnp.zeros_like(lesser)
    for k in range(energy_count):
        window = padded[k:k + energy_count]
        straight = straight + window * greater[k:k + 1]
        crossed = crossed + window * swapped[k:k + 1]
    joined = jnp.concatenate(
        [straight[:, :width] - straight[:, width:], crossed[:, :width] + crossed[:, width:]], axis=1
    )
    out_ref[:, 0, :] = (joined * factor).astype(out_ref.dtype)


def lag_sums(by_element):
    energy_count, _, joined = by_element.shape
    width = joined // 4
    kernel = functools.partial(_lag_kernel, width=width, factor=1.0 / math.sqrt(energy_count))
    return pl.pallas_call(
        kernel,
        out_shape=jax.ShapeDtypeStruct((energy_count, 1, 2 * width), jnp.bfloat16),
    )(by_element)


def _screen_kernel(polar_ref, place_ref, screen_ref, out_ref, polar_scr, *, rows, cols):
    def nt(a, b):
        return lax.dot_general(a, b, (((1,), (1,)), ((), ())), preferred_element_type=jnp.float32)

    def nn(a, b):
        return jnp.dot(a, b, preferred_element_type=jnp.float32)

    row_hit, col_hit = _place_hits(place_ref, rows, cols)
    col_hit = col_hit.astype(jnp.bfloat16)
    chunks = polar_ref.shape[0]
    width = polar_ref.shape[2] // 2
    for chunk in range(chunks):
        piece = polar_ref[chunk]
        for part in range(2):
            polar_scr[part:part + 1, chunk * width:(chunk + 1) * width] = piece[:, part * width:(part + 1) * width]
    polar = polar_scr[...].astype(jnp.float32)
    spread = jnp.concatenate(
        [jnp.where(row_hit, polar[part:part + 1, :], 0.0) for part in range(2)], axis=0
    ).astype(jnp.bfloat16)
    dense = nt(spread, col_hit).astype(jnp.bfloat16)
    dense_real = dense[:rows]
    dense_imag = dense[rows:]
    screen_real = screen_ref[0]
    screen_imag = screen_ref[1]
    both = nt(dense, jnp.concatenate([screen_real, screen_imag], axis=0))
    inner_real = (both[:rows, :rows] + both[rows:, rows:]).astype(jnp.bfloat16)
    inner_imag = (both[rows:, :rows] - both[:rows, rows:]).astype(jnp.bfloat16)
    near = jnp.concatenate([screen_real[:, :rows], screen_imag[:, :rows]], axis=0)
    edge = cols - rows
    across = nn(near, jnp.concatenate([dense_real[:, rows:], dense_imag[:, rows:]], axis=1))
    across_real = (across[:rows, :edge] - across[rows:, edge:]).astype(jnp.bfloat16)
    across_imag = (across[:rows, edge:] + across[rows:, :edge]).astype(jnp.bfloat16)
    first = nn(near, jnp.concatenate([inner_real, inner_imag], axis=1))
    side = jnp.concatenate([screen_real[:, rows:], screen_imag[:, rows:]], axis=0)
    second = nt(side, jnp.concatenate([across_real, across_imag], axis=0))
    out_ref[0] = (first[:rows, :rows] - first[rows:, rows:]) + (second[:rows, :rows] + second[rows:, rows:])
    out_ref[1] = (first[:rows, rows:] + first[rows:, :rows]) + (second[rows:, :rows] - second[:rows, rows:])


def screen(polar_row, pattern_row, screen_block):
    rows = screen_block.shape[1]
    cols = screen_block.shape[2]
    kernel = functools.partial(_screen_kernel, rows=rows, cols=cols)
    return pl.pallas_call(
        kernel,
        out_shape=jax.ShapeDtypeStruct((2, rows, rows), jnp.float32),
        scratch_shapes=[pltpu.VMEM((2, pattern_row.shape[1]), polar_row.dtype)],
    )(polar_row, pattern_row, screen_block)


def split_exact(value):
    high = lax.reduce_precision(value, exponent_bits=8, mantissa_bits=7)
    rest = value - high
    middle = lax.reduce_precision(rest, exponent_bits=8, mantissa_bits=7)
    low = rest - middle
    return jnp.stack([high, middle, low], axis=0).astype(jnp.bfloat16)


def body(green_slab, self_energy, pattern, screened):
    own_rate = self_energy[0, 0]
    block_order = own_rate.shape[-1]
    previous_rate = passed_along(own_rate, "domain", 1)
    edge_block = green_slab[0, 0, :, 0:2, :EDGE, :]
    bundle = jnp.concatenate(
        [edge_block.reshape(-1, block_order), split_exact(own_rate).reshape(-1, block_order)], axis=0
    )
    bundle = passed_along(bundle, "domain", -1)
    chunks = lax.axis_size("energy")
    values = element_values(green_slab[0, 0], bundle, previous_rate, own_rate, pattern, EDGE, chunks)
    by_element = lax.all_to_all(values, "energy", split_axis=0, concat_axis=0, tiled=True)
    polarization = lag_sums(by_element)
    per_energy = lax.all_to_all(polarization, "energy", split_axis=0, concat_axis=0, tiled=True)
    result = screen(per_energy, pattern, screened[0, 0])
    return result[None, None]


def solution(mesh):
    placed = (
        P("energy", "domain", None, None, None, None),
        P("energy", "domain", None, None, None),
        P("domain", None),
        P("energy", "domain", None, None, None),
    )
    return jax.shard_map(
        body,
        mesh=mesh,
        in_specs=placed,
        out_specs=P("energy", "domain", None, None, None),
        check_vma=False,
    )
```

```python
import functools
import math

import jax
import jax.numpy as jnp
from jax import lax
from jax.experimental import pallas as pl
from jax.experimental.pallas import tpu as pltpu
from jax.sharding import PartitionSpec as P

EDGE = 16


def passed_along(x, axis, by):
    length = lax.axis_size(axis)
    pairs = [(i, i + by) for i in range(length) if 0 <= i + by < length]
    return lax.ppermute(x, axis, pairs)


def _weigh(real_f, imag_f, rate_ref, block, factor):
    pieces = []
    for q in range(2):
        rate_real = rate_ref[block, q, 0:1, :] * factor
        rate_imag = rate_ref[block, q, 1:2, :] * factor
        pieces.append((real_f * rate_real - imag_f * rate_imag).astype(jnp.bfloat16))
        pieces.append((real_f * rate_imag + imag_f * rate_real).astype(jnp.bfloat16))
    return jnp.concatenate(pieces, axis=0)


def _adjoint_parts(prod, q, rows, start, width):
    wr = prod[2 * q * rows:(2 * q + 1) * rows]
    wi = prod[(2 * q + 1) * rows:(2 * q + 2) * rows]
    real = wr[:, start:start + width] + wi[:, start + width:start + 2 * width]
    imag = wi[:, start:start + width] - wr[:, start + width:start + 2 * width]
    return real, imag


def _place_hits(pattern_ref, rows, cols):
    count = pattern_ref.shape[1]
    position = pattern_ref[...].astype(jnp.float32)
    row = jnp.floor((position + 0.5) * (1.0 / cols))
    col = position - row * cols
    row_hit = lax.broadcasted_iota(jnp.int32, (rows, count), 0).astype(jnp.float32) == row
    col_hit = lax.broadcasted_iota(jnp.int32, (cols, count), 0).astype(jnp.float32) == col
    return row_hit, col_hit


def _nt(a, b):
    return lax.dot_general(a, b, (((1,), (1,)), ((), ())), preferred_element_type=jnp.float32)


def _early_kernel(slab_ref, previous_ref, own_ref, near_ref, held_ref, rate_scr, *, factor, rows):
    step = pl.program_id(0)

    @pl.when(step == 0)
    def _():
        near_ref[...] = jnp.zeros_like(near_ref)
        rate_scr[0] = previous_ref[...]

    @pl.when(step > 0)
    def _():
        rate_scr[0] = own_ref[...]

    slab_real = slab_ref[0, 0]
    slab_imag = slab_ref[1, 0]
    left = _weigh(slab_real.astype(jnp.float32), slab_imag.astype(jnp.float32), rate_scr, 0, factor)
    prod = _nt(left, jnp.concatenate([slab_real, slab_imag], axis=0))
    for q in range(2):
        real, imag = _adjoint_parts(prod, q, rows, 0, rows)
        near_ref[q, 0] += real
        near_ref[q, 1] += imag

    @pl.when(step == pl.num_programs(0) - 1)
    def _():
        held_ref[...] = left


def _late_kernel(slab_ref, bundle_ref, near_ref, held_ref, place_ref, out_ref, rate_scr,
                 *, factor, rows, edge):
    cols = rows + edge
    edge_rows = 4 * edge
    for piece_q in range(2):
        for part in range(2):
            k = piece_q * 2 + part
            pieces = [bundle_ref[edge_rows + 4 * t + k:edge_rows + 4 * t + k + 1, :].astype(jnp.float32)
                      for t in range(3)]
            rate_scr[0, piece_q, part:part + 1, :] = (pieces[0] + pieces[1]) + pieces[2]
    slab_real = slab_ref[0, 0]
    slab_imag = slab_ref[1, 0]
    left = _weigh(slab_real.astype(jnp.float32), slab_imag.astype(jnp.float32), rate_scr, 0, factor)

    def edge_of(part, block):
        start = part * 2 * edge + block * edge
        return bundle_ref[start:start + edge, :]

    far = _nt(left, jnp.concatenate([slab_real, slab_imag, edge_of(0, 1), edge_of(1, 1)], axis=0))
    own = _nt(held_ref[...], jnp.concatenate([edge_of(0, 0), edge_of(1, 0)], axis=0))
    joined = []
    for q in range(2):
        near_real, near_imag = _adjoint_parts(far, q, rows, 0, rows)
        far_real, far_imag = _adjoint_parts(far, q, rows, 2 * rows, edge)
        own_real, own_imag = _adjoint_parts(own, q, rows, 0, edge)
        joined.append(jnp.concatenate([near_ref[q, 0] + near_real, far_real + own_real], axis=1))
        joined.append(jnp.concatenate([near_ref[q, 1] + near_imag, far_imag + own_imag], axis=1))
    joined = jnp.concatenate(joined, axis=0).astype(jnp.bfloat16)
    row_hit, col_hit = _place_hits(place_ref, rows, cols)
    by_column = jnp.dot(joined, col_hit.astype(jnp.bfloat16), preferred_element_type=jnp.float32)
    chunks = out_ref.shape[0]
    width = out_ref.shape[2] // 4
    for k in range(4):
        picked = jnp.where(row_hit, by_column[k * rows:(k + 1) * rows], 0.0)
        picked = jnp.sum(picked, axis=0, keepdims=True).astype(out_ref.dtype)
        for chunk in range(chunks):
            out_ref[chunk, :, k * width:(k + 1) * width] = picked[:, chunk * width:(chunk + 1) * width]


def element_values(own_slab, bundle, previous_rate, own_rate, pattern_row, edge, chunks):
    _, blocks, rows, block_order = own_slab.shape
    count = pattern_row.shape[1]
    factor = 1.0 / math.sqrt(3.0 * block_order)
    near, held = pl.pallas_call(
        functools.partial(_early_kernel, factor=factor, rows=rows),
        grid=(blocks - 1,),
        in_specs=[
            pl.BlockSpec((2, 1, rows, block_order), lambda j: (0, j, 0, 0)),
            pl.BlockSpec((2, 2, block_order), lambda j: (0, 0, 0)),
            pl.BlockSpec((2, 2, block_order), lambda j: (0, 0, 0)),
        ],
        out_specs=[
            pl.BlockSpec((2, 2, rows, rows), lambda j: (0, 0, 0, 0)),
            pl.BlockSpec((4 * rows, block_order), lambda j: (0, 0)),
        ],
        scratch_shapes=[pltpu.VMEM((1, 2, 2, block_order), jnp.float32)],
        out_shape=[
            jax.ShapeDtypeStruct((2, 2, rows, rows), jnp.float32),
            jax.ShapeDtypeStruct((4 * rows, block_order), jnp.bfloat16),
        ],
    )(own_slab, previous_rate, own_rate)
    last = blocks - 1
    return pl.pallas_call(
        functools.partial(_late_kernel, factor=factor, rows=rows, edge=edge),
        grid=(1,),
        in_specs=[
            pl.BlockSpec((2, 1, rows, block_order), lambda j: (0, last, 0, 0)),
            pl.BlockSpec(bundle.shape, lambda j: (0, 0)),
            pl.BlockSpec((2, 2, rows, rows), lambda j: (0, 0, 0, 0)),
            pl.BlockSpec((4 * rows, block_order), lambda j: (0, 0)),
            pl.BlockSpec((1, count), lambda j: (0, 0)),
        ],
        out_specs=pl.BlockSpec((chunks, 1, 4 * count // chunks), lambda j: (0, 0, 0)),
        out_shape=jax.ShapeDtypeStruct((chunks, 1, 4 * count // chunks), jnp.bfloat16),
        scratch_shapes=[pltpu.VMEM((1, 2, 2, block_order), jnp.float32)],
    )(own_slab, bundle, near, held, pattern_row)


def _lag_kernel(in_ref, out_ref, *, width, factor):
    values = in_ref[:, 0, :].astype(jnp.float32)
    energy_count = values.shape[0]
    lesser = values[:, 0:2 * width]
    greater = values[:, 2 * width:4 * width]
    swapped = jnp.concatenate([greater[:, width:], greater[:, :width]], axis=1)
    padded = jnp.concatenate([lesser, jnp.zeros_like(lesser)], axis=0)
    straight = jnp.zeros_like(lesser)
    crossed = jnp.zeros_like(lesser)
    for k in range(energy_count):
        window = padded[k:k + energy_count]
        straight = straight + window * greater[k:k + 1]
        crossed = crossed + window * swapped[k:k + 1]
    joined = jnp.concatenate(
        [straight[:, :width] - straight[:, width:], crossed[:, :width] + crossed[:, width:]], axis=1
    )
    out_ref[:, 0, :] = (joined * factor).astype(out_ref.dtype)


def lag_sums(by_element):
    energy_count, _, joined = by_element.shape
    width = joined // 4
    kernel = functools.partial(_lag_kernel, width=width, factor=1.0 / math.sqrt(energy_count))
    return pl.pallas_call(
        kernel,
        out_shape=jax.ShapeDtypeStruct((energy_count, 1, 2 * width), jnp.bfloat16),
    )(by_element)


def _screen_kernel(polar_ref, place_ref, screen_ref, out_ref, polar_scr, *, rows, cols):
    def nt(a, b):
        return lax.dot_general(a, b, (((1,), (1,)), ((), ())), preferred_element_type=jnp.float32)

    def nn(a, b):
        return jnp.dot(a, b, preferred_element_type=jnp.float32)

    row_hit, col_hit = _place_hits(place_ref, rows, cols)
    col_hit = col_hit.astype(jnp.bfloat16)
    chunks = polar_ref.shape[0]
    width = polar_ref.shape[2] // 2
    for chunk in range(chunks):
        piece = polar_ref[chunk]
        for part in range(2):
            polar_scr[part:part + 1, chunk * width:(chunk + 1) * width] = piece[:, part * width:(part + 1) * width]
    polar = polar_scr[...].astype(jnp.float32)
    dense = []
    for part in range(2):
        spread = jnp.where(row_hit, polar[part:part + 1, :], 0.0).astype(jnp.bfloat16)
        dense.append(nt(spread, col_hit).astype(jnp.bfloat16))
    dense_real, dense_imag = dense
    screen_real = screen_ref[0]
    screen_imag = screen_ref[1]
    inner_real = (nt(dense_real, screen_real) + nt(dense_imag, screen_imag)).astype(jnp.bfloat16)
    inner_imag = (nt(dense_imag, screen_real) - nt(dense_real, screen_imag)).astype(jnp.bfloat16)
    near_real = screen_real[:, :rows]
    near_imag = screen_imag[:, :rows]
    side_real = screen_real[:, rows:]
    side_imag = screen_imag[:, rows:]
    edge_real = dense_real[:, rows:]
    edge_imag = dense_imag[:, rows:]
    across_real = (nn(near_real, edge_real) - nn(near_imag, edge_imag)).astype(jnp.bfloat16)
    across_imag = (nn(near_real, edge_imag) + nn(near_imag, edge_real)).astype(jnp.bfloat16)
    first_real = nn(near_real, inner_real) - nn(near_imag, inner_imag)
    first_imag = nn(near_real, inner_imag) + nn(near_imag, inner_real)
    second_real = nt(side_real, across_real) + nt(side_imag, across_imag)
    second_imag = nt(side_imag, across_real) - nt(side_real, across_imag)
    out_ref[0] = first_real + second_real
    out_ref[1] = first_imag + second_imag


def screen(polar_row, pattern_row, screen_block):
    rows = screen_block.shape[1]
    cols = screen_block.shape[2]
    kernel = functools.partial(_screen_kernel, rows=rows, cols=cols)
    return pl.pallas_call(
        kernel,
        out_shape=jax.ShapeDtypeStruct((2, rows, rows), jnp.float32),
        scratch_shapes=[pltpu.VMEM((2, pattern_row.shape[1]), polar_row.dtype)],
    )(polar_row, pattern_row, screen_block)


def split_exact(value):
    high = lax.reduce_precision(value, exponent_bits=8, mantissa_bits=7)
    rest = value - high
    middle = lax.reduce_precision(rest, exponent_bits=8, mantissa_bits=7)
    low = rest - middle
    return jnp.stack([high, middle, low], axis=0).astype(jnp.bfloat16)


def body(green_slab, self_energy, pattern, screened):
    own_rate = self_energy[0, 0]
    block_order = own_rate.shape[-1]
    previous_rate = passed_along(own_rate, "domain", 1)
    edge_block = green_slab[0, 0, :, 0:2, :EDGE, :]
    bundle = jnp.concatenate(
        [edge_block.reshape(-1, block_order), split_exact(own_rate).reshape(-1, block_order)], axis=0
    )
    bundle = passed_along(bundle, "domain", -1)
    chunks = lax.axis_size("energy")
    values = element_values(green_slab[0, 0], bundle, previous_rate, own_rate, pattern, EDGE, chunks)
    by_element = lax.all_to_all(values, "energy", split_axis=0, concat_axis=0, tiled=True)
    polarization = lag_sums(by_element)
    per_energy = lax.all_to_all(polarization, "energy", split_axis=0, concat_axis=0, tiled=True)
    result = screen(per_energy, pattern, screened[0, 0])
    return result[None, None]


def solution(mesh):
    placed = (
        P("energy", "domain", None, None, None, None),
        P("energy", "domain", None, None, None),
        P("domain", None),
        P("energy", "domain", None, None, None),
    )
    return jax.shard_map(
        body,
        mesh=mesh,
        in_specs=placed,
        out_specs=P("energy", "domain", None, None, None),
        check_vma=False,
    )
```

```python
import functools
import math

import jax
import jax.numpy as jnp
from jax import lax
from jax.experimental import pallas as pl
from jax.experimental.pallas import tpu as pltpu
from jax.sharding import PartitionSpec as P

EDGE = 16


def passed_along(x, axis, by):
    length = lax.axis_size(axis)
    pairs = [(i, i + by) for i in range(length) if 0 <= i + by < length]
    return lax.ppermute(x, axis, pairs)


def _weigh(real_f, imag_f, rate_ref, block, factor):
    pieces = []
    for q in range(2):
        rate_real = rate_ref[block, q, 0:1, :]
        rate_imag = rate_ref[block, q, 1:2, :]
        pieces.append(((real_f * rate_real - imag_f * rate_imag) * factor).astype(jnp.bfloat16))
        pieces.append(((real_f * rate_imag + imag_f * rate_real) * factor).astype(jnp.bfloat16))
    return jnp.concatenate(pieces, axis=0)


def _adjoint_parts(prod, q, rows, start, width):
    wr = prod[2 * q * rows:(2 * q + 1) * rows]
    wi = prod[(2 * q + 1) * rows:(2 * q + 2) * rows]
    real = wr[:, start:start + width] + wi[:, start + width:start + 2 * width]
    imag = wi[:, start:start + width] - wr[:, start + width:start + 2 * width]
    return real, imag


def _place_hits(pattern_ref, rows, cols):
    count = pattern_ref.shape[1]
    position = pattern_ref[...].astype(jnp.float32)
    row = jnp.floor((position + 0.5) * (1.0 / cols))
    col = (position - row * cols).astype(jnp.int32)
    row = row.astype(jnp.int32)
    row_hit = lax.broadcasted_iota(jnp.int32, (rows, count), 0) == row
    col_hit = lax.broadcasted_iota(jnp.int32, (cols, count), 0) == col
    return row_hit, col_hit


def _nt(a, b):
    return lax.dot_general(a, b, (((1,), (1,)), ((), ())), preferred_element_type=jnp.float32)


def _early_kernel(slab_ref, previous_ref, own_ref, near_ref, held_ref, rate_scr, *, factor, rows):
    step = pl.program_id(0)

    @pl.when(step == 0)
    def _():
        near_ref[...] = jnp.zeros_like(near_ref)
        rate_scr[0] = previous_ref[...]

    @pl.when(step > 0)
    def _():
        rate_scr[0] = own_ref[...]

    slab_real = slab_ref[0, 0]
    slab_imag = slab_ref[1, 0]
    left = _weigh(slab_real.astype(jnp.float32), slab_imag.astype(jnp.float32), rate_scr, 0, factor)
    prod = _nt(left, jnp.concatenate([slab_real, slab_imag], axis=0))
    for q in range(2):
        real, imag = _adjoint_parts(prod, q, rows, 0, rows)
        near_ref[q, 0] += real
        near_ref[q, 1] += imag

    @pl.when(step == pl.num_programs(0) - 1)
    def _():
        held_ref[...] = left


def _late_kernel(slab_ref, bundle_ref, near_ref, held_ref, place_ref, out_ref, rate_scr,
                 *, factor, rows, edge):
    cols = rows + edge
    edge_rows = 4 * edge
    for piece_q in range(2):
        for part in range(2):
            k = piece_q * 2 + part
            pieces = [bundle_ref[edge_rows + 4 * t + k:edge_rows + 4 * t + k + 1, :].astype(jnp.float32)
                      for t in range(3)]
            rate_scr[0, piece_q, part:part + 1, :] = (pieces[0] + pieces[1]) + pieces[2]
    slab_real = slab_ref[0, 0]
    slab_imag = slab_ref[1, 0]
    left = _weigh(slab_real.astype(jnp.float32), slab_imag.astype(jnp.float32), rate_scr, 0, factor)

    def edge_of(part, block):
        start = part * 2 * edge + block * edge
        return bundle_ref[start:start + edge, :]

    far = _nt(left, jnp.concatenate([slab_real, slab_imag, edge_of(0, 1), edge_of(1, 1)], axis=0))
    own = _nt(held_ref[...], jnp.concatenate([edge_of(0, 0), edge_of(1, 0)], axis=0))
    joined = []
    for q in range(2):
        near_real, near_imag = _adjoint_parts(far, q, rows, 0, rows)
        far_real, far_imag = _adjoint_parts(far, q, rows, 2 * rows, edge)
        own_real, own_imag = _adjoint_parts(own, q, rows, 0, edge)
        joined.append(jnp.concatenate([near_ref[q, 0] + near_real, far_real + own_real], axis=1))
        joined.append(jnp.concatenate([near_ref[q, 1] + near_imag, far_imag + own_imag], axis=1))
    joined = jnp.concatenate(joined, axis=0).astype(jnp.bfloat16)
    row_hit, col_hit = _place_hits(place_ref, rows, cols)
    by_column = jnp.dot(joined, col_hit.astype(jnp.bfloat16), preferred_element_type=jnp.float32)
    chunks = out_ref.shape[0]
    width = out_ref.shape[2] // 4
    for k in range(4):
        picked = jnp.where(row_hit, by_column[k * rows:(k + 1) * rows], 0.0)
        picked = jnp.sum(picked, axis=0, keepdims=True).astype(out_ref.dtype)
        for chunk in range(chunks):
            out_ref[chunk, :, k * width:(k + 1) * width] = picked[:, chunk * width:(chunk + 1) * width]


def element_values(own_slab, bundle, previous_rate, own_rate, pattern_row, edge, chunks):
    _, blocks, rows, block_order = own_slab.shape
    count = pattern_row.shape[1]
    factor = 1.0 / math.sqrt(3.0 * block_order)
    near, held = pl.pallas_call(
        functools.partial(_early_kernel, factor=factor, rows=rows),
        grid=(blocks - 1,),
        in_specs=[
            pl.BlockSpec((2, 1, rows, block_order), lambda j: (0, j, 0, 0)),
            pl.BlockSpec((2, 2, block_order), lambda j: (0, 0, 0)),
            pl.BlockSpec((2, 2, block_order), lambda j: (0, 0, 0)),
        ],
        out_specs=[
            pl.BlockSpec((2, 2, rows, rows), lambda j: (0, 0, 0, 0)),
            pl.BlockSpec((4 * rows, block_order), lambda j: (0, 0)),
        ],
        scratch_shapes=[pltpu.VMEM((1, 2, 2, block_order), jnp.float32)],
        out_shape=[
            jax.ShapeDtypeStruct((2, 2, rows, rows), jnp.float32),
            jax.ShapeDtypeStruct((4 * rows, block_order), jnp.bfloat16),
        ],
    )(own_slab, previous_rate, own_rate)
    last = blocks - 1
    return pl.pallas_call(
        functools.partial(_late_kernel, factor=factor, rows=rows, edge=edge),
        grid=(1,),
        in_specs=[
            pl.BlockSpec((2, 1, rows, block_order), lambda j: (0, last, 0, 0)),
            pl.BlockSpec(bundle.shape, lambda j: (0, 0)),
            pl.BlockSpec((2, 2, rows, rows), lambda j: (0, 0, 0, 0)),
            pl.BlockSpec((4 * rows, block_order), lambda j: (0, 0)),
            pl.BlockSpec((1, count), lambda j: (0, 0)),
        ],
        out_specs=pl.BlockSpec((chunks, 1, 4 * count // chunks), lambda j: (0, 0, 0)),
        out_shape=jax.ShapeDtypeStruct((chunks, 1, 4 * count // chunks), jnp.bfloat16),
        scratch_shapes=[pltpu.VMEM((1, 2, 2, block_order), jnp.float32)],
    )(own_slab, bundle, near, held, pattern_row)


def _lag_kernel(in_ref, out_ref, *, width, factor):
    values = in_ref[:, 0, :].astype(jnp.float32)
    energy_count = values.shape[0]
    lesser = values[:, 0:2 * width]
    greater = values[:, 2 * width:4 * width]
    swapped = jnp.concatenate([greater[:, width:], greater[:, :width]], axis=1)
    padded = jnp.concatenate([lesser, jnp.zeros_like(lesser)], axis=0)
    straight = jnp.zeros_like(lesser)
    crossed = jnp.zeros_like(lesser)
    for k in range(energy_count):
        window = padded[k:k + energy_count]
        straight = straight + window * greater[k:k + 1]
        crossed = crossed + window * swapped[k:k + 1]
    joined = jnp.concatenate(
        [straight[:, :width] - straight[:, width:], crossed[:, :width] + crossed[:, width:]], axis=1
    )
    out_ref[:, 0, :] = (joined * factor).astype(out_ref.dtype)


def lag_sums(by_element):
    energy_count, _, joined = by_element.shape
    width = joined // 4
    kernel = functools.partial(_lag_kernel, width=width, factor=1.0 / math.sqrt(energy_count))
    return pl.pallas_call(
        kernel,
        out_shape=jax.ShapeDtypeStruct((energy_count, 1, 2 * width), jnp.bfloat16),
    )(by_element)


def _screen_kernel(polar_ref, place_ref, screen_ref, out_ref, polar_scr, *, rows, cols):
    def nt(a, b):
        return lax.dot_general(a, b, (((1,), (1,)), ((), ())), preferred_element_type=jnp.float32)

    def nn(a, b):
        return jnp.dot(a, b, preferred_element_type=jnp.float32)

    row_hit, col_hit = _place_hits(place_ref, rows, cols)
    col_hit = col_hit.astype(jnp.bfloat16)
    chunks = polar_ref.shape[0]
    width = polar_ref.shape[2] // 2
    for chunk in range(chunks):
        piece = polar_ref[chunk]
        for part in range(2):
            polar_scr[part:part + 1, chunk * width:(chunk + 1) * width] = piece[:, part * width:(part + 1) * width]
    polar = polar_scr[...].astype(jnp.float32)
    dense = []
    for part in range(2):
        spread = jnp.where(row_hit, polar[part:part + 1, :], 0.0).astype(jnp.bfloat16)
        dense.append(nt(spread, col_hit).astype(jnp.bfloat16))
    dense_real, dense_imag = dense
    screen_real = screen_ref[0]
    screen_imag = screen_ref[1]
    inner_real = (nt(dense_real, screen_real) + nt(dense_imag, screen_imag)).astype(jnp.bfloat16)
    inner_imag = (nt(dense_imag, screen_real) - nt(dense_real, screen_imag)).astype(jnp.bfloat16)
    near_real = screen_real[:, :rows]
    near_imag = screen_imag[:, :rows]
    side_real = screen_real[:, rows:]
    side_imag = screen_imag[:, rows:]
    edge_real = dense_real[:, rows:]
    edge_imag = dense_imag[:, rows:]
    across_real = (nn(near_real, edge_real) - nn(near_imag, edge_imag)).astype(jnp.bfloat16)
    across_imag = (nn(near_real, edge_imag) + nn(near_imag, edge_real)).astype(jnp.bfloat16)
    first_real = nn(near_real, inner_real) - nn(near_imag, inner_imag)
    first_imag = nn(near_real, inner_imag) + nn(near_imag, inner_real)
    second_real = nt(side_real, across_real) + nt(side_imag, across_imag)
    second_imag = nt(side_imag, across_real) - nt(side_real, across_imag)
    out_ref[0] = first_real + second_real
    out_ref[1] = first_imag + second_imag


def screen(polar_row, pattern_row, screen_block):
    rows = screen_block.shape[1]
    cols = screen_block.shape[2]
    kernel = functools.partial(_screen_kernel, rows=rows, cols=cols)
    return pl.pallas_call(
        kernel,
        out_shape=jax.ShapeDtypeStruct((2, rows, rows), jnp.float32),
        scratch_shapes=[pltpu.VMEM((2, pattern_row.shape[1]), polar_row.dtype)],
    )(polar_row, pattern_row, screen_block)


def split_exact(value):
    high = lax.reduce_precision(value, exponent_bits=8, mantissa_bits=7)
    rest = value - high
    middle = lax.reduce_precision(rest, exponent_bits=8, mantissa_bits=7)
    low = rest - middle
    return jnp.stack([high, middle, low], axis=0).astype(jnp.bfloat16)


def body(green_slab, self_energy, pattern, screened):
    own_rate = self_energy[0, 0]
    block_order = own_rate.shape[-1]
    previous_rate = passed_along(own_rate, "domain", 1)
    edge_block = green_slab[0, 0, :, 0:2, :EDGE, :]
    bundle = jnp.concatenate(
        [edge_block.reshape(-1, block_order), split_exact(own_rate).reshape(-1, block_order)], axis=0
    )
    bundle = passed_along(bundle, "domain", -1)
    chunks = lax.axis_size("energy")
    values = element_values(green_slab[0, 0], bundle, previous_rate, own_rate, pattern, EDGE, chunks)
    by_element = lax.all_to_all(values, "energy", split_axis=0, concat_axis=0, tiled=True)
    polarization = lag_sums(by_element)
    per_energy = lax.all_to_all(polarization, "energy", split_axis=0, concat_axis=0, tiled=True)
    result = screen(per_energy, pattern, screened[0, 0])
    return result[None, None]


def solution(mesh):
    placed = (
        P("energy", "domain", None, None, None, None),
        P("energy", "domain", None, None, None),
        P("domain", None),
        P("energy", "domain", None, None, None),
    )
    return jax.shard_map(
        body,
        mesh=mesh,
        in_specs=placed,
        out_specs=P("energy", "domain", None, None, None),
        check_vma=False,
    )
```
